32 devices in a mesh: grp: 2 (over x), seq: 16 (over z, y, core).
Axes of the slice: x: 2, y: 2, z: 4, core: 2. Of those that a mesh axis runs over, the one named last changes fastest.
Arguments:
- tokens: int32 [4, 2048], P('grp', 'seq'), parts along dimension 0, may hold values from 0 to 3
- emb_half: bfloat16 [2, 512], replicated, may hold values from -6 to 6
- norm_gain: float32 [512], replicated, may hold values from 0.1 to 1.9
- w_xbc: bfloat16 [512, 1152], replicated, may hold values from -0.25 to 0.25
- w_z: bfloat16 [512, 1024], replicated, may hold values from -0.25 to 0.25
- w_dt: bfloat16 [512, 16], replicated, may hold values from -0.25 to 0.25
- conv_w: float32 [4, 1152], replicated, may hold values from -3 to 3
- conv_bias: float32 [1152], replicated, may hold values from -3 to 3
- dt_bias: float32 [16], replicated, may hold values from -1 to 1
- a_log: float32 [16], replicated
- d_skip: float32 [16], replicated, may hold values from 0.5 to 1.5
- inner_gain: float32 [1024], replicated, may hold values from 0.1 to 1.9
- w_out: bfloat16 [1024, 512], replicated, may hold values from -0.1875 to 0.1875
- final_gain: float32 [512], replicated, may hold values from 0.1 to 1.9
- w_head_half: bfloat16 [512, 2], replicated, may hold values from -0.25 to 0.25
- teacher_top: int32 [4, 2, 2048], P('grp', None, 'seq'), parts along dimension 0, may hold values from 0 to 3, as said below
- teacher_vals: float32 [4, 2, 2048], P('grp', None, 'seq'), parts along dimension 0, may hold values from -8 to 405
Outputs:
- hidden_out: bfloat16 [4, 2048, 512], P('grp', 'seq'), parts along dimension 0
- divergence: float32 [4, 2048], P('grp', 'seq'), parts along dimension 0
The draws below stay inside these ranges and needn't reach their ends.
There are 2 independent parts, one for each index of `grp`. The reference program is written for one: setup_inputs(seed, part) draws one part's arguments, and reference() takes and returns one part's arrays. A program takes and returns all parts, laid end to end along the dimension named above; an argument that names none is the same for every part. Nothing has to cross between parts.
Inputs may be any that keep to these rules, and one draw needn't show every extreme that they name: `teacher_top`: the 2 bases kept at a position are distinct.
All inputs are finite; a program needn't handle non-finite values.
Results may differ from the reference program's by a relative error of at most 0.012.
Values may be sent and summed in bfloat16 or wider, within the bound.
No kernel may reach another device: no remote copies, remote signals or barrier semaphores. Data moves between devices by JAX's collectives and lax.ppermute only.
A program may use at most 320 MiB of HBM per device.

```python
import jax
import jax.numpy as jnp
from jax import lax

D = 512
INNER = 1024
HD = 64
NS = 64
KW = 4
BLK = 128
MB = 2
TOPK = 2
HEADS = 16
CONVW = 1152
TOKENS = 2048


def draw_a_log(key, part):
    first_key, second_key, third_key = jax.random.split(key, 3)
    chooser = jax.random.uniform(first_key, (HEADS,))
    slow_share = 0.5
    slow_rate = jnp.log(jax.random.uniform(second_key, (HEADS,), minval=0.05, maxval=0.5)) - jnp.log(TOKENS * 1.0)
    fast_rate = jnp.log(jax.random.uniform(third_key, (HEADS,), minval=0.02, maxval=0.06))
    return jnp.where(chooser < slow_share, slow_rate, fast_rate).astype(jnp.float32)


def draw_teacher_top(key, part):
    first_key, second_key = jax.random.split(jax.random.fold_in(key, 7))
    first_base = jax.random.randint(first_key, (MB, 1, TOKENS), 0, 4)
    step_base = jax.random.randint(second_key, (MB, 1, TOKENS), 1, 4)
    return jnp.concatenate([first_base, (first_base + step_base) % 4], axis=1).astype(jnp.int32)


def draw_teacher_vals(key, part):
    keys = jax.random.split(jax.random.fold_in(key, 11), 1)
    return jnp.clip(2.5 * jax.random.normal(keys[0], (MB, TOPK, TOKENS)), -8.0, 8.0).astype(jnp.float32)


def set_ends(entries, own_key, smallest, high):
    dims = entries.shape
    place = [jax.random.randint(jax.random.fold_in(own_key, axis), (), 0, dims[axis]) for axis in range(len(dims))]
    entries = entries.at[tuple(place)].set(smallest)
    longest = dims.index(max(dims))
    place[longest] = (place[longest] + 1) % dims[longest]
    return entries.at[tuple(place)].set(high)


def noise(own_key, extent, deviation, reach, kind=jnp.bfloat16):
    return jnp.clip(deviation * jax.random.normal(own_key, extent, jnp.float32), -reach, reach).astype(kind)


def setup_inputs(seed: int = 0, part: int = 0) -> dict:
    key_of = jax.random.split(jax.random.key(seed), 18)
    own_keys = jax.random.split(jax.random.fold_in(key_of[17], part), 18)
    tokens = set_ends(jax.random.randint(own_keys[0], (MB, TOKENS), 0, 4), jax.random.fold_in(own_keys[0], 1), 0, 3).astype(jnp.int32)
    emb_half = noise(key_of[1], (2, D), 1.0, 6.0)
    norm_gain = jnp.clip(1.0 + 0.18 * jax.random.normal(key_of[2], (D,), jnp.float32), 0.1, 1.9)
    w_xbc = noise(key_of[3], (D, CONVW), D ** -0.5, 0.25)
    w_z = noise(key_of[4], (D, INNER), D ** -0.5, 0.25)
    w_dt = noise(key_of[5], (D, HEADS), D ** -0.5, 0.25)
    conv_w = noise(key_of[6], (KW, CONVW), 0.5, 3.0, jnp.float32)
    conv_bias = noise(key_of[7], (CONVW,), 0.5, 3.0, jnp.float32)
    dt_bias = jnp.clip(jax.random.uniform(key_of[8], (HEADS,), jnp.float32, -1.0, 1.0), -1.0, 1.0)
    a_log = draw_a_log(jax.random.fold_in(key_of[17], 71), part)
    d_skip = jnp.clip(jax.random.uniform(key_of[10], (HEADS,), jnp.float32, 0.5, 1.5), 0.5, 1.5)
    inner_gain = jnp.clip(1.0 + 0.18 * jax.random.normal(key_of[11], (INNER,), jnp.float32), 0.1, 1.9)
    w_out = noise(key_of[12], (INNER, D), INNER ** -0.5, 0.1875)
    final_gain = jnp.clip(1.0 + 0.18 * jax.random.normal(key_of[13], (D,), jnp.float32), 0.1, 1.9)
    w_head_half = noise(key_of[14], (D, 2), D ** -0.5, 0.25)
    teacher_top = draw_teacher_top(jax.random.fold_in(jax.random.fold_in(key_of[17], part), 71), part)
    teacher_vals = draw_teacher_vals(jax.random.fold_in(jax.random.fold_in(key_of[17], part), 71), part)
    return {"tokens": tokens, "emb_half": emb_half, "norm_gain": norm_gain, "w_xbc": w_xbc, "w_z": w_z, "w_dt": w_dt, "conv_w": conv_w, "conv_bias": conv_bias, "dt_bias": dt_bias, "a_log": a_log, "d_skip": d_skip, "inner_gain": inner_gain, "w_out": w_out, "final_gain": final_gain, "w_head_half": w_head_half, "teacher_top": teacher_top, "teacher_vals": teacher_vals}


EPS = 1e-05
HIGH = lax.Precision.HIGHEST

def rms_gain(values, gain_row):
    return values * lax.rsqrt(lax.optimization_barrier(jnp.mean(values * values, axis=-1, keepdims=True)) + EPS) * gain_row

def to_blocks(values, block_width):
    streams, count = (values.shape[0], values.shape[1])
    return jnp.moveaxis(values.reshape((streams, count // block_width, block_width) + values.shape[2:]), 1, 0)

def ssd_block(carry_state, block_in):
    x_blk, b_blk, c_blk, decay_blk, dt_blk = block_in
    cumulated = jnp.cumsum(decay_blk, axis=2)
    block_len = decay_blk.shape[2]
    scores = jnp.einsum('gtn,gsn->gts', c_blk, b_blk, precision=HIGH)
    seg_diff = cumulated[:, :, :, None] - cumulated[:, :, None, :]
    lower_mask = jnp.arange(block_len)[:, None] >= jnp.arange(block_len)[None, :]
    decays = jnp.where(lower_mask, jnp.exp(jnp.where(lower_mask, seg_diff, 0.0)), 0.0)
    weights = (scores[:, None] * decays * dt_blk[:, :, None, :]).astype(jnp.bfloat16)
    y_intra = jnp.einsum('ghts,gshp->gthp', weights.astype(jnp.float32), x_blk.astype(jnp.float32), precision=HIGH)
    y_inter = jnp.einsum('gtn,ghpn->gthp', c_blk, carry_state, precision=HIGH) * jnp.swapaxes(jnp.exp(cumulated), 1, 2)[..., None]
    last_cum = cumulated[:, :, -1:]
    scaled = jnp.exp(last_cum - cumulated) * dt_blk
    x_weighted = x_blk.astype(jnp.float32) * jnp.swapaxes(scaled, 1, 2)[..., None]
    new_state = jnp.exp(last_cum)[..., None] * carry_state + jnp.einsum('gshp,gsn->ghpn', x_weighted, b_blk, precision=HIGH)
    return (new_state, y_intra + y_inter)

def mamba_mixer(stream, norm_gain, w_xbc, w_z, w_dt, conv_w, conv_bias, dt_bias, a_log, d_skip, inner_gain, w_out):
    streams, count = (stream.shape[0], stream.shape[1])
    normed_in = rms_gain(stream.astype(jnp.float32), norm_gain).astype(jnp.bfloat16).reshape(-1, D)
    xbc = jnp.dot(normed_in, w_xbc, preferred_element_type=jnp.float32).astype(jnp.bfloat16).reshape(streams, count, CONVW)
    gate_z = jnp.dot(normed_in, w_z, preferred_element_type=jnp.float32).astype(jnp.bfloat16).reshape(streams, count, INNER)
    dt_raw = jnp.dot(normed_in, w_dt, preferred_element_type=jnp.float32).reshape(streams, count, HEADS)
    padded = jnp.pad(xbc, ((0, 0), (KW - 1, 0), (0, 0)))
    conv_sum = jnp.zeros((streams, count, CONVW), jnp.float32) + conv_bias
    for offset in range(KW):
        conv_sum = conv_sum + conv_w[offset] * padded[:, offset:offset + count].astype(jnp.float32)
    activated = jax.nn.silu(conv_sum)
    x_act = activated[..., :INNER].astype(jnp.bfloat16)
    b_all = activated[..., INNER:INNER + NS]
    c_all = activated[..., INNER + NS:]
    step_dt = jax.nn.softplus(dt_raw + dt_bias)
    log_decay = -jnp.exp(a_log) * step_dt
    blocks = (to_blocks(x_act.reshape(streams, count, HEADS, HD), BLK), to_blocks(b_all, BLK), to_blocks(c_all, BLK), jnp.swapaxes(to_blocks(log_decay, BLK), 2, 3), jnp.swapaxes(to_blocks(step_dt, BLK), 2, 3))
    zero_state = jnp.zeros((streams, HEADS, HD, NS), jnp.float32)
    end_state, y_blocks = lax.scan(ssd_block, zero_state, blocks)
    y_all = jnp.moveaxis(y_blocks, 0, 1).reshape(streams, count, HEADS, HD)
    y_all = y_all + d_skip[:, None] * x_act.astype(jnp.float32).reshape(streams, count, HEADS, HD)
    gated_y = y_all * jax.nn.silu(gate_z.astype(jnp.float32)).reshape(streams, count, HEADS, HD)
    normed = rms_gain(gated_y, inner_gain.reshape(HEADS, HD)).astype(jnp.bfloat16).reshape(-1, INNER)
    return jnp.dot(normed, w_out, preferred_element_type=jnp.float32).astype(jnp.bfloat16).reshape(streams, count, D)

def reference(tokens, emb_half, norm_gain, w_xbc, w_z, w_dt, conv_w, conv_bias, dt_bias, a_log, d_skip, inner_gain, w_out, final_gain, w_head_half, teacher_top, teacher_vals):
    emb_full = jnp.concatenate([emb_half, emb_half[::-1, ::-1]], axis=0)
    embedded = emb_full[tokens]
    stream = jnp.concatenate([embedded, embedded[:, ::-1, ::-1]], axis=0)
    outputs = mamba_mixer(stream, norm_gain, w_xbc, w_z, w_dt, conv_w, conv_bias, dt_bias, a_log, d_skip, inner_gain, w_out)
    returned = outputs[MB:, ::-1, ::-1]
    hidden_out = (embedded.astype(jnp.float32) + outputs[:MB].astype(jnp.float32) + returned.astype(jnp.float32)).astype(jnp.bfloat16)
    final_normed = rms_gain(hidden_out.astype(jnp.float32), final_gain).astype(jnp.bfloat16)
    head_full = jnp.concatenate([w_head_half, w_head_half[::-1, ::-1]], axis=1)
    logits = jnp.dot(final_normed.reshape(-1, D), head_full, preferred_element_type=jnp.float32).reshape(MB, -1, 4)
    log_q = logits - jnp.log(lax.optimization_barrier(jnp.sum(jnp.exp(logits), axis=-1, keepdims=True)))
    top_value = lax.optimization_barrier(jnp.max(teacher_vals, axis=1, keepdims=True))
    shifted = teacher_vals - top_value
    log_p = shifted - jnp.log(lax.optimization_barrier(jnp.sum(jnp.exp(shifted), axis=1, keepdims=True)))
    matches = teacher_top[..., None] == jnp.arange(4, dtype=jnp.int32)
    picked = lax.optimization_barrier(jnp.sum(jnp.where(matches, log_q[:, None, :, :], 0.0), axis=-1))
    divergence = lax.optimization_barrier(jnp.sum(jnp.exp(log_p) * (log_p - picked), axis=1))
    return (hidden_out, divergence)
```

```python
import jax
import jax.numpy as jnp
import numpy as np
from jax import lax
from jax.sharding import PartitionSpec as P

INNER = 1024
HD = 64
NS = 64
KW = 4
BLK = 128
HEADS = 16
CONVW = 1152
BASES = 4
PAD = 4
GRAMS = (BASES + 1) ** KW


EPS = 1e-05
HIGH = lax.Precision.HIGHEST


def rms_gain(values, gain_row):
    return values * lax.rsqrt(jnp.mean(values * values, axis=-1, keepdims=True) + EPS) * gain_row


def to_blocks(values, block_width):
    streams, count = (values.shape[0], values.shape[1])
    return jnp.moveaxis(
        values.reshape((streams, count // block_width, block_width) + values.shape[2:]), 1, 0
    )


def ssd_block(carry_state, block_in):
    x_blk, b_blk, c_blk, decay_blk, dt_blk = block_in
    cumulated = jnp.cumsum(decay_blk, axis=2)
    block_len = decay_blk.shape[2]
    scores = jnp.einsum("gtn,gsn->gts", c_blk, b_blk, precision=HIGH)
    seg_diff = cumulated[:, :, :, None] - cumulated[:, :, None, :]
    lower_mask = jnp.arange(block_len)[:, None] >= jnp.arange(block_len)[None, :]
    decays = jnp.where(lower_mask, jnp.exp(jnp.where(lower_mask, seg_diff, 0.0)), 0.0)
    weights = (scores[:, None] * decays * dt_blk[:, :, None, :]).astype(jnp.bfloat16)
    y_intra = jnp.einsum("ghts,gshp->gthp", weights, x_blk, preferred_element_type=jnp.float32)
    y_inter = (
        jnp.einsum("gtn,ghpn->gthp", c_blk, carry_state, precision=HIGH)
        * jnp.swapaxes(jnp.exp(cumulated), 1, 2)[..., None]
    )
    last_cum = cumulated[:, :, -1:]
    scaled = jnp.exp(last_cum - cumulated) * dt_blk
    x_weighted = x_blk.astype(jnp.float32) * jnp.swapaxes(scaled, 1, 2)[..., None]
    new_state = jnp.exp(last_cum)[..., None] * carry_state + jnp.einsum(
        "gshp,gsn->ghpn", x_weighted, b_blk, precision=HIGH
    )
    return (new_state, y_intra + y_inter)


def gram_tables(emb_full, norm_gain, w_xbc, w_z, w_dt, conv_w, conv_bias):
    row_norm = rms_gain(emb_full.astype(jnp.float32), norm_gain).astype(jnp.bfloat16)
    xbc_rows = jnp.dot(row_norm, w_xbc, preferred_element_type=jnp.float32).astype(jnp.bfloat16)
    z_rows = jnp.dot(row_norm, w_z, preferred_element_type=jnp.float32).astype(jnp.bfloat16)
    dt_rows = jnp.dot(row_norm, w_dt, preferred_element_type=jnp.float32)
    xbc_pad = jnp.concatenate([xbc_rows, jnp.zeros((1, CONVW), jnp.bfloat16)], axis=0)
    xbc_pad = xbc_pad.astype(jnp.float32)
    conv_sum = jnp.zeros((BASES + 1,) * KW + (CONVW,), jnp.float32) + conv_bias
    for offset in range(KW):
        shape = [1] * KW + [CONVW]
        shape[offset] = BASES + 1
        conv_sum = conv_sum + (conv_w[offset] * xbc_pad).reshape(shape)
    activated = jax.nn.silu(conv_sum).reshape(GRAMS, CONVW)
    return activated, z_rows, dt_rows


def base_lookup(rows, bases):
    picked = jnp.zeros(bases.shape + rows.shape[1:], jnp.float32)
    for base in range(BASES):
        picked = picked + jnp.where(
            (bases == base)[..., None], rows[base].astype(jnp.float32), 0.0
        )
    return picked


def local(
    tokens,
    emb_half,
    norm_gain,
    w_xbc,
    w_z,
    w_dt,
    conv_w,
    conv_bias,
    dt_bias,
    a_log,
    d_skip,
    inner_gain,
    w_out,
    final_gain,
    w_head_half,
    teacher_top,
    teacher_vals,
):
    windows, count = tokens.shape
    nseq = lax.axis_size("seq")
    place = lax.axis_index("seq")
    total = count * nseq
    nblk = total // BLK
    streams = 2 * windows

    emb_full = jnp.concatenate([emb_half, emb_half[::-1, ::-1]], axis=0)
    activated_tab, z_rows, dt_rows = gram_tables(
        emb_full, norm_gain, w_xbc, w_z, w_dt, conv_w, conv_bias
    )
    x_tab = activated_tab[:, :INNER].astype(jnp.bfloat16)
    b_tab = activated_tab[:, INNER : INNER + NS]

    every = lax.all_gather(tokens, "seq", axis=1, tiled=True)
    seq_tok = jnp.concatenate([every, (BASES - 1) - every[:, ::-1]], axis=0)
    padded = jnp.concatenate(
        [jnp.full((streams, KW - 1), PAD, seq_tok.dtype), seq_tok], axis=1
    )
    gram = padded[:, 0:total]
    for offset in range(1, KW):
        gram = gram * (BASES + 1) + padded[:, offset : offset + total]

    step_dt = jax.nn.softplus(base_lookup(dt_rows, seq_tok) + dt_bias)
    log_decay = -jnp.exp(a_log) * step_dt

    fwd_start = place * count
    rc_start = (nseq - 1 - place) * count
    start = jnp.concatenate(
        [jnp.full((windows,), fwd_start), jnp.full((windows,), rc_start)]
    )
    first_blk = start // BLK

    cum = jnp.cumsum(log_decay.reshape(streams, nblk, BLK, HEADS), axis=2)
    blk_total = cum[:, :, -1, :]
    within = jnp.exp(blk_total[:, :, None, :] - cum) * step_dt.reshape(
        streams, nblk, BLK, HEADS
    )
    blk_idx = jnp.arange(nblk)
    between = (blk_idx[None, :, None] < blk_idx[None, None, :]) & (
        blk_idx[None, None, :] < first_blk[:, None, None]
    )
    span = jnp.sum(
        jnp.where(between[..., None], blk_total[:, None, :, :], 0.0), axis=2
    )
    across = jnp.where(
        (blk_idx[None, :] < first_blk[:, None])[..., None], jnp.exp(span), 0.0
    )
    weight = (within * across[:, :, None, :]).reshape(streams, total, HEADS)

    onehot = (gram[..., None] == jnp.arange(GRAMS, dtype=gram.dtype)).astype(jnp.bfloat16)
    weight_hi = weight.astype(jnp.bfloat16)
    weight_lo = (weight - weight_hi.astype(jnp.float32)).astype(jnp.bfloat16)
    per_gram = jnp.einsum(
        "rpg,rph->rgh", onehot, weight_hi, preferred_element_type=jnp.float32
    ) + jnp.einsum("rpg,rph->rgh", onehot, weight_lo, preferred_element_type=jnp.float32)
    x_scaled = x_tab.astype(jnp.float32).reshape(GRAMS, HEADS, HD)[None] * per_gram[..., None]
    start_state = jnp.einsum("rghp,gn->rhpn", x_scaled, b_tab, precision=HIGH)

    def mine(values):
        fwd = lax.dynamic_slice_in_dim(values[:windows], fwd_start, count, axis=1)
        rc = lax.dynamic_slice_in_dim(values[windows:], rc_start, count, axis=1)
        return jnp.concatenate([fwd, rc], axis=0)

    act = jnp.take(activated_tab, mine(gram), axis=0)
    x_act = act[..., :INNER].astype(jnp.bfloat16)
    b_all = act[..., INNER : INNER + NS]
    c_all = act[..., INNER + NS :]
    local_tok = jnp.concatenate([tokens, (BASES - 1) - tokens[:, ::-1]], axis=0)
    gate_z = jnp.take(z_rows, local_tok, axis=0)
    blocks = (
        to_blocks(x_act.reshape(streams, count, HEADS, HD), BLK),
        to_blocks(b_all, BLK),
        to_blocks(c_all, BLK),
        jnp.swapaxes(to_blocks(mine(log_decay), BLK), 2, 3),
        jnp.swapaxes(to_blocks(mine(step_dt), BLK), 2, 3),
    )
    _, y_blocks = lax.scan(ssd_block, start_state, blocks)
    y_local = jnp.moveaxis(y_blocks, 0, 1).reshape(streams, count, HEADS, HD)
    y_all = y_local + d_skip[:, None] * x_act.astype(jnp.float32).reshape(
        streams, count, HEADS, HD
    )
    gated_y = y_all * jax.nn.silu(gate_z.astype(jnp.float32)).reshape(streams, count, HEADS, HD)
    normed = (
        rms_gain(gated_y, inner_gain.reshape(HEADS, HD))
        .astype(jnp.bfloat16)
        .reshape(streams, count, INNER)
    )
    outputs = jnp.einsum("gre,ed->grd", normed, w_out, preferred_element_type=jnp.float32).astype(
        jnp.bfloat16
    )

    embedded = jnp.take(emb_full, tokens, axis=0)
    returned = outputs[windows:, ::-1, ::-1]
    hidden_out = (
        embedded.astype(jnp.float32)
        + outputs[:windows].astype(jnp.float32)
        + returned.astype(jnp.float32)
    ).astype(jnp.bfloat16)
    final_normed = rms_gain(hidden_out.astype(jnp.float32), final_gain).astype(jnp.bfloat16)
    head_full = jnp.concatenate([w_head_half, w_head_half[::-1, ::-1]], axis=1)
    logits = jnp.einsum("grd,db->grb", final_normed, head_full, preferred_element_type=jnp.float32)
    log_q = logits - jnp.log(jnp.sum(jnp.exp(logits), axis=-1, keepdims=True))
    top_value = jnp.max(teacher_vals, axis=1, keepdims=True)
    shifted = teacher_vals - top_value
    log_p = shifted - jnp.log(jnp.sum(jnp.exp(shifted), axis=1, keepdims=True))
    matches = teacher_top[..., None] == jnp.arange(4, dtype=jnp.int32)
    picked = jnp.sum(jnp.where(matches, log_q[:, None, :, :], 0.0), axis=-1)
    divergence = jnp.sum(jnp.exp(log_p) * (log_p - picked), axis=1)
    return (hidden_out, divergence)


def solution(mesh):
    placed = (
        P("grp", "seq"),
        P(),
        P(),
        P(),
        P(),
        P(),
        P(),
        P(),
        P(),
        P(),
        P(),
        P(),
        P(),
        P(),
        P(),
        P("grp", None, "seq"),
        P("grp", None, "seq"),
    )
    return jax.shard_map(
        local,
        mesh=mesh,
        in_specs=placed,
        out_specs=(P("grp", "seq", None), P("grp", "seq")),
        check_vma=False,
    )
```

```python
import jax
import jax.numpy as jnp
import numpy as np
from jax import lax
from jax.sharding import PartitionSpec as P

INNER = 1024
HD = 64
NS = 64
KW = 4
BLK = 128
HEADS = 16
CONVW = 1152
BASES = 4
GRAMS = 344


EPS = 1e-05
HIGH = lax.Precision.HIGHEST


def rms_gain(values, gain_row):
    return values * lax.rsqrt(jnp.mean(values * values, axis=-1, keepdims=True) + EPS) * gain_row


def to_blocks(values, block_width):
    streams, count = (values.shape[0], values.shape[1])
    return jnp.moveaxis(
        values.reshape((streams, count // block_width, block_width) + values.shape[2:]), 1, 0
    )


def ssd_block(carry_state, block_in):
    x_blk, b_blk, c_blk, decay_blk, dt_blk = block_in
    cumulated = jnp.cumsum(decay_blk, axis=2)
    block_len = decay_blk.shape[2]
    scores = jnp.einsum("gtn,gsn->gts", c_blk, b_blk, precision=HIGH)
    seg_diff = cumulated[:, :, :, None] - cumulated[:, :, None, :]
    lower_mask = jnp.arange(block_len)[:, None] >= jnp.arange(block_len)[None, :]
    decays = jnp.where(lower_mask, jnp.exp(jnp.where(lower_mask, seg_diff, 0.0)), 0.0)
    weights = (scores[:, None] * decays * dt_blk[:, :, None, :]).astype(jnp.bfloat16)
    y_intra = jnp.einsum("ghts,gshp->gthp", weights, x_blk, preferred_element_type=jnp.float32)
    y_inter = (
        jnp.einsum("gtn,ghpn->gthp", c_blk, carry_state, precision=HIGH)
        * jnp.swapaxes(jnp.exp(cumulated), 1, 2)[..., None]
    )
    last_cum = cumulated[:, :, -1:]
    scaled = jnp.exp(last_cum - cumulated) * dt_blk
    x_weighted = x_blk.astype(jnp.float32) * jnp.swapaxes(scaled, 1, 2)[..., None]
    new_state = jnp.exp(last_cum)[..., None] * carry_state + jnp.einsum(
        "gshp,gsn->ghpn", x_weighted, b_blk, precision=HIGH
    )
    return (new_state, y_intra + y_inter)


def gram_layout():
    rows = []
    for real in range(1, KW + 1):
        for code in range(BASES**real):
            taps = [None] * (KW - real) + [
                (code // BASES ** (real - 1 - k)) % BASES for k in range(real)
            ]
            rows.append(taps)
    picks = np.zeros((GRAMS, KW * BASES), np.float32)
    for row, taps in enumerate(rows):
        for offset, base in enumerate(taps):
            if base is not None:
                picks[row, offset * BASES + base] = 1.0
    return picks


def gram_tables(emb_full, norm_gain, w_xbc, w_z, w_dt, conv_w, conv_bias):
    row_norm = rms_gain(emb_full.astype(jnp.float32), norm_gain).astype(jnp.bfloat16)
    xbc_rows = jnp.dot(row_norm, w_xbc, preferred_element_type=jnp.float32).astype(jnp.bfloat16)
    z_rows = jnp.dot(row_norm, w_z, preferred_element_type=jnp.float32).astype(jnp.bfloat16)
    dt_rows = jnp.dot(row_norm, w_dt, preferred_element_type=jnp.float32)
    taps = (conv_w[:, None, :] * xbc_rows.astype(jnp.float32)[None]).reshape(KW * BASES, CONVW)
    conv_sum = conv_bias + jnp.dot(jnp.asarray(gram_layout()), taps, precision=HIGH)
    return jax.nn.silu(conv_sum), z_rows, dt_rows


def gram_ids(seq_tok):
    streams, total = seq_tok.shape
    padded = jnp.concatenate([jnp.zeros((streams, KW - 1), seq_tok.dtype), seq_tok], axis=1)
    where_in = jnp.arange(total)[None, :]
    code = jnp.zeros_like(seq_tok)
    ids = jnp.zeros_like(seq_tok)
    offset_of = 0
    for real in range(1, KW + 1):
        code = code + padded[:, KW - real : KW - real + total] * BASES ** (real - 1)
        chosen = (where_in >= real - 1) if real == KW else (where_in == real - 1)
        ids = jnp.where(chosen, offset_of + code, ids)
        offset_of += BASES**real
    return ids


def gather_all(tokens, axis):
    count = lax.axis_size(axis)
    place = lax.axis_index(axis)
    held = tokens
    bit = 0
    while 2**bit < count:
        mask = 2**bit
        other = lax.ppermute(held, axis, [(src, src ^ mask) for src in range(count)])
        upper = (place // mask) % 2 == 1
        held = jnp.where(
            upper,
            jnp.concatenate([other, held], axis=1),
            jnp.concatenate([held, other], axis=1),
        )
        bit += 1
    return held


def base_lookup(rows, bases):
    picked = jnp.zeros(bases.shape + rows.shape[1:], jnp.float32)
    for base in range(BASES):
        picked = picked + jnp.where(
            (bases == base)[..., None], rows[base].astype(jnp.float32), 0.0
        )
    return picked


def local(
    tokens,
    emb_half,
    norm_gain,
    w_xbc,
    w_z,
    w_dt,
    conv_w,
    conv_bias,
    dt_bias,
    a_log,
    d_skip,
    inner_gain,
    w_out,
    final_gain,
    w_head_half,
    teacher_top,
    teacher_vals,
):
    windows, count = tokens.shape
    nseq = lax.axis_size("seq")
    place = lax.axis_index("seq")
    total = count * nseq
    nblk = total // BLK
    streams = 2 * windows

    emb_full = jnp.concatenate([emb_half, emb_half[::-1, ::-1]], axis=0)
    activated_tab, z_rows, dt_rows = gram_tables(
        emb_full, norm_gain, w_xbc, w_z, w_dt, conv_w, conv_bias
    )
    x_tab = activated_tab[:, :INNER].astype(jnp.bfloat16)
    b_tab = activated_tab[:, INNER : INNER + NS]

    every = gather_all(tokens, "seq")
    seq_tok = jnp.concatenate([every, (BASES - 1) - every[:, ::-1]], axis=0)
    gram = gram_ids(seq_tok)

    step_dt = jax.nn.softplus(base_lookup(dt_rows, seq_tok) + dt_bias)
    log_decay = -jnp.exp(a_log) * step_dt

    fwd_start = place * count
    rc_start = (nseq - 1 - place) * count
    start = jnp.concatenate(
        [jnp.full((windows,), fwd_start), jnp.full((windows,), rc_start)]
    )
    first_blk = start // BLK

    cum = jnp.cumsum(log_decay.reshape(streams, nblk, BLK, HEADS), axis=2)
    blk_total = cum[:, :, -1, :]
    within = jnp.exp(blk_total[:, :, None, :] - cum) * step_dt.reshape(
        streams, nblk, BLK, HEADS
    )
    blk_idx = jnp.arange(nblk)
    between = (blk_idx[None, :, None] < blk_idx[None, None, :]) & (
        blk_idx[None, None, :] < first_blk[:, None, None]
    )
    span = jnp.sum(
        jnp.where(between[..., None], blk_total[:, None, :, :], 0.0), axis=2
    )
    across = jnp.where(
        (blk_idx[None, :] < first_blk[:, None])[..., None], jnp.exp(span), 0.0
    )
    weight = (within * across[:, :, None, :]).reshape(streams, total, HEADS)

    onehot = (gram[..., None] == jnp.arange(GRAMS, dtype=gram.dtype)).astype(jnp.bfloat16)
    weight_hi = weight.astype(jnp.bfloat16)
    weight_lo = (weight - weight_hi.astype(jnp.float32)).astype(jnp.bfloat16)
    per_gram = jnp.einsum(
        "rpg,rph->rgh", onehot, weight_hi, preferred_element_type=jnp.float32
    ) + jnp.einsum("rpg,rph->rgh", onehot, weight_lo, preferred_element_type=jnp.float32)
    b_scaled = per_gram.transpose(0, 2, 1)[..., None] * b_tab[None, None]
    b_hi = b_scaled.astype(jnp.bfloat16)
    b_lo = (b_scaled - b_hi.astype(jnp.float32)).astype(jnp.bfloat16)
    x_heads = x_tab.reshape(GRAMS, HEADS, HD).transpose(1, 0, 2)
    start_state = jnp.einsum(
        "hgp,rhgn->rhpn", x_heads, b_hi, preferred_element_type=jnp.float32
    ) + jnp.einsum("hgp,rhgn->rhpn", x_heads, b_lo, preferred_element_type=jnp.float32)

    def mine(values):
        fwd = lax.dynamic_slice_in_dim(values[:windows], fwd_start, count, axis=1)
        rc = lax.dynamic_slice_in_dim(values[windows:], rc_start, count, axis=1)
        return jnp.concatenate([fwd, rc], axis=0)

    act = jnp.take(activated_tab, mine(gram), axis=0)
    x_act = act[..., :INNER].astype(jnp.bfloat16)
    b_all = act[..., INNER : INNER + NS]
    c_all = act[..., INNER + NS :]
    local_tok = jnp.concatenate([tokens, (BASES - 1) - tokens[:, ::-1]], axis=0)
    gate_z = jnp.take(z_rows, local_tok, axis=0)
    blocks = (
        to_blocks(x_act.reshape(streams, count, HEADS, HD), BLK),
        to_blocks(b_all, BLK),
        to_blocks(c_all, BLK),
        jnp.swapaxes(to_blocks(mine(log_decay), BLK), 2, 3),
        jnp.swapaxes(to_blocks(mine(step_dt), BLK), 2, 3),
    )
    _, y_blocks = lax.scan(ssd_block, start_state, blocks)
    y_local = jnp.moveaxis(y_blocks, 0, 1).reshape(streams, count, HEADS, HD)
    y_all = y_local + d_skip[:, None] * x_act.astype(jnp.float32).reshape(
        streams, count, HEADS, HD
    )
    gated_y = y_all * jax.nn.silu(gate_z.astype(jnp.float32)).reshape(streams, count, HEADS, HD)
    normed = (
        rms_gain(gated_y, inner_gain.reshape(HEADS, HD))
        .astype(jnp.bfloat16)
        .reshape(streams, count, INNER)
    )
    outputs = jnp.einsum("gre,ed->grd", normed, w_out, preferred_element_type=jnp.float32).astype(
        jnp.bfloat16
    )

    embedded = jnp.take(emb_full, tokens, axis=0)
    returned = outputs[windows:, ::-1, ::-1]
    hidden_out = (
        embedded.astype(jnp.float32)
        + outputs[:windows].astype(jnp.float32)
        + returned.astype(jnp.float32)
    ).astype(jnp.bfloat16)
    final_normed = rms_gain(hidden_out.astype(jnp.float32), final_gain).astype(jnp.bfloat16)
    head_full = jnp.concatenate([w_head_half, w_head_half[::-1, ::-1]], axis=1)
    logits = jnp.einsum("grd,db->grb", final_normed, head_full, preferred_element_type=jnp.float32)
    log_q = logits - jnp.log(jnp.sum(jnp.exp(logits), axis=-1, keepdims=True))
    top_value = jnp.max(teacher_vals, axis=1, keepdims=True)
    shifted = teacher_vals - top_value
    log_p = shifted - jnp.log(jnp.sum(jnp.exp(shifted), axis=1, keepdims=True))
    matches = teacher_top[..., None] == jnp.arange(4, dtype=jnp.int32)
    picked = jnp.sum(jnp.where(matches, log_q[:, None, :, :], 0.0), axis=-1)
    divergence = jnp.sum(jnp.exp(log_p) * (log_p - picked), axis=1)
    return (hidden_out, divergence)


def solution(mesh):
    placed = (
        P("grp", "seq"),
        P(),
        P(),
        P(),
        P(),
        P(),
        P(),
        P(),
        P(),
        P(),
        P(),
        P(),
        P(),
        P(),
        P(),
        P("grp", None, "seq"),
        P("grp", None, "seq"),
    )
    return jax.shard_map(
        local,
        mesh=mesh,
        in_specs=placed,
        out_specs=(P("grp", "seq", None), P("grp", "seq")),
        check_vma=False,
    )
```

```python
import jax
import jax.numpy as jnp
import numpy as np
from jax import lax
from jax.sharding import PartitionSpec as P

INNER = 1024
HD = 64
NS = 64
KW = 4
BLK = 128
HEADS = 16
CONVW = 1152
BASES = 4
GRAMS = 344


EPS = 1e-05
HIGH = lax.Precision.HIGHEST


def rms_gain(values, gain_row):
    return values * lax.rsqrt(jnp.mean(values * values, axis=-1, keepdims=True) + EPS) * gain_row


def to_blocks(values, block_width):
    streams, count = (values.shape[0], values.shape[1])
    return jnp.moveaxis(
        values.reshape((streams, count // block_width, block_width) + values.shape[2:]), 1, 0
    )


def ssd_block(carry_state, block_in):
    x_blk, b_blk, c_blk, decay_blk, dt_blk = block_in
    cumulated = jnp.cumsum(decay_blk, axis=2)
    block_len = decay_blk.shape[2]
    scores = jnp.einsum("gtn,gsn->gts", c_blk, b_blk, precision=HIGH)
    seg_diff = cumulated[:, :, :, None] - cumulated[:, :, None, :]
    lower_mask = jnp.arange(block_len)[:, None] >= jnp.arange(block_len)[None, :]
    decays = jnp.where(lower_mask, jnp.exp(jnp.where(lower_mask, seg_diff, 0.0)), 0.0)
    weights = (scores[:, None] * decays * dt_blk[:, :, None, :]).astype(jnp.bfloat16)
    y_intra = jnp.einsum("ghts,gshp->gthp", weights, x_blk, preferred_element_type=jnp.float32)
    y_inter = (
        jnp.einsum("gtn,ghpn->gthp", c_blk, carry_state, precision=HIGH)
        * jnp.swapaxes(jnp.exp(cumulated), 1, 2)[..., None]
    )
    last_cum = cumulated[:, :, -1:]
    scaled = jnp.exp(last_cum - cumulated) * dt_blk
    x_weighted = x_blk.astype(jnp.float32) * jnp.swapaxes(scaled, 1, 2)[..., None]
    new_state = jnp.exp(last_cum)[..., None] * carry_state + jnp.einsum(
        "gshp,gsn->ghpn", x_weighted, b_blk, precision=HIGH
    )
    return (new_state, y_intra + y_inter)


def gram_layout():
    rows = []
    for real in range(1, KW + 1):
        for code in range(BASES**real):
            taps = [None] * (KW - real) + [
                (code // BASES ** (real - 1 - k)) % BASES for k in range(real)
            ]
            rows.append(taps)
    picks = np.zeros((GRAMS, KW * BASES), np.float32)
    for row, taps in enumerate(rows):
        for offset, base in enumerate(taps):
            if base is not None:
                picks[row, offset * BASES + base] = 1.0
    return picks


def gram_tables(emb_full, norm_gain, w_xbc, w_z, w_dt, conv_w, conv_bias):
    row_norm = rms_gain(emb_full.astype(jnp.float32), norm_gain).astype(jnp.bfloat16)
    xbc_rows = jnp.dot(row_norm, w_xbc, preferred_element_type=jnp.float32).astype(jnp.bfloat16)
    z_rows = jnp.dot(row_norm, w_z, preferred_element_type=jnp.float32).astype(jnp.bfloat16)
    dt_rows = jnp.dot(row_norm, w_dt, preferred_element_type=jnp.float32)
    taps = (conv_w[:, None, :] * xbc_rows.astype(jnp.float32)[None]).reshape(KW * BASES, CONVW)
    conv_sum = conv_bias + jnp.dot(jnp.asarray(gram_layout()), taps, precision=HIGH)
    return jax.nn.silu(conv_sum), z_rows, dt_rows


def gram_ids(ext, where_in):
    count = where_in.shape[1]
    code = jnp.zeros_like(where_in)
    ids = jnp.zeros_like(where_in)
    offset_of = 0
    for real in range(1, KW + 1):
        code = code + ext[:, KW - real : KW - real + count] * BASES ** (real - 1)
        chosen = (where_in >= real - 1) if real == KW else (where_in == real - 1)
        ids = jnp.where(chosen, offset_of + code, ids)
        offset_of += BASES**real
    return ids


def gather_all(tokens, axis):
    count = lax.axis_size(axis)
    place = lax.axis_index(axis)
    held = tokens
    bit = 0
    while 2**bit < count:
        mask = 2**bit
        other = lax.ppermute(held, axis, [(src, src ^ mask) for src in range(count)])
        upper = (place // mask) % 2 == 1
        held = jnp.where(
            upper,
            jnp.concatenate([other, held], axis=1),
            jnp.concatenate([held, other], axis=1),
        )
        bit += 1
    return held


def heads_lookup(rows, bases):
    picked = jnp.zeros(bases.shape[:-1] + (rows.shape[1], bases.shape[-1]), jnp.float32)
    for base in range(BASES):
        picked = picked + jnp.where(
            (bases == base)[..., None, :], rows[base][:, None], 0.0
        )
    return picked


def onehot(ids, size):
    return (ids[..., None] == jnp.arange(size, dtype=ids.dtype)).astype(jnp.bfloat16)


def split_bf16(values):
    high = values.astype(jnp.bfloat16)
    return high, (values - high.astype(jnp.float32)).astype(jnp.bfloat16)


def block_cumsum(values, tri):
    return jnp.einsum("...s,st->...t", values, tri, precision=HIGH)


def local(
    tokens,
    emb_half,
    norm_gain,
    w_xbc,
    w_z,
    w_dt,
    conv_w,
    conv_bias,
    dt_bias,
    a_log,
    d_skip,
    inner_gain,
    w_out,
    final_gain,
    w_head_half,
    teacher_top,
    teacher_vals,
):
    windows, count = tokens.shape
    nseq = lax.axis_size("seq")
    place = lax.axis_index("seq")
    total = count * nseq
    nblk = total // BLK
    nloc = count // BLK
    streams = 2 * windows
    units = streams * nloc
    tri = (jnp.arange(BLK)[:, None] <= jnp.arange(BLK)[None, :]).astype(jnp.float32)

    emb_full = jnp.concatenate([emb_half, emb_half[::-1, ::-1]], axis=0)
    act_tab, z_rows, dt_rows = gram_tables(emb_full, norm_gain, w_xbc, w_z, w_dt, conv_w, conv_bias)
    x_tab = act_tab[:, :INNER].astype(jnp.bfloat16)
    b_tab = act_tab[:, INNER : INNER + NS]
    bc_tab = act_tab[:, INNER:]
    x_heads = x_tab.reshape(GRAMS, HEADS, HD).transpose(1, 0, 2)
    neg_rate = -jnp.exp(a_log)[:, None]

    rc_tok = (BASES - 1) - tokens[:, ::-1]
    fwd_rim = lax.ppermute(
        tokens[:, count - (KW - 1) :], "seq", [(src, src + 1) for src in range(nseq - 1)]
    )
    rc_rim = lax.ppermute(
        rc_tok[:, count - (KW - 1) :], "seq", [(src, src - 1) for src in range(1, nseq)]
    )
    local_tok = jnp.concatenate([tokens, rc_tok], axis=0)
    ext = jnp.concatenate([jnp.concatenate([fwd_rim, rc_rim], axis=0), local_tok], axis=1)
    pos0 = jnp.concatenate(
        [jnp.full((windows, 1), place * count), jnp.full((windows, 1), (nseq - 1 - place) * count)]
    ).astype(jnp.int32)
    local_gram = gram_ids(ext, pos0 + jnp.arange(count, dtype=jnp.int32)[None, :])

    oh_loc = onehot(local_gram, GRAMS)
    x_loc = jnp.einsum("rtg,gc->rtc", oh_loc, x_tab, preferred_element_type=jnp.float32).astype(
        jnp.bfloat16
    )
    bc_loc = jnp.einsum("rtg,gc->rtc", oh_loc, bc_tab, precision=HIGH)
    oh_tok = onehot(local_tok, BASES)
    z_loc = jnp.einsum("rtk,kc->rtc", oh_tok, z_rows, preferred_element_type=jnp.float32)
    dt_loc = jax.nn.softplus(heads_lookup(dt_rows, local_tok) + dt_bias[:, None])
    ld_loc = neg_rate * dt_loc

    def per_unit(values, axis):
        shape = values.shape
        split = shape[:axis] + (nloc, BLK) + shape[axis + 1 :]
        moved = jnp.moveaxis(values.reshape(split), axis, 1)
        return moved.reshape((units,) + moved.shape[2:])

    x_u = per_unit(x_loc, 1).reshape(units, BLK, HEADS, HD)
    b_u = per_unit(bc_loc[..., :NS], 1)
    c_u = per_unit(bc_loc[..., NS:], 1)
    dt_u = per_unit(dt_loc, 2)
    cum_u = block_cumsum(per_unit(ld_loc, 2), tri)

    scores = jnp.einsum("utn,usn->uts", c_u, b_u, precision=HIGH)
    seg_diff = cum_u[:, :, :, None] - cum_u[:, :, None, :]
    lower = tri.T > 0
    decays = jnp.where(lower, jnp.exp(jnp.where(lower, seg_diff, 0.0)), 0.0)
    weights = (scores[:, None] * decays * dt_u[:, :, None, :]).astype(jnp.bfloat16)
    y_intra = jnp.einsum("uhts,ushp->uthp", weights, x_u, preferred_element_type=jnp.float32)

    every = gather_all(tokens, "seq")
    seq_tok = jnp.concatenate([every, (BASES - 1) - every[:, ::-1]], axis=0)
    ext_all = jnp.concatenate([jnp.zeros((streams, KW - 1), seq_tok.dtype), seq_tok], axis=1)
    gram = gram_ids(ext_all, jnp.broadcast_to(jnp.arange(total, dtype=jnp.int32), (streams, total)))
    dt_all = jax.nn.softplus(heads_lookup(dt_rows, seq_tok) + dt_bias[:, None])
    ld_all = neg_rate * dt_all
    cum = block_cumsum(ld_all.reshape(streams, HEADS, nblk, BLK), tri)
    blk_total = cum[..., -1]
    within = jnp.exp(blk_total[..., None] - cum) * dt_all.reshape(streams, HEADS, nblk, BLK)

    first_blk = (
        jnp.repeat(pos0[:, 0] // BLK, nloc) + jnp.tile(jnp.arange(nloc, dtype=jnp.int32), streams)
    )
    blk_idx = jnp.arange(nblk)
    total_u = jnp.repeat(blk_total, nloc, axis=0)
    between = (blk_idx[:, None] < blk_idx[None, :])[None] & (
        blk_idx[None, None, :] < first_blk[:, None, None]
    )
    span = jnp.sum(jnp.where(between[:, None], total_u[:, :, None, :], 0.0), axis=3)
    across = jnp.where(blk_idx[None, None, :] < first_blk[:, None, None], jnp.exp(span), 0.0)
    weight = (jnp.repeat(within, nloc, axis=0) * across[..., None]).reshape(units, HEADS, total)
    w_hi, w_lo = split_bf16(weight)
    oh_all = jnp.repeat(onehot(gram, GRAMS), nloc, axis=0)
    per_gram = jnp.einsum(
        "uhp,upg->uhg",
        jnp.concatenate([w_hi, w_lo], axis=1),
        oh_all,
        preferred_element_type=jnp.float32,
    )
    per_gram = per_gram[:, :HEADS] + per_gram[:, HEADS:]
    b_hi, b_lo = split_bf16(per_gram[..., None] * b_tab[None, None])
    start_state = jnp.einsum(
        "hgp,uhgn->uhpn", x_heads, b_hi, preferred_element_type=jnp.float32
    ) + jnp.einsum("hgp,uhgn->uhpn", x_heads, b_lo, preferred_element_type=jnp.float32)

    y_inter = (
        jnp.einsum("utn,uhpn->uthp", c_u, start_state, precision=HIGH)
        * jnp.exp(cum_u).transpose(0, 2, 1)[..., None]
    )
    y_u = y_intra + y_inter + d_skip[:, None] * x_u.astype(jnp.float32)
    z_u = per_unit(z_loc, 1).reshape(units, BLK, HEADS, HD)
    gated_y = y_u * jax.nn.silu(z_u)
    normed = rms_gain(gated_y, inner_gain.reshape(HEADS, HD)).astype(jnp.bfloat16)
    normed = jnp.moveaxis(normed.reshape(streams, nloc, BLK, INNER), 1, 1).reshape(
        streams, count, INNER
    )
    outputs = jnp.einsum("gre,ed->grd", normed, w_out, preferred_element_type=jnp.float32).astype(
        jnp.bfloat16
    )

    embedded = jnp.einsum(
        "grk,kd->grd", oh_tok[:windows], emb_full, preferred_element_type=jnp.float32
    ).astype(jnp.bfloat16)
    returned = outputs[windows:, ::-1, ::-1]
    hidden_out = (
        embedded.astype(jnp.float32)
        + outputs[:windows].astype(jnp.float32)
        + returned.astype(jnp.float32)
    ).astype(jnp.bfloat16)
    final_normed = rms_gain(hidden_out.astype(jnp.float32), final_gain).astype(jnp.bfloat16)
    head_full = jnp.concatenate([w_head_half, w_head_half[::-1, ::-1]], axis=1)
    logits = jnp.einsum("grd,db->grb", final_normed, head_full, preferred_element_type=jnp.float32)
    log_q = logits - jnp.log(jnp.sum(jnp.exp(logits), axis=-1, keepdims=True))
    top_value = jnp.max(teacher_vals, axis=1, keepdims=True)
    shifted = teacher_vals - top_value
    log_p = shifted - jnp.log(jnp.sum(jnp.exp(shifted), axis=1, keepdims=True))
    matches = teacher_top[..., None] == jnp.arange(4, dtype=jnp.int32)
    picked = jnp.sum(jnp.where(matches, log_q[:, None, :, :], 0.0), axis=-1)
    divergence = jnp.sum(jnp.exp(log_p) * (log_p - picked), axis=1)
    return (hidden_out, divergence)


def solution(mesh):
    placed = (
        P("grp", "seq"),
        P(),
        P(),
        P(),
        P(),
        P(),
        P(),
        P(),
        P(),
        P(),
        P(),
        P(),
        P(),
        P(),
        P(),
        P("grp", None, "seq"),
        P("grp", None, "seq"),
    )
    return jax.shard_map(
        local,
        mesh=mesh,
        in_specs=placed,
        out_specs=(P("grp", "seq", None), P("grp", "seq")),
        check_vma=False,
    )
```

```python
import jax
import jax.numpy as jnp
import numpy as np
from jax import lax
from jax.sharding import PartitionSpec as P

INNER = 1024
HD = 64
NS = 64
KW = 4
BLK = 128
HEADS = 16
CONVW = 1152
BASES = 4
GRAMS = 344


EPS = 1e-05
HIGH = lax.Precision.HIGHEST


def rms_gain(values, gain_row):
    return values * lax.rsqrt(jnp.mean(values * values, axis=-1, keepdims=True) + EPS) * gain_row


def to_blocks(values, block_width):
    streams, count = (values.shape[0], values.shape[1])
    return jnp.moveaxis(
        values.reshape((streams, count // block_width, block_width) + values.shape[2:]), 1, 0
    )


def ssd_block(carry_state, block_in):
    x_blk, b_blk, c_blk, decay_blk, dt_blk = block_in
    cumulated = jnp.cumsum(decay_blk, axis=2)
    block_len = decay_blk.shape[2]
    scores = jnp.einsum("gtn,gsn->gts", c_blk, b_blk, precision=HIGH)
    seg_diff = cumulated[:, :, :, None] - cumulated[:, :, None, :]
    lower_mask = jnp.arange(block_len)[:, None] >= jnp.arange(block_len)[None, :]
    decays = jnp.where(lower_mask, jnp.exp(jnp.where(lower_mask, seg_diff, 0.0)), 0.0)
    weights = (scores[:, None] * decays * dt_blk[:, :, None, :]).astype(jnp.bfloat16)
    y_intra = jnp.einsum("ghts,gshp->gthp", weights, x_blk, preferred_element_type=jnp.float32)
    y_inter = (
        jnp.einsum("gtn,ghpn->gthp", c_blk, carry_state, precision=HIGH)
        * jnp.swapaxes(jnp.exp(cumulated), 1, 2)[..., None]
    )
    last_cum = cumulated[:, :, -1:]
    scaled = jnp.exp(last_cum - cumulated) * dt_blk
    x_weighted = x_blk.astype(jnp.float32) * jnp.swapaxes(scaled, 1, 2)[..., None]
    new_state = jnp.exp(last_cum)[..., None] * carry_state + jnp.einsum(
        "gshp,gsn->ghpn", x_weighted, b_blk, precision=HIGH
    )
    return (new_state, y_intra + y_inter)


def gram_layout():
    rows = []
    for real in range(1, KW + 1):
        for code in range(BASES**real):
            taps = [None] * (KW - real) + [
                (code // BASES ** (real - 1 - k)) % BASES for k in range(real)
            ]
            rows.append(taps)
    picks = np.zeros((GRAMS, KW * BASES), np.float32)
    for row, taps in enumerate(rows):
        for offset, base in enumerate(taps):
            if base is not None:
                picks[row, offset * BASES + base] = 1.0
    return picks


def gram_tables(emb_full, norm_gain, w_xbc, w_z, w_dt, conv_w, conv_bias):
    row_norm = rms_gain(emb_full.astype(jnp.float32), norm_gain).astype(jnp.bfloat16)
    xbc_rows = jnp.dot(row_norm, w_xbc, preferred_element_type=jnp.float32).astype(jnp.bfloat16)
    z_rows = jnp.dot(row_norm, w_z, preferred_element_type=jnp.float32).astype(jnp.bfloat16)
    dt_rows = jnp.dot(row_norm, w_dt, preferred_element_type=jnp.float32)
    taps = (conv_w[:, None, :] * xbc_rows.astype(jnp.float32)[None]).reshape(KW * BASES, CONVW)
    conv_sum = conv_bias + jnp.dot(jnp.asarray(gram_layout()), taps, precision=HIGH)
    return jax.nn.silu(conv_sum), z_rows, dt_rows


def gram_ids(ext, where_in):
    count = where_in.shape[1]
    code = jnp.zeros_like(where_in)
    ids = jnp.zeros_like(where_in)
    offset_of = 0
    for real in range(1, KW + 1):
        code = code + ext[:, KW - real : KW - real + count] * BASES ** (real - 1)
        chosen = (where_in >= real - 1) if real == KW else (where_in == real - 1)
        ids = jnp.where(chosen, offset_of + code, ids)
        offset_of += BASES**real
    return ids


def gather_all(tokens, axis):
    count = lax.axis_size(axis)
    place = lax.axis_index(axis)
    held = tokens
    bit = 0
    while 2**bit < count:
        mask = 2**bit
        other = lax.ppermute(held, axis, [(src, src ^ mask) for src in range(count)])
        upper = (place // mask) % 2 == 1
        held = jnp.where(
            upper,
            jnp.concatenate([other, held], axis=1),
            jnp.concatenate([held, other], axis=1),
        )
        bit += 1
    return held


def heads_lookup(rows, bases):
    picked = jnp.zeros(bases.shape[:-1] + (rows.shape[1], bases.shape[-1]), jnp.float32)
    for base in range(BASES):
        picked = picked + jnp.where(
            (bases == base)[..., None, :], rows[base][:, None], 0.0
        )
    return picked


def onehot(ids, size):
    return (ids[..., None] == jnp.arange(size, dtype=ids.dtype)).astype(jnp.bfloat16)


def split_bf16(values):
    high = values.astype(jnp.bfloat16)
    return high, (values - high.astype(jnp.float32)).astype(jnp.bfloat16)


def block_cumsum(values, tri):
    return jnp.einsum("...s,st->...t", values, tri, precision=HIGH)


def local(
    tokens,
    emb_half,
    norm_gain,
    w_xbc,
    w_z,
    w_dt,
    conv_w,
    conv_bias,
    dt_bias,
    a_log,
    d_skip,
    inner_gain,
    w_out,
    final_gain,
    w_head_half,
    teacher_top,
    teacher_vals,
):
    windows, count = tokens.shape
    nseq = lax.axis_size("seq")
    place = lax.axis_index("seq")
    total = count * nseq
    nblk = total // BLK
    nloc = count // BLK
    streams = 2 * windows
    units = streams * nloc
    tri = (jnp.arange(BLK)[:, None] <= jnp.arange(BLK)[None, :]).astype(jnp.float32)

    emb_full = jnp.concatenate([emb_half, emb_half[::-1, ::-1]], axis=0)
    act_tab, z_rows, dt_rows = gram_tables(emb_full, norm_gain, w_xbc, w_z, w_dt, conv_w, conv_bias)
    x_tab = act_tab[:, :INNER].astype(jnp.bfloat16)
    b_tab = act_tab[:, INNER : INNER + NS]
    bc_tab = act_tab[:, INNER:]
    x_heads = x_tab.reshape(GRAMS, HEADS, HD).transpose(1, 0, 2)
    neg_rate = -jnp.exp(a_log)[:, None]

    rc_tok = (BASES - 1) - tokens[:, ::-1]
    fwd_rim = lax.ppermute(
        tokens[:, count - (KW - 1) :], "seq", [(src, src + 1) for src in range(nseq - 1)]
    )
    rc_rim = lax.ppermute(
        rc_tok[:, count - (KW - 1) :], "seq", [(src, src - 1) for src in range(1, nseq)]
    )
    local_tok = jnp.concatenate([tokens, rc_tok], axis=0)
    ext = jnp.concatenate([jnp.concatenate([fwd_rim, rc_rim], axis=0), local_tok], axis=1)
    pos0 = jnp.concatenate(
        [jnp.full((windows, 1), place * count), jnp.full((windows, 1), (nseq - 1 - place) * count)]
    ).astype(jnp.int32)
    local_gram = gram_ids(ext, pos0 + jnp.arange(count, dtype=jnp.int32)[None, :])

    oh_loc = onehot(local_gram, GRAMS)
    x_loc = jnp.einsum("rtg,gc->rtc", oh_loc, x_tab, preferred_element_type=jnp.float32).astype(
        jnp.bfloat16
    )
    bc_loc = jnp.einsum("rtg,gc->rtc", oh_loc, bc_tab, precision=HIGH)
    oh_tok = onehot(local_tok, BASES)
    z_loc = jnp.einsum("rtk,kc->rtc", oh_tok, z_rows, preferred_element_type=jnp.float32)
    dt_loc = jax.nn.softplus(heads_lookup(dt_rows, local_tok) + dt_bias[:, None])
    ld_loc = neg_rate * dt_loc

    def per_unit(values, axis):
        shape = values.shape
        split = shape[:axis] + (nloc, BLK) + shape[axis + 1 :]
        moved = jnp.moveaxis(values.reshape(split), axis, 1)
        return moved.reshape((units,) + moved.shape[2:])

    x_u = per_unit(x_loc, 1).reshape(units, BLK, HEADS, HD)
    b_u = per_unit(bc_loc[..., :NS], 1)
    c_u = per_unit(bc_loc[..., NS:], 1)
    dt_u = per_unit(dt_loc, 2)
    cum_u = block_cumsum(per_unit(ld_loc, 2), tri)

    scores = jnp.einsum("utn,usn->uts", c_u, b_u, precision=HIGH)
    seg_diff = cum_u[:, :, :, None] - cum_u[:, :, None, :]
    lower = tri.T > 0
    decays = jnp.where(lower, jnp.exp(jnp.where(lower, seg_diff, 0.0)), 0.0)
    weights = (scores[:, None] * decays * dt_u[:, :, None, :]).astype(jnp.bfloat16)
    y_intra = jnp.einsum("uhts,ushp->uthp", weights, x_u, preferred_element_type=jnp.float32)

    mine = jnp.concatenate([tokens, rc_tok], axis=0).astype(jnp.float32)
    slots = jnp.where(
        (jnp.arange(nseq) == place)[:, None, None], mine[None], 0.0
    )
    slots = lax.psum(slots, "seq").astype(jnp.int32)
    fwd_all = jnp.moveaxis(slots[:, :windows], 0, 1).reshape(windows, total)
    rc_all = jnp.moveaxis(slots[::-1, windows:], 0, 1).reshape(windows, total)
    seq_tok = jnp.concatenate([fwd_all, rc_all], axis=0)
    ext_all = jnp.concatenate([jnp.zeros((streams, KW - 1), seq_tok.dtype), seq_tok], axis=1)
    gram = gram_ids(ext_all, jnp.broadcast_to(jnp.arange(total, dtype=jnp.int32), (streams, total)))
    dt_all = jax.nn.softplus(heads_lookup(dt_rows, seq_tok) + dt_bias[:, None])
    ld_all = neg_rate * dt_all
    cum = block_cumsum(ld_all.reshape(streams, HEADS, nblk, BLK), tri)
    blk_total = cum[..., -1]
    within = jnp.exp(blk_total[..., None] - cum) * dt_all.reshape(streams, HEADS, nblk, BLK)

    first_blk = (
        jnp.repeat(pos0[:, 0] // BLK, nloc) + jnp.tile(jnp.arange(nloc, dtype=jnp.int32), streams)
    )
    blk_idx = jnp.arange(nblk)
    total_u = jnp.repeat(blk_total, nloc, axis=0)
    between = (blk_idx[:, None] < blk_idx[None, :])[None] & (
        blk_idx[None, None, :] < first_blk[:, None, None]
    )
    span = jnp.sum(jnp.where(between[:, None], total_u[:, :, None, :], 0.0), axis=3)
    across = jnp.where(blk_idx[None, None, :] < first_blk[:, None, None], jnp.exp(span), 0.0)
    weight = (jnp.repeat(within, nloc, axis=0) * across[..., None]).reshape(units, HEADS, total)
    w_hi, w_lo = split_bf16(weight)
    oh_all = jnp.repeat(onehot(gram, GRAMS), nloc, axis=0)
    per_gram = jnp.einsum(
        "uhp,upg->uhg",
        jnp.concatenate([w_hi, w_lo], axis=1),
        oh_all,
        preferred_element_type=jnp.float32,
    )
    per_gram = per_gram[:, :HEADS] + per_gram[:, HEADS:]
    b_hi, b_lo = split_bf16(per_gram[..., None] * b_tab[None, None])
    start_state = jnp.einsum(
        "hgp,uhgn->uhpn", x_heads, b_hi, preferred_element_type=jnp.float32
    ) + jnp.einsum("hgp,uhgn->uhpn", x_heads, b_lo, preferred_element_type=jnp.float32)

    y_inter = (
        jnp.einsum("utn,uhpn->uthp", c_u, start_state, precision=HIGH)
        * jnp.exp(cum_u).transpose(0, 2, 1)[..., None]
    )
    y_u = y_intra + y_inter + d_skip[:, None] * x_u.astype(jnp.float32)
    z_u = per_unit(z_loc, 1).reshape(units, BLK, HEADS, HD)
    gated_y = y_u * jax.nn.silu(z_u)
    normed = rms_gain(gated_y, inner_gain.reshape(HEADS, HD)).astype(jnp.bfloat16)
    normed = jnp.moveaxis(normed.reshape(streams, nloc, BLK, INNER), 1, 1).reshape(
        streams, count, INNER
    )
    outputs = jnp.einsum("gre,ed->grd", normed, w_out, preferred_element_type=jnp.float32).astype(
        jnp.bfloat16
    )

    embedded = jnp.einsum(
        "grk,kd->grd", oh_tok[:windows], emb_full, preferred_element_type=jnp.float32
    ).astype(jnp.bfloat16)
    returned = outputs[windows:, ::-1, ::-1]
    hidden_out = (
        embedded.astype(jnp.float32)
        + outputs[:windows].astype(jnp.float32)
        + returned.astype(jnp.float32)
    ).astype(jnp.bfloat16)
    final_normed = rms_gain(hidden_out.astype(jnp.float32), final_gain).astype(jnp.bfloat16)
    head_full = jnp.concatenate([w_head_half, w_head_half[::-1, ::-1]], axis=1)
    logits = jnp.einsum("grd,db->grb", final_normed, head_full, preferred_element_type=jnp.float32)
    log_q = logits - jnp.log(jnp.sum(jnp.exp(logits), axis=-1, keepdims=True))
    top_value = jnp.max(teacher_vals, axis=1, keepdims=True)
    shifted = teacher_vals - top_value
    log_p = shifted - jnp.log(jnp.sum(jnp.exp(shifted), axis=1, keepdims=True))
    matches = teacher_top[..., None] == jnp.arange(4, dtype=jnp.int32)
    picked = jnp.sum(jnp.where(matches, log_q[:, None, :, :], 0.0), axis=-1)
    divergence = jnp.sum(jnp.exp(log_p) * (log_p - picked), axis=1)
    return (hidden_out, divergence)


def solution(mesh):
    placed = (
        P("grp", "seq"),
        P(),
        P(),
        P(),
        P(),
        P(),
        P(),
        P(),
        P(),
        P(),
        P(),
        P(),
        P(),
        P(),
        P(),
        P("grp", None, "seq"),
        P("grp", None, "seq"),
    )
    return jax.shard_map(
        local,
        mesh=mesh,
        in_specs=placed,
        out_specs=(P("grp", "seq", None), P("grp", "seq")),
        check_vma=False,
    )
```

```python
import jax
import jax.numpy as jnp
import numpy as np
from jax import lax
from jax.sharding import PartitionSpec as P

INNER = 1024
HD = 64
NS = 64
KW = 4
BLK = 128
HEADS = 16
CONVW = 1152
BASES = 4
GRAMS = 344


EPS = 1e-05
HIGH = lax.Precision.HIGHEST


def rms_gain(values, gain_row):
    return values * lax.rsqrt(jnp.mean(values * values, axis=-1, keepdims=True) + EPS) * gain_row


def to_blocks(values, block_width):
    streams, count = (values.shape[0], values.shape[1])
    return jnp.moveaxis(
        values.reshape((streams, count // block_width, block_width) + values.shape[2:]), 1, 0
    )


def ssd_block(carry_state, block_in):
    x_blk, b_blk, c_blk, decay_blk, dt_blk = block_in
    cumulated = jnp.cumsum(decay_blk, axis=2)
    block_len = decay_blk.shape[2]
    scores = jnp.einsum("gtn,gsn->gts", c_blk, b_blk, precision=HIGH)
    seg_diff = cumulated[:, :, :, None] - cumulated[:, :, None, :]
    lower_mask = jnp.arange(block_len)[:, None] >= jnp.arange(block_len)[None, :]
    decays = jnp.where(lower_mask, jnp.exp(jnp.where(lower_mask, seg_diff, 0.0)), 0.0)
    weights = (scores[:, None] * decays * dt_blk[:, :, None, :]).astype(jnp.bfloat16)
    y_intra = jnp.einsum("ghts,gshp->gthp", weights, x_blk, preferred_element_type=jnp.float32)
    y_inter = (
        jnp.einsum("gtn,ghpn->gthp", c_blk, carry_state, precision=HIGH)
        * jnp.swapaxes(jnp.exp(cumulated), 1, 2)[..., None]
    )
    last_cum = cumulated[:, :, -1:]
    scaled = jnp.exp(last_cum - cumulated) * dt_blk
    x_weighted = x_blk.astype(jnp.float32) * jnp.swapaxes(scaled, 1, 2)[..., None]
    new_state = jnp.exp(last_cum)[..., None] * carry_state + jnp.einsum(
        "gshp,gsn->ghpn", x_weighted, b_blk, precision=HIGH
    )
    return (new_state, y_intra + y_inter)


def gram_layout():
    rows = []
    for real in range(1, KW + 1):
        for code in range(BASES**real):
            taps = [None] * (KW - real) + [
                (code // BASES ** (real - 1 - k)) % BASES for k in range(real)
            ]
            rows.append(taps)
    picks = np.zeros((GRAMS, KW * BASES), np.float32)
    for row, taps in enumerate(rows):
        for offset, base in enumerate(taps):
            if base is not None:
                picks[row, offset * BASES + base] = 1.0
    return picks


def gram_tables(emb_full, norm_gain, w_xbc, w_z, w_dt, conv_w, conv_bias):
    row_norm = rms_gain(emb_full.astype(jnp.float32), norm_gain).astype(jnp.bfloat16)
    xbc_rows = jnp.dot(row_norm, w_xbc, preferred_element_type=jnp.float32).astype(jnp.bfloat16)
    z_rows = jnp.dot(row_norm, w_z, preferred_element_type=jnp.float32).astype(jnp.bfloat16)
    dt_rows = jnp.dot(row_norm, w_dt, preferred_element_type=jnp.float32)
    taps = (conv_w[:, None, :] * xbc_rows.astype(jnp.float32)[None]).reshape(KW * BASES, CONVW)
    conv_sum = conv_bias + jnp.dot(jnp.asarray(gram_layout()), taps, precision=HIGH)
    return jax.nn.silu(conv_sum), z_rows, dt_rows


def gram_ids(ext, where_in):
    count = where_in.shape[1]
    code = jnp.zeros_like(where_in)
    ids = jnp.zeros_like(where_in)
    offset_of = 0
    for real in range(1, KW + 1):
        code = code + ext[:, KW - real : KW - real + count] * BASES ** (real - 1)
        chosen = (where_in >= real - 1) if real == KW else (where_in == real - 1)
        ids = jnp.where(chosen, offset_of + code, ids)
        offset_of += BASES**real
    return ids


def gather_all(fwd, rc, axis):
    count = lax.axis_size(axis)
    place = lax.axis_index(axis)
    rows = fwd.shape[0]
    held = jnp.concatenate([fwd, rc], axis=0)
    bit = 0
    while 2**bit < count:
        mask = 2**bit
        other = lax.ppermute(held, axis, [(src, src ^ mask) for src in range(count)])
        upper = (place // mask) % 2 == 1
        low_first = jnp.concatenate([held, other], axis=1)
        high_first = jnp.concatenate([other, held], axis=1)
        held = jnp.concatenate(
            [
                jnp.where(upper, high_first[:rows], low_first[:rows]),
                jnp.where(upper, low_first[rows:], high_first[rows:]),
            ],
            axis=0,
        )
        bit += 1
    return held


def heads_lookup(rows, bases):
    picked = jnp.zeros(bases.shape[:-1] + (rows.shape[1], bases.shape[-1]), jnp.float32)
    for base in range(BASES):
        picked = picked + jnp.where(
            (bases == base)[..., None, :], rows[base][:, None], 0.0
        )
    return picked


def onehot(ids, size):
    return (ids[..., None] == jnp.arange(size, dtype=ids.dtype)).astype(jnp.bfloat16)


def split_bf16(values):
    high = values.astype(jnp.bfloat16)
    return high, (values - high.astype(jnp.float32)).astype(jnp.bfloat16)


def block_cumsum(values, tri):
    return jnp.einsum("...s,st->...t", values, tri, precision=HIGH)


def local(
    tokens,
    emb_half,
    norm_gain,
    w_xbc,
    w_z,
    w_dt,
    conv_w,
    conv_bias,
    dt_bias,
    a_log,
    d_skip,
    inner_gain,
    w_out,
    final_gain,
    w_head_half,
    teacher_top,
    teacher_vals,
):
    windows, count = tokens.shape
    nseq = lax.axis_size("seq")
    place = lax.axis_index("seq")
    total = count * nseq
    nblk = total // BLK
    nloc = count // BLK
    streams = 2 * windows
    units = streams * nloc
    tri = (jnp.arange(BLK)[:, None] <= jnp.arange(BLK)[None, :]).astype(jnp.float32)

    emb_full = jnp.concatenate([emb_half, emb_half[::-1, ::-1]], axis=0)
    act_tab, z_rows, dt_rows = gram_tables(emb_full, norm_gain, w_xbc, w_z, w_dt, conv_w, conv_bias)
    x_tab = act_tab[:, :INNER].astype(jnp.bfloat16)
    b_tab = act_tab[:, INNER : INNER + NS]
    bc_tab = act_tab[:, INNER:]
    x_heads = x_tab.reshape(GRAMS, HEADS, HD).transpose(1, 0, 2)
    neg_rate = -jnp.exp(a_log)[:, None]

    rc_tok = (BASES - 1) - tokens[:, ::-1]
    fwd_rim = lax.ppermute(
        tokens[:, count - (KW - 1) :], "seq", [(src, src + 1) for src in range(nseq - 1)]
    )
    rc_rim = lax.ppermute(
        rc_tok[:, count - (KW - 1) :], "seq", [(src, src - 1) for src in range(1, nseq)]
    )
    local_tok = jnp.concatenate([tokens, rc_tok], axis=0)
    ext = jnp.concatenate([jnp.concatenate([fwd_rim, rc_rim], axis=0), local_tok], axis=1)
    pos0 = jnp.concatenate(
        [jnp.full((windows, 1), place * count), jnp.full((windows, 1), (nseq - 1 - place) * count)]
    ).astype(jnp.int32)
    local_gram = gram_ids(ext, pos0 + jnp.arange(count, dtype=jnp.int32)[None, :])

    oh_loc = onehot(local_gram, GRAMS)
    x_loc = jnp.einsum("rtg,gc->rtc", oh_loc, x_tab, preferred_element_type=jnp.float32).astype(
        jnp.bfloat16
    )
    bc_loc = jnp.einsum("rtg,gc->rtc", oh_loc, bc_tab, precision=HIGH)
    oh_tok = onehot(local_tok, BASES)
    z_loc = jnp.einsum("rtk,kc->rtc", oh_tok, z_rows, preferred_element_type=jnp.float32)
    dt_loc = jax.nn.softplus(heads_lookup(dt_rows, local_tok) + dt_bias[:, None])
    ld_loc = neg_rate * dt_loc

    def per_unit(values, axis):
        shape = values.shape
        split = shape[:axis] + (nloc, BLK) + shape[axis + 1 :]
        moved = jnp.moveaxis(values.reshape(split), axis, 1)
        return moved.reshape((units,) + moved.shape[2:])

    x_u = per_unit(x_loc, 1).reshape(units, BLK, HEADS, HD)
    b_u = per_unit(bc_loc[..., :NS], 1)
    c_u = per_unit(bc_loc[..., NS:], 1)
    dt_u = per_unit(dt_loc, 2)
    cum_u = block_cumsum(per_unit(ld_loc, 2), tri)

    scores = jnp.einsum("utn,usn->uts", c_u, b_u, precision=HIGH)
    seg_diff = cum_u[:, :, :, None] - cum_u[:, :, None, :]
    lower = tri.T > 0
    decays = jnp.where(lower, jnp.exp(jnp.where(lower, seg_diff, 0.0)), 0.0)
    weights = (scores[:, None] * decays * dt_u[:, :, None, :]).astype(jnp.bfloat16)
    y_intra = jnp.einsum("uhts,ushp->uthp", weights, x_u, preferred_element_type=jnp.float32)

    seq_tok = gather_all(tokens, rc_tok, "seq")
    ext_all = jnp.concatenate([jnp.zeros((streams, KW - 1), seq_tok.dtype), seq_tok], axis=1)
    gram = gram_ids(ext_all, jnp.broadcast_to(jnp.arange(total, dtype=jnp.int32), (streams, total)))
    dt_all = jax.nn.softplus(heads_lookup(dt_rows, seq_tok) + dt_bias[:, None])
    ld_all = neg_rate * dt_all
    cum = block_cumsum(ld_all.reshape(streams, HEADS, nblk, BLK), tri)
    blk_total = cum[..., -1]
    within = jnp.exp(blk_total[..., None] - cum) * dt_all.reshape(streams, HEADS, nblk, BLK)

    first_blk = (
        jnp.repeat(pos0[:, 0] // BLK, nloc) + jnp.tile(jnp.arange(nloc, dtype=jnp.int32), streams)
    )
    blk_idx = jnp.arange(nblk)
    total_u = jnp.repeat(blk_total, nloc, axis=0)
    between = (blk_idx[:, None] < blk_idx[None, :])[None] & (
        blk_idx[None, None, :] < first_blk[:, None, None]
    )
    span = jnp.sum(jnp.where(between[:, None], total_u[:, :, None, :], 0.0), axis=3)
    across = jnp.where(blk_idx[None, None, :] < first_blk[:, None, None], jnp.exp(span), 0.0)
    weight = (jnp.repeat(within, nloc, axis=0) * across[..., None]).reshape(units, HEADS, total)
    w_hi, w_lo = split_bf16(weight)
    oh_all = jnp.repeat(onehot(gram, GRAMS), nloc, axis=0)
    per_gram = jnp.einsum(
        "uhp,upg->uhg",
        jnp.concatenate([w_hi, w_lo], axis=1),
        oh_all,
        preferred_element_type=jnp.float32,
    )
    per_gram = per_gram[:, :HEADS] + per_gram[:, HEADS:]
    b_hi, b_lo = split_bf16(per_gram[..., None] * b_tab[None, None])
    start_state = jnp.einsum(
        "hgp,uhgn->uhpn", x_heads, b_hi, preferred_element_type=jnp.float32
    ) + jnp.einsum("hgp,uhgn->uhpn", x_heads, b_lo, preferred_element_type=jnp.float32)

    y_inter = (
        jnp.einsum("utn,uhpn->uthp", c_u, start_state, precision=HIGH)
        * jnp.exp(cum_u).transpose(0, 2, 1)[..., None]
    )
    y_u = y_intra + y_inter + d_skip[:, None] * x_u.astype(jnp.float32)
    z_u = per_unit(z_loc, 1).reshape(units, BLK, HEADS, HD)
    gated_y = y_u * jax.nn.silu(z_u)
    normed = rms_gain(gated_y, inner_gain.reshape(HEADS, HD)).astype(jnp.bfloat16)
    normed = jnp.moveaxis(normed.reshape(streams, nloc, BLK, INNER), 1, 1).reshape(
        streams, count, INNER
    )
    outputs = jnp.einsum("gre,ed->grd", normed, w_out, preferred_element_type=jnp.float32).astype(
        jnp.bfloat16
    )

    embedded = jnp.einsum(
        "grk,kd->grd", oh_tok[:windows], emb_full, preferred_element_type=jnp.float32
    ).astype(jnp.bfloat16)
    returned = outputs[windows:, ::-1, ::-1]
    hidden_out = (
        embedded.astype(jnp.float32)
        + outputs[:windows].astype(jnp.float32)
        + returned.astype(jnp.float32)
    ).astype(jnp.bfloat16)
    final_normed = rms_gain(hidden_out.astype(jnp.float32), final_gain).astype(jnp.bfloat16)
    head_full = jnp.concatenate([w_head_half, w_head_half[::-1, ::-1]], axis=1)
    logits = jnp.einsum("grd,db->grb", final_normed, head_full, preferred_element_type=jnp.float32)
    log_q = logits - jnp.log(jnp.sum(jnp.exp(logits), axis=-1, keepdims=True))
    top_value = jnp.max(teacher_vals, axis=1, keepdims=True)
    shifted = teacher_vals - top_value
    log_p = shifted - jnp.log(jnp.sum(jnp.exp(shifted), axis=1, keepdims=True))
    matches = teacher_top[..., None] == jnp.arange(4, dtype=jnp.int32)
    picked = jnp.sum(jnp.where(matches, log_q[:, None, :, :], 0.0), axis=-1)
    divergence = jnp.sum(jnp.exp(log_p) * (log_p - picked), axis=1)
    return (hidden_out, divergence)


def solution(mesh):
    placed = (
        P("grp", "seq"),
        P(),
        P(),
        P(),
        P(),
        P(),
        P(),
        P(),
        P(),
        P(),
        P(),
        P(),
        P(),
        P(),
        P(),
        P("grp", None, "seq"),
        P("grp", None, "seq"),
    )
    return jax.shard_map(
        local,
        mesh=mesh,
        in_specs=placed,
        out_specs=(P("grp", "seq", None), P("grp", "seq")),
        check_vma=False,
    )
```

```python
import jax
import jax.numpy as jnp
import numpy as np
from jax import lax
from jax.sharding import PartitionSpec as P

INNER = 1024
HD = 64
NS = 64
KW = 4
BLK = 128
HEADS = 16
CONVW = 1152
BASES = 4
GRAMS = 344


EPS = 1e-05
HIGH = lax.Precision.HIGHEST


def rms_gain(values, gain_row):
    return values * lax.rsqrt(jnp.mean(values * values, axis=-1, keepdims=True) + EPS) * gain_row


def to_blocks(values, block_width):
    streams, count = (values.shape[0], values.shape[1])
    return jnp.moveaxis(
        values.reshape((streams, count // block_width, block_width) + values.shape[2:]), 1, 0
    )


def ssd_block(carry_state, block_in):
    x_blk, b_blk, c_blk, decay_blk, dt_blk = block_in
    cumulated = jnp.cumsum(decay_blk, axis=2)
    block_len = decay_blk.shape[2]
    scores = jnp.einsum("gtn,gsn->gts", c_blk, b_blk, precision=HIGH)
    seg_diff = cumulated[:, :, :, None] - cumulated[:, :, None, :]
    lower_mask = jnp.arange(block_len)[:, None] >= jnp.arange(block_len)[None, :]
    decays = jnp.where(lower_mask, jnp.exp(jnp.where(lower_mask, seg_diff, 0.0)), 0.0)
    weights = (scores[:, None] * decays * dt_blk[:, :, None, :]).astype(jnp.bfloat16)
    y_intra = jnp.einsum("ghts,gshp->gthp", weights, x_blk, preferred_element_type=jnp.float32)
    y_inter = (
        jnp.einsum("gtn,ghpn->gthp", c_blk, carry_state, precision=HIGH)
        * jnp.swapaxes(jnp.exp(cumulated), 1, 2)[..., None]
    )
    last_cum = cumulated[:, :, -1:]
    scaled = jnp.exp(last_cum - cumulated) * dt_blk
    x_weighted = x_blk.astype(jnp.float32) * jnp.swapaxes(scaled, 1, 2)[..., None]
    new_state = jnp.exp(last_cum)[..., None] * carry_state + jnp.einsum(
        "gshp,gsn->ghpn", x_weighted, b_blk, precision=HIGH
    )
    return (new_state, y_intra + y_inter)


def gram_layout():
    rows = []
    for real in range(1, KW + 1):
        for code in range(BASES**real):
            taps = [None] * (KW - real) + [
                (code // BASES ** (real - 1 - k)) % BASES for k in range(real)
            ]
            rows.append(taps)
    picks = np.zeros((GRAMS, KW * BASES), np.float32)
    for row, taps in enumerate(rows):
        for offset, base in enumerate(taps):
            if base is not None:
                picks[row, offset * BASES + base] = 1.0
    return picks


def gram_tables(emb_full, norm_gain, w_xbc, w_z, w_dt, conv_w, conv_bias):
    row_norm = rms_gain(emb_full.astype(jnp.float32), norm_gain).astype(jnp.bfloat16)
    xbc_rows = jnp.dot(row_norm, w_xbc, preferred_element_type=jnp.float32).astype(jnp.bfloat16)
    z_rows = jnp.dot(row_norm, w_z, preferred_element_type=jnp.float32).astype(jnp.bfloat16)
    dt_rows = jnp.dot(row_norm, w_dt, preferred_element_type=jnp.float32)
    taps = (conv_w[:, None, :] * xbc_rows.astype(jnp.float32)[None]).reshape(KW * BASES, CONVW)
    conv_sum = conv_bias + jnp.dot(jnp.asarray(gram_layout()), taps, precision=HIGH)
    return jax.nn.silu(conv_sum), z_rows, dt_rows


def gram_ids(ext, where_in):
    count = where_in.shape[1]
    code = jnp.zeros_like(where_in)
    ids = jnp.zeros_like(where_in)
    offset_of = 0
    for real in range(1, KW + 1):
        code = code + ext[:, KW - real : KW - real + count] * BASES ** (real - 1)
        chosen = (where_in >= real - 1) if real == KW else (where_in == real - 1)
        ids = jnp.where(chosen, offset_of + code, ids)
        offset_of += BASES**real
    return ids


def gather_all(fwd, rc, axis):
    count = lax.axis_size(axis)
    place = lax.axis_index(axis)
    rows = fwd.shape[0]
    held = jnp.concatenate([fwd, rc], axis=0)
    bit = 0
    while 2**bit < count:
        mask = 2**bit
        other = lax.ppermute(held, axis, [(src, src ^ mask) for src in range(count)])
        upper = (place // mask) % 2 == 1
        low_first = jnp.concatenate([held, other], axis=1)
        high_first = jnp.concatenate([other, held], axis=1)
        held = jnp.concatenate(
            [
                jnp.where(upper, high_first[:rows], low_first[:rows]),
                jnp.where(upper, low_first[rows:], high_first[rows:]),
            ],
            axis=0,
        )
        bit += 1
    return held


def heads_lookup(rows, bases):
    picked = jnp.zeros(bases.shape[:-1] + (rows.shape[1], bases.shape[-1]), jnp.float32)
    for base in range(BASES):
        picked = picked + jnp.where(
            (bases == base)[..., None, :], rows[base][:, None], 0.0
        )
    return picked


def onehot(ids, size):
    return (ids[..., None] == jnp.arange(size, dtype=ids.dtype)).astype(jnp.bfloat16)


def split_bf16(values):
    high = values.astype(jnp.bfloat16)
    return high, (values - high.astype(jnp.float32)).astype(jnp.bfloat16)


def block_cumsum(values, tri):
    return jnp.einsum("...s,st->...t", values, tri, precision=HIGH)


def local(
    tokens,
    emb_half,
    norm_gain,
    w_xbc,
    w_z,
    w_dt,
    conv_w,
    conv_bias,
    dt_bias,
    a_log,
    d_skip,
    inner_gain,
    w_out,
    final_gain,
    w_head_half,
    teacher_top,
    teacher_vals,
):
    windows, count = tokens.shape
    nseq = lax.axis_size("seq")
    place = lax.axis_index("seq")
    total = count * nseq
    nblk = total // BLK
    nloc = count // BLK
    streams = 2 * windows
    units = streams * nloc
    tri = (jnp.arange(BLK)[:, None] <= jnp.arange(BLK)[None, :]).astype(jnp.float32)

    emb_full = jnp.concatenate([emb_half, emb_half[::-1, ::-1]], axis=0)
    act_tab, z_rows, dt_rows = gram_tables(emb_full, norm_gain, w_xbc, w_z, w_dt, conv_w, conv_bias)
    x_tab = act_tab[:, :INNER].astype(jnp.bfloat16)
    b_tab = act_tab[:, INNER : INNER + NS]
    bc_tab = act_tab[:, INNER:]
    x_heads = x_tab.reshape(GRAMS, HEADS, HD).transpose(1, 0, 2)
    neg_rate = -jnp.exp(a_log)[:, None]

    rc_tok = (BASES - 1) - tokens[:, ::-1]
    local_tok = jnp.concatenate([tokens, rc_tok], axis=0)
    pos0 = jnp.concatenate(
        [jnp.full((windows, 1), place * count), jnp.full((windows, 1), (nseq - 1 - place) * count)]
    ).astype(jnp.int32)

    seq_tok = gather_all(tokens, rc_tok, "seq")
    ext_all = jnp.concatenate([jnp.zeros((streams, KW - 1), seq_tok.dtype), seq_tok], axis=1)
    gram = gram_ids(ext_all, jnp.broadcast_to(jnp.arange(total, dtype=jnp.int32), (streams, total)))
    local_gram = jnp.concatenate(
        [
            lax.dynamic_slice_in_dim(gram[:windows], place * count, count, axis=1),
            lax.dynamic_slice_in_dim(gram[windows:], (nseq - 1 - place) * count, count, axis=1),
        ],
        axis=0,
    )

    oh_loc = onehot(local_gram, GRAMS)
    x_loc = jnp.einsum("rtg,gc->rtc", oh_loc, x_tab, preferred_element_type=jnp.float32).astype(
        jnp.bfloat16
    )
    bc_loc = jnp.einsum("rtg,gc->rtc", oh_loc, bc_tab, precision=HIGH)
    oh_tok = onehot(local_tok, BASES)
    z_loc = jnp.einsum("rtk,kc->rtc", oh_tok, z_rows, preferred_element_type=jnp.float32)
    dt_loc = jax.nn.softplus(heads_lookup(dt_rows, local_tok) + dt_bias[:, None])
    ld_loc = neg_rate * dt_loc

    def per_unit(values, axis):
        shape = values.shape
        split = shape[:axis] + (nloc, BLK) + shape[axis + 1 :]
        moved = jnp.moveaxis(values.reshape(split), axis, 1)
        return moved.reshape((units,) + moved.shape[2:])

    x_u = per_unit(x_loc, 1).reshape(units, BLK, HEADS, HD)
    b_u = per_unit(bc_loc[..., :NS], 1)
    c_u = per_unit(bc_loc[..., NS:], 1)
    dt_u = per_unit(dt_loc, 2)
    cum_u = block_cumsum(per_unit(ld_loc, 2), tri)

    scores = jnp.einsum("utn,usn->uts", c_u, b_u, precision=HIGH)
    seg_diff = cum_u[:, :, :, None] - cum_u[:, :, None, :]
    lower = tri.T > 0
    decays = jnp.where(lower, jnp.exp(jnp.where(lower, seg_diff, 0.0)), 0.0)
    weights = (scores[:, None] * decays * dt_u[:, :, None, :]).astype(jnp.bfloat16)
    y_intra = jnp.einsum("uhts,ushp->uthp", weights, x_u, preferred_element_type=jnp.float32)

    dt_all = jax.nn.softplus(heads_lookup(dt_rows, seq_tok) + dt_bias[:, None])
    ld_all = neg_rate * dt_all
    cum = block_cumsum(ld_all.reshape(streams, HEADS, nblk, BLK), tri)
    blk_total = cum[..., -1]
    within = jnp.exp(blk_total[..., None] - cum) * dt_all.reshape(streams, HEADS, nblk, BLK)

    first_blk = (
        jnp.repeat(pos0[:, 0] // BLK, nloc) + jnp.tile(jnp.arange(nloc, dtype=jnp.int32), streams)
    )
    blk_idx = jnp.arange(nblk)
    total_u = jnp.repeat(blk_total, nloc, axis=0)
    between = (blk_idx[:, None] < blk_idx[None, :])[None] & (
        blk_idx[None, None, :] < first_blk[:, None, None]
    )
    span = jnp.sum(jnp.where(between[:, None], total_u[:, :, None, :], 0.0), axis=3)
    across = jnp.where(blk_idx[None, None, :] < first_blk[:, None, None], jnp.exp(span), 0.0)
    weight = jnp.repeat(within, nloc, axis=0) * across[..., None]
    w_hi, w_lo = split_bf16(weight)
    oh_all = jnp.repeat(onehot(gram, GRAMS), nloc, axis=0).reshape(units, nblk, BLK, GRAMS)
    per_gram = jnp.einsum(
        "uhbs,ubsg->uhg",
        jnp.concatenate([w_hi, w_lo], axis=1),
        oh_all,
        preferred_element_type=jnp.float32,
    )
    per_gram = per_gram[:, :HEADS] + per_gram[:, HEADS:]
    b_hi, b_lo = split_bf16(per_gram[..., None] * b_tab[None, None])
    start_state = jnp.einsum(
        "hgp,uhgn->uhpn", x_heads, b_hi, preferred_element_type=jnp.float32
    ) + jnp.einsum("hgp,uhgn->uhpn", x_heads, b_lo, preferred_element_type=jnp.float32)

    y_inter = (
        jnp.einsum("utn,uhpn->uthp", c_u, start_state, precision=HIGH)
        * jnp.exp(cum_u).transpose(0, 2, 1)[..., None]
    )
    y_u = y_intra + y_inter + d_skip[:, None] * x_u.astype(jnp.float32)
    z_u = per_unit(z_loc, 1).reshape(units, BLK, HEADS, HD)
    gated_y = y_u * jax.nn.silu(z_u)
    normed = rms_gain(gated_y, inner_gain.reshape(HEADS, HD)).astype(jnp.bfloat16)
    normed = jnp.moveaxis(normed.reshape(streams, nloc, BLK, INNER), 1, 1).reshape(
        streams, count, INNER
    )
    outputs = jnp.einsum("gre,ed->grd", normed, w_out, preferred_element_type=jnp.float32).astype(
        jnp.bfloat16
    )

    embedded = jnp.einsum(
        "grk,kd->grd", oh_tok[:windows], emb_full, preferred_element_type=jnp.float32
    ).astype(jnp.bfloat16)
    returned = outputs[windows:, ::-1, ::-1]
    hidden_out = (
        embedded.astype(jnp.float32)
        + outputs[:windows].astype(jnp.float32)
        + returned.astype(jnp.float32)
    ).astype(jnp.bfloat16)
    final_normed = rms_gain(hidden_out.astype(jnp.float32), final_gain).astype(jnp.bfloat16)
    head_full = jnp.concatenate([w_head_half, w_head_half[::-1, ::-1]], axis=1)
    logits = jnp.einsum("grd,db->grb", final_normed, head_full, preferred_element_type=jnp.float32)
    log_q = logits - jnp.log(jnp.sum(jnp.exp(logits), axis=-1, keepdims=True))
    top_value = jnp.max(teacher_vals, axis=1, keepdims=True)
    shifted = teacher_vals - top_value
    log_p = shifted - jnp.log(jnp.sum(jnp.exp(shifted), axis=1, keepdims=True))
    matches = teacher_top[..., None] == jnp.arange(4, dtype=jnp.int32)
    picked = jnp.sum(jnp.where(matches, log_q[:, None, :, :], 0.0), axis=-1)
    divergence = jnp.sum(jnp.exp(log_p) * (log_p - picked), axis=1)
    return (hidden_out, divergence)


def solution(mesh):
    placed = (
        P("grp", "seq"),
        P(),
        P(),
        P(),
        P(),
        P(),
        P(),
        P(),
        P(),
        P(),
        P(),
        P(),
        P(),
        P(),
        P(),
        P("grp", None, "seq"),
        P("grp", None, "seq"),
    )
    return jax.shard_map(
        local,
        mesh=mesh,
        in_specs=placed,
        out_specs=(P("grp", "seq", None), P("grp", "seq")),
        check_vma=False,
    )
```

```python
import jax
import jax.numpy as jnp
import numpy as np
from jax import lax
from jax.sharding import PartitionSpec as P

INNER = 1024
HD = 64
NS = 64
KW = 4
BLK = 128
HEADS = 16
CONVW = 1152
BASES = 4
GRAMS = 344


EPS = 1e-05
HIGH = lax.Precision.HIGHEST


def rms_gain(values, gain_row):
    return values * lax.rsqrt(jnp.mean(values * values, axis=-1, keepdims=True) + EPS) * gain_row


def to_blocks(values, block_width):
    streams, count = (values.shape[0], values.shape[1])
    return jnp.moveaxis(
        values.reshape((streams, count // block_width, block_width) + values.shape[2:]), 1, 0
    )


def ssd_block(carry_state, block_in):
    x_blk, b_blk, c_blk, decay_blk, dt_blk = block_in
    cumulated = jnp.cumsum(decay_blk, axis=2)
    block_len = decay_blk.shape[2]
    scores = jnp.einsum("gtn,gsn->gts", c_blk, b_blk, precision=HIGH)
    seg_diff = cumulated[:, :, :, None] - cumulated[:, :, None, :]
    lower_mask = jnp.arange(block_len)[:, None] >= jnp.arange(block_len)[None, :]
    decays = jnp.where(lower_mask, jnp.exp(jnp.where(lower_mask, seg_diff, 0.0)), 0.0)
    weights = (scores[:, None] * decays * dt_blk[:, :, None, :]).astype(jnp.bfloat16)
    y_intra = jnp.einsum("ghts,gshp->gthp", weights, x_blk, preferred_element_type=jnp.float32)
    y_inter = (
        jnp.einsum("gtn,ghpn->gthp", c_blk, carry_state, precision=HIGH)
        * jnp.swapaxes(jnp.exp(cumulated), 1, 2)[..., None]
    )
    last_cum = cumulated[:, :, -1:]
    scaled = jnp.exp(last_cum - cumulated) * dt_blk
    x_weighted = x_blk.astype(jnp.float32) * jnp.swapaxes(scaled, 1, 2)[..., None]
    new_state = jnp.exp(last_cum)[..., None] * carry_state + jnp.einsum(
        "gshp,gsn->ghpn", x_weighted, b_blk, precision=HIGH
    )
    return (new_state, y_intra + y_inter)


def gram_layout():
    rows = []
    for real in range(1, KW + 1):
        for code in range(BASES**real):
            taps = [None] * (KW - real) + [
                (code // BASES ** (real - 1 - k)) % BASES for k in range(real)
            ]
            rows.append(taps)
    picks = np.zeros((GRAMS, KW * BASES), np.float32)
    for row, taps in enumerate(rows):
        for offset, base in enumerate(taps):
            if base is not None:
                picks[row, offset * BASES + base] = 1.0
    return picks


def gram_tables(emb_full, norm_gain, w_xbc, w_z, w_dt, conv_w, conv_bias):
    row_norm = rms_gain(emb_full.astype(jnp.float32), norm_gain).astype(jnp.bfloat16)
    xbc_rows = jnp.dot(row_norm, w_xbc, preferred_element_type=jnp.float32).astype(jnp.bfloat16)
    z_rows = jnp.dot(row_norm, w_z, preferred_element_type=jnp.float32).astype(jnp.bfloat16)
    dt_rows = jnp.dot(row_norm, w_dt, preferred_element_type=jnp.float32)
    taps = (conv_w[:, None, :] * xbc_rows.astype(jnp.float32)[None]).reshape(KW * BASES, CONVW)
    conv_sum = conv_bias + jnp.dot(jnp.asarray(gram_layout()), taps, precision=HIGH)
    return jax.nn.silu(conv_sum), z_rows, dt_rows


def gram_ids(ext, where_in):
    count = where_in.shape[1]
    code = jnp.zeros_like(where_in)
    ids = jnp.zeros_like(where_in)
    offset_of = 0
    for real in range(1, KW + 1):
        code = code + ext[:, KW - real : KW - real + count] * BASES ** (real - 1)
        chosen = (where_in >= real - 1) if real == KW else (where_in == real - 1)
        ids = jnp.where(chosen, offset_of + code, ids)
        offset_of += BASES**real
    return ids


def gather_all(fwd, rc, axis):
    count = lax.axis_size(axis)
    place = lax.axis_index(axis)
    rows = fwd.shape[0]
    held = jnp.concatenate([fwd, rc], axis=0)
    bit = 0
    while 2**bit < count:
        mask = 2**bit
        other = lax.ppermute(held, axis, [(src, src ^ mask) for src in range(count)])
        upper = (place // mask) % 2 == 1
        low_first = jnp.concatenate([held, other], axis=1)
        high_first = jnp.concatenate([other, held], axis=1)
        held = jnp.concatenate(
            [
                jnp.where(upper, high_first[:rows], low_first[:rows]),
                jnp.where(upper, low_first[rows:], high_first[rows:]),
            ],
            axis=0,
        )
        bit += 1
    return held


def heads_lookup(rows, bases):
    picked = jnp.zeros(bases.shape[:-1] + (rows.shape[1], bases.shape[-1]), jnp.float32)
    for base in range(BASES):
        picked = picked + jnp.where(
            (bases == base)[..., None, :], rows[base][:, None], 0.0
        )
    return picked


def onehot(ids, size):
    return (ids[..., None] == jnp.arange(size, dtype=ids.dtype)).astype(jnp.bfloat16)


def exchange(size):
    rows = lax.broadcasted_iota(jnp.int32, (size, size), 0)
    cols = lax.broadcasted_iota(jnp.int32, (size, size), 1)
    return (rows + cols == size - 1).astype(jnp.bfloat16)


def split_bf16(values):
    high = values.astype(jnp.bfloat16)
    return high, (values - high.astype(jnp.float32)).astype(jnp.bfloat16)


def block_cumsum(values, tri):
    return jnp.einsum("...s,st->...t", values, tri, precision=HIGH)


def local(
    tokens,
    emb_half,
    norm_gain,
    w_xbc,
    w_z,
    w_dt,
    conv_w,
    conv_bias,
    dt_bias,
    a_log,
    d_skip,
    inner_gain,
    w_out,
    final_gain,
    w_head_half,
    teacher_top,
    teacher_vals,
):
    windows, count = tokens.shape
    nseq = lax.axis_size("seq")
    place = lax.axis_index("seq")
    total = count * nseq
    nblk = total // BLK
    nloc = count // BLK
    streams = 2 * windows
    units = streams * nloc
    tri = (jnp.arange(BLK)[:, None] <= jnp.arange(BLK)[None, :]).astype(jnp.float32)

    flip_d = exchange(emb_half.shape[1])
    emb_flip = jnp.dot(emb_half, flip_d, preferred_element_type=jnp.float32).astype(jnp.bfloat16)
    emb_full = jnp.concatenate([emb_half, emb_flip[1:2], emb_flip[0:1]], axis=0)
    act_tab, z_rows, dt_rows = gram_tables(emb_full, norm_gain, w_xbc, w_z, w_dt, conv_w, conv_bias)
    x_tab = act_tab[:, :INNER].astype(jnp.bfloat16)
    b_tab = act_tab[:, INNER : INNER + NS]
    bc_tab = act_tab[:, INNER:]
    x_heads = x_tab.reshape(GRAMS, HEADS, HD).transpose(1, 0, 2)
    neg_rate = -jnp.exp(a_log)[:, None]

    flip_t = exchange(count)
    rc_tok = (BASES - 1) - jnp.dot(
        tokens.astype(jnp.bfloat16), flip_t, preferred_element_type=jnp.float32
    ).astype(jnp.int32)
    local_tok = jnp.concatenate([tokens, rc_tok], axis=0)
    pos0 = jnp.concatenate(
        [jnp.full((windows, 1), place * count), jnp.full((windows, 1), (nseq - 1 - place) * count)]
    ).astype(jnp.int32)

    seq_tok = gather_all(tokens, rc_tok, "seq")
    ext_all = jnp.concatenate([jnp.zeros((streams, KW - 1), seq_tok.dtype), seq_tok], axis=1)
    gram = gram_ids(ext_all, jnp.broadcast_to(jnp.arange(total, dtype=jnp.int32), (streams, total)))
    local_gram = jnp.concatenate(
        [
            lax.dynamic_slice_in_dim(gram[:windows], place * count, count, axis=1),
            lax.dynamic_slice_in_dim(gram[windows:], (nseq - 1 - place) * count, count, axis=1),
        ],
        axis=0,
    )

    oh_loc = onehot(local_gram, GRAMS)
    x_loc = jnp.einsum("rtg,gc->rtc", oh_loc, x_tab, preferred_element_type=jnp.float32).astype(
        jnp.bfloat16
    )
    bc_loc = jnp.einsum("rtg,gc->rtc", oh_loc, bc_tab, precision=HIGH)
    oh_tok = onehot(local_tok, BASES)
    gate_rows = jax.nn.silu(z_rows.astype(jnp.float32))
    gate_loc = jnp.zeros((streams, count, INNER), jnp.float32)
    for base in range(BASES):
        gate_loc = gate_loc + jnp.where((local_tok == base)[..., None], gate_rows[base], 0.0)
    dt_loc = jax.nn.softplus(heads_lookup(dt_rows, local_tok) + dt_bias[:, None])
    ld_loc = neg_rate * dt_loc

    def per_unit(values, axis):
        shape = values.shape
        split = shape[:axis] + (nloc, BLK) + shape[axis + 1 :]
        moved = jnp.moveaxis(values.reshape(split), axis, 1)
        return moved.reshape((units,) + moved.shape[2:])

    x_u = per_unit(x_loc, 1).reshape(units, BLK, HEADS, HD)
    b_u = per_unit(bc_loc[..., :NS], 1)
    c_u = per_unit(bc_loc[..., NS:], 1)
    dt_u = per_unit(dt_loc, 2)
    cum_u = block_cumsum(per_unit(ld_loc, 2), tri)

    scores = jnp.einsum("utn,usn->uts", c_u, b_u, precision=lax.Precision.HIGH)
    seg_diff = cum_u[:, :, :, None] - cum_u[:, :, None, :]
    lower = tri.T > 0
    decays = jnp.where(lower, jnp.exp(jnp.where(lower, seg_diff, 0.0)), 0.0)
    weights = (scores[:, None] * decays * dt_u[:, :, None, :]).astype(jnp.bfloat16)
    y_intra = jnp.einsum("uhts,ushp->uthp", weights, x_u, preferred_element_type=jnp.float32)

    dt_all = jax.nn.softplus(heads_lookup(dt_rows, seq_tok) + dt_bias[:, None])
    ld_all = neg_rate * dt_all
    cum = block_cumsum(ld_all.reshape(streams, HEADS, nblk, BLK), tri)
    blk_total = cum[..., -1]
    within = jnp.exp(blk_total[..., None] - cum) * dt_all.reshape(streams, HEADS, nblk, BLK)

    first_blk = (
        jnp.repeat(pos0[:, 0] // BLK, nloc) + jnp.tile(jnp.arange(nloc, dtype=jnp.int32), streams)
    )
    blk_idx = jnp.arange(nblk)
    total_u = jnp.repeat(blk_total, nloc, axis=0)
    between = (blk_idx[:, None] < blk_idx[None, :])[None] & (
        blk_idx[None, None, :] < first_blk[:, None, None]
    )
    span = jnp.sum(jnp.where(between[:, None], total_u[:, :, None, :], 0.0), axis=3)
    across = jnp.where(blk_idx[None, None, :] < first_blk[:, None, None], jnp.exp(span), 0.0)
    weight = jnp.repeat(within, nloc, axis=0) * across[..., None]
    w_hi, w_lo = split_bf16(weight)
    oh_all = jnp.repeat(onehot(gram, GRAMS), nloc, axis=0).reshape(units, nblk, BLK, GRAMS)
    per_gram = jnp.einsum(
        "uhbs,ubsg->uhg",
        jnp.concatenate([w_hi, w_lo], axis=1),
        oh_all,
        preferred_element_type=jnp.float32,
    )
    per_gram = per_gram[:, :HEADS] + per_gram[:, HEADS:]
    b_hi, b_lo = split_bf16(per_gram[..., None] * b_tab[None, None])
    both = jnp.einsum(
        "hgp,uhgn->uhpn",
        x_heads,
        jnp.concatenate([b_hi, b_lo], axis=-1),
        preferred_element_type=jnp.float32,
    )
    start_state = both[..., :NS] + both[..., NS:]

    y_inter = (
        jnp.einsum("utn,uhpn->uthp", c_u, start_state, precision=lax.Precision.HIGH)
        * jnp.exp(cum_u).transpose(0, 2, 1)[..., None]
    )
    y_u = y_intra + y_inter + d_skip[:, None] * x_u.astype(jnp.float32)
    gated_y = y_u * per_unit(gate_loc, 1).reshape(units, BLK, HEADS, HD)
    normed = rms_gain(gated_y, inner_gain.reshape(HEADS, HD)).astype(jnp.bfloat16)
    normed = jnp.moveaxis(normed.reshape(streams, nloc, BLK, INNER), 1, 1).reshape(
        streams, count, INNER
    )
    outputs = jnp.einsum("gre,ed->grd", normed, w_out, preferred_element_type=jnp.float32).astype(
        jnp.bfloat16
    )

    embedded = jnp.einsum(
        "grk,kd->grd", oh_tok[:windows], emb_full, preferred_element_type=jnp.float32
    ).astype(jnp.bfloat16)
    returned = outputs[windows:, ::-1, ::-1]
    hidden_out = (
        embedded.astype(jnp.float32)
        + outputs[:windows].astype(jnp.float32)
        + returned.astype(jnp.float32)
    ).astype(jnp.bfloat16)
    final_normed = rms_gain(hidden_out.astype(jnp.float32), final_gain).astype(jnp.bfloat16)
    head_flip = jnp.dot(flip_d, w_head_half, preferred_element_type=jnp.float32).astype(
        jnp.bfloat16
    )
    head_full = jnp.concatenate([w_head_half, head_flip[:, 1:2], head_flip[:, 0:1]], axis=1)
    logits = jnp.einsum("grd,db->grb", final_normed, head_full, preferred_element_type=jnp.float32)
    log_q = logits - jnp.log(jnp.sum(jnp.exp(logits), axis=-1, keepdims=True))
    top_value = jnp.max(teacher_vals, axis=1, keepdims=True)
    shifted = teacher_vals - top_value
    log_p = shifted - jnp.log(jnp.sum(jnp.exp(shifted), axis=1, keepdims=True))
    matches = teacher_top[..., None] == jnp.arange(4, dtype=jnp.int32)
    picked = jnp.sum(jnp.where(matches, log_q[:, None, :, :], 0.0), axis=-1)
    divergence = jnp.sum(jnp.exp(log_p) * (log_p - picked), axis=1)
    return (hidden_out, divergence)


def solution(mesh):
    placed = (
        P("grp", "seq"),
        P(),
        P(),
        P(),
        P(),
        P(),
        P(),
        P(),
        P(),
        P(),
        P(),
        P(),
        P(),
        P(),
        P(),
        P("grp", None, "seq"),
        P("grp", None, "seq"),
    )
    return jax.shard_map(
        local,
        mesh=mesh,
        in_specs=placed,
        out_specs=(P("grp", "seq", None), P("grp", "seq")),
        check_vma=False,
    )
```

```python
import jax
import jax.numpy as jnp
import numpy as np
from jax import lax
from jax.sharding import PartitionSpec as P

INNER = 1024
HD = 64
NS = 64
KW = 4
BLK = 128
HEADS = 16
CONVW = 1152
BASES = 4
GRAMS = 344


EPS = 1e-05
HIGH = lax.Precision.HIGHEST


def rms_gain(values, gain_row):
    return values * lax.rsqrt(jnp.mean(values * values, axis=-1, keepdims=True) + EPS) * gain_row


def to_blocks(values, block_width):
    streams, count = (values.shape[0], values.shape[1])
    return jnp.moveaxis(
        values.reshape((streams, count // block_width, block_width) + values.shape[2:]), 1, 0
    )


def ssd_block(carry_state, block_in):
    x_blk, b_blk, c_blk, decay_blk, dt_blk = block_in
    cumulated = jnp.cumsum(decay_blk, axis=2)
    block_len = decay_blk.shape[2]
    scores = jnp.einsum("gtn,gsn->gts", c_blk, b_blk, precision=HIGH)
    seg_diff = cumulated[:, :, :, None] - cumulated[:, :, None, :]
    lower_mask = jnp.arange(block_len)[:, None] >= jnp.arange(block_len)[None, :]
    decays = jnp.where(lower_mask, jnp.exp(jnp.where(lower_mask, seg_diff, 0.0)), 0.0)
    weights = (scores[:, None] * decays * dt_blk[:, :, None, :]).astype(jnp.bfloat16)
    y_intra = jnp.einsum("ghts,gshp->gthp", weights, x_blk, preferred_element_type=jnp.float32)
    y_inter = (
        jnp.einsum("gtn,ghpn->gthp", c_blk, carry_state, precision=HIGH)
        * jnp.swapaxes(jnp.exp(cumulated), 1, 2)[..., None]
    )
    last_cum = cumulated[:, :, -1:]
    scaled = jnp.exp(last_cum - cumulated) * dt_blk
    x_weighted = x_blk.astype(jnp.float32) * jnp.swapaxes(scaled, 1, 2)[..., None]
    new_state = jnp.exp(last_cum)[..., None] * carry_state + jnp.einsum(
        "gshp,gsn->ghpn", x_weighted, b_blk, precision=HIGH
    )
    return (new_state, y_intra + y_inter)


def gram_layout():
    rows = []
    for real in range(1, KW + 1):
        for code in range(BASES**real):
            taps = [None] * (KW - real) + [
                (code // BASES ** (real - 1 - k)) % BASES for k in range(real)
            ]
            rows.append(taps)
    picks = np.zeros((GRAMS, KW * BASES), np.float32)
    for row, taps in enumerate(rows):
        for offset, base in enumerate(taps):
            if base is not None:
                picks[row, offset * BASES + base] = 1.0
    return picks


def gram_tables(emb_full, norm_gain, w_xbc, w_z, w_dt, conv_w, conv_bias):
    row_norm = rms_gain(emb_full.astype(jnp.float32), norm_gain).astype(jnp.bfloat16)
    xbc_rows = jnp.dot(row_norm, w_xbc, preferred_element_type=jnp.float32).astype(jnp.bfloat16)
    z_rows = jnp.dot(row_norm, w_z, preferred_element_type=jnp.float32).astype(jnp.bfloat16)
    dt_rows = jnp.dot(row_norm, w_dt, preferred_element_type=jnp.float32)
    taps = (conv_w[:, None, :] * xbc_rows.astype(jnp.float32)[None]).reshape(KW * BASES, CONVW)
    conv_sum = conv_bias + jnp.dot(jnp.asarray(gram_layout()), taps, precision=HIGH)
    return jax.nn.silu(conv_sum), z_rows, dt_rows


def gram_ids(ext, where_in):
    count = where_in.shape[1]
    code = jnp.zeros_like(where_in)
    ids = jnp.zeros_like(where_in)
    offset_of = 0
    for real in range(1, KW + 1):
        code = code + ext[:, KW - real : KW - real + count] * BASES ** (real - 1)
        chosen = (where_in >= real - 1) if real == KW else (where_in == real - 1)
        ids = jnp.where(chosen, offset_of + code, ids)
        offset_of += BASES**real
    return ids


def gather_all(fwd, rc, axis):
    count = lax.axis_size(axis)
    place = lax.axis_index(axis)
    rows = fwd.shape[0]
    held = jnp.concatenate([fwd, rc], axis=0)
    bit = 0
    while 2**bit < count:
        mask = 2**bit
        other = lax.ppermute(held, axis, [(src, src ^ mask) for src in range(count)])
        upper = (place // mask) % 2 == 1
        low_first = jnp.concatenate([held, other], axis=1)
        high_first = jnp.concatenate([other, held], axis=1)
        held = jnp.concatenate(
            [
                jnp.where(upper, high_first[:rows], low_first[:rows]),
                jnp.where(upper, low_first[rows:], high_first[rows:]),
            ],
            axis=0,
        )
        bit += 1
    return held


def heads_lookup(rows, bases):
    picked = jnp.zeros(bases.shape[:-1] + (rows.shape[1], bases.shape[-1]), jnp.float32)
    for base in range(BASES):
        picked = picked + jnp.where(
            (bases == base)[..., None, :], rows[base][:, None], 0.0
        )
    return picked


def onehot(ids, size):
    return (ids[..., None] == jnp.arange(size, dtype=ids.dtype)).astype(jnp.bfloat16)


def exchange(size):
    rows = lax.broadcasted_iota(jnp.int32, (size, size), 0)
    cols = lax.broadcasted_iota(jnp.int32, (size, size), 1)
    return (rows + cols == size - 1).astype(jnp.bfloat16)


def split_bf16(values):
    high = values.astype(jnp.bfloat16)
    return high, (values - high.astype(jnp.float32)).astype(jnp.bfloat16)


def block_cumsum(values, tri):
    return jnp.einsum("...s,st->...t", values, tri, precision=HIGH)


def local(
    tokens,
    emb_half,
    norm_gain,
    w_xbc,
    w_z,
    w_dt,
    conv_w,
    conv_bias,
    dt_bias,
    a_log,
    d_skip,
    inner_gain,
    w_out,
    final_gain,
    w_head_half,
    teacher_top,
    teacher_vals,
):
    windows, count = tokens.shape
    nseq = lax.axis_size("seq")
    place = lax.axis_index("seq")
    total = count * nseq
    nblk = total // BLK
    nloc = count // BLK
    streams = 2 * windows
    units = streams * nloc
    tri = (jnp.arange(BLK)[:, None] <= jnp.arange(BLK)[None, :]).astype(jnp.float32)

    flip_d = exchange(emb_half.shape[1])
    emb_flip = jnp.dot(emb_half, flip_d, preferred_element_type=jnp.float32).astype(jnp.bfloat16)
    emb_full = jnp.concatenate([emb_half, emb_flip[1:2], emb_flip[0:1]], axis=0)
    act_tab, z_rows, dt_rows = gram_tables(emb_full, norm_gain, w_xbc, w_z, w_dt, conv_w, conv_bias)
    x_tab = act_tab[:, :INNER].astype(jnp.bfloat16)
    b_tab = act_tab[:, INNER : INNER + NS]
    bc_tab = act_tab[:, INNER:]
    x_heads = x_tab.reshape(GRAMS, HEADS, HD).transpose(1, 0, 2)
    neg_rate = -jnp.exp(a_log)[:, None]

    flip_t = exchange(count)
    rc_tok = (BASES - 1) - jnp.dot(
        tokens.astype(jnp.bfloat16), flip_t, preferred_element_type=jnp.float32
    ).astype(jnp.int32)
    local_tok = jnp.concatenate([tokens, rc_tok], axis=0)
    pos0 = jnp.concatenate(
        [jnp.full((windows, 1), place * count), jnp.full((windows, 1), (nseq - 1 - place) * count)]
    ).astype(jnp.int32)

    seq_tok = gather_all(tokens, rc_tok, "seq")
    ext_all = jnp.concatenate([jnp.zeros((streams, KW - 1), seq_tok.dtype), seq_tok], axis=1)
    gram = gram_ids(ext_all, jnp.broadcast_to(jnp.arange(total, dtype=jnp.int32), (streams, total)))
    local_gram = jnp.concatenate(
        [
            lax.dynamic_slice_in_dim(gram[:windows], place * count, count, axis=1),
            lax.dynamic_slice_in_dim(gram[windows:], (nseq - 1 - place) * count, count, axis=1),
        ],
        axis=0,
    )

    oh_loc = onehot(local_gram, GRAMS)
    x_loc = jnp.einsum("rtg,gc->rtc", oh_loc, x_tab, preferred_element_type=jnp.float32).astype(
        jnp.bfloat16
    )
    bc_loc = jnp.einsum("rtg,gc->rtc", oh_loc, bc_tab, precision=HIGH)
    oh_tok = onehot(local_tok, BASES)
    z_loc = jnp.einsum("rtk,kc->rtc", oh_tok, z_rows, preferred_element_type=jnp.float32)
    dt_loc = jax.nn.softplus(heads_lookup(dt_rows, local_tok) + dt_bias[:, None])
    ld_loc = neg_rate * dt_loc

    def per_unit(values, axis):
        shape = values.shape
        split = shape[:axis] + (nloc, BLK) + shape[axis + 1 :]
        moved = jnp.moveaxis(values.reshape(split), axis, 1)
        return moved.reshape((units,) + moved.shape[2:])

    x_u = per_unit(x_loc, 1).reshape(units, BLK, HEADS, HD)
    b_u = per_unit(bc_loc[..., :NS], 1)
    c_u = per_unit(bc_loc[..., NS:], 1)
    dt_u = per_unit(dt_loc, 2)
    cum_u = block_cumsum(per_unit(ld_loc, 2), tri)

    scores = jnp.einsum("utn,usn->uts", c_u, b_u, precision=lax.Precision.HIGH)
    seg_diff = cum_u[:, :, :, None] - cum_u[:, :, None, :]
    lower = tri.T > 0
    decays = jnp.where(lower, jnp.exp(jnp.where(lower, seg_diff, 0.0)), 0.0)
    weights = (scores[:, None] * decays * dt_u[:, :, None, :]).astype(jnp.bfloat16)
    y_intra = jnp.einsum("uhts,ushp->uthp", weights, x_u, preferred_element_type=jnp.float32)

    dt_all = jax.nn.softplus(heads_lookup(dt_rows, seq_tok) + dt_bias[:, None])
    ld_all = neg_rate * dt_all
    cum = block_cumsum(ld_all.reshape(streams, HEADS, nblk, BLK), tri)
    blk_total = cum[..., -1]
    within = jnp.exp(blk_total[..., None] - cum) * dt_all.reshape(streams, HEADS, nblk, BLK)

    first_blk = (
        jnp.repeat(pos0[:, 0] // BLK, nloc) + jnp.tile(jnp.arange(nloc, dtype=jnp.int32), streams)
    )
    blk_idx = jnp.arange(nblk)
    total_u = jnp.repeat(blk_total, nloc, axis=0)
    between = (blk_idx[:, None] < blk_idx[None, :])[None] & (
        blk_idx[None, None, :] < first_blk[:, None, None]
    )
    span = jnp.sum(jnp.where(between[:, None], total_u[:, :, None, :], 0.0), axis=3)
    across = jnp.where(blk_idx[None, None, :] < first_blk[:, None, None], jnp.exp(span), 0.0)
    weight = jnp.repeat(within, nloc, axis=0) * across[..., None]
    w_hi, w_lo = split_bf16(weight)
    oh_all = jnp.repeat(onehot(gram, GRAMS), nloc, axis=0).reshape(units, nblk, BLK, GRAMS)
    per_gram = jnp.einsum(
        "uhbs,ubsg->uhg",
        jnp.concatenate([w_hi, w_lo], axis=1),
        oh_all,
        preferred_element_type=jnp.float32,
    )
    per_gram = per_gram[:, :HEADS] + per_gram[:, HEADS:]
    b_hi, b_lo = split_bf16(per_gram[..., None] * b_tab[None, None])
    both = jnp.einsum(
        "hgp,uhgn->uhpn",
        x_heads,
        jnp.concatenate([b_hi, b_lo], axis=-1),
        preferred_element_type=jnp.float32,
    )
    start_state = both[..., :NS] + both[..., NS:]

    y_inter = (
        jnp.einsum("utn,uhpn->uthp", c_u, start_state, precision=lax.Precision.HIGH)
        * jnp.exp(cum_u).transpose(0, 2, 1)[..., None]
    )
    y_u = y_intra + y_inter + d_skip[:, None] * x_u.astype(jnp.float32)
    z_u = per_unit(z_loc, 1).reshape(units, BLK, HEADS, HD)
    gated_y = y_u * jax.nn.silu(z_u)
    normed = rms_gain(gated_y, inner_gain.reshape(HEADS, HD)).astype(jnp.bfloat16)
    normed = jnp.moveaxis(normed.reshape(streams, nloc, BLK, INNER), 1, 1).reshape(
        streams, count, INNER
    )
    outputs = jnp.einsum("gre,ed->grd", normed, w_out, preferred_element_type=jnp.float32).astype(
        jnp.bfloat16
    )

    embedded = jnp.einsum(
        "grk,kd->grd", oh_tok[:windows], emb_full, preferred_element_type=jnp.float32
    ).astype(jnp.bfloat16)
    returned = outputs[windows:, ::-1, ::-1]
    hidden_out = (
        embedded.astype(jnp.float32)
        + outputs[:windows].astype(jnp.float32)
        + returned.astype(jnp.float32)
    ).astype(jnp.bfloat16)
    final_normed = rms_gain(hidden_out.astype(jnp.float32), final_gain).astype(jnp.bfloat16)
    head_flip = jnp.dot(flip_d, w_head_half, preferred_element_type=jnp.float32).astype(
        jnp.bfloat16
    )
    head_full = jnp.concatenate([w_head_half, head_flip[:, 1:2], head_flip[:, 0:1]], axis=1)
    logits = jnp.einsum("grd,db->grb", final_normed, head_full, preferred_element_type=jnp.float32)
    log_q = logits - jnp.log(jnp.sum(jnp.exp(logits), axis=-1, keepdims=True))
    top_value = jnp.max(teacher_vals, axis=1, keepdims=True)
    shifted = teacher_vals - top_value
    log_p = shifted - jnp.log(jnp.sum(jnp.exp(shifted), axis=1, keepdims=True))
    matches = teacher_top[..., None] == jnp.arange(4, dtype=jnp.int32)
    picked = jnp.sum(jnp.where(matches, log_q[:, None, :, :], 0.0), axis=-1)
    divergence = jnp.sum(jnp.exp(log_p) * (log_p - picked), axis=1)
    return (hidden_out, divergence)


def solution(mesh):
    placed = (
        P("grp", "seq"),
        P(),
        P(),
        P(),
        P(),
        P(),
        P(),
        P(),
        P(),
        P(),
        P(),
        P(),
        P(),
        P(),
        P(),
        P("grp", None, "seq"),
        P("grp", None, "seq"),
    )
    return jax.shard_map(
        local,
        mesh=mesh,
        in_specs=placed,
        out_specs=(P("grp", "seq", None), P("grp", "seq")),
        check_vma=False,
    )
```

```python
import jax
import jax.numpy as jnp
import numpy as np
from jax import lax
from jax.sharding import PartitionSpec as P

INNER = 1024
HD = 64
NS = 64
KW = 4
BLK = 128
HEADS = 16
CONVW = 1152
BASES = 4
GRAMS = 344


EPS = 1e-05
HIGH = lax.Precision.HIGHEST


def rms_gain(values, gain_row):
    return values * lax.rsqrt(jnp.mean(values * values, axis=-1, keepdims=True) + EPS) * gain_row


def to_blocks(values, block_width):
    streams, count = (values.shape[0], values.shape[1])
    return jnp.moveaxis(
        values.reshape((streams, count // block_width, block_width) + values.shape[2:]), 1, 0
    )


def ssd_block(carry_state, block_in):
    x_blk, b_blk, c_blk, decay_blk, dt_blk = block_in
    cumulated = jnp.cumsum(decay_blk, axis=2)
    block_len = decay_blk.shape[2]
    scores = jnp.einsum("gtn,gsn->gts", c_blk, b_blk, precision=HIGH)
    seg_diff = cumulated[:, :, :, None] - cumulated[:, :, None, :]
    lower_mask = jnp.arange(block_len)[:, None] >= jnp.arange(block_len)[None, :]
    decays = jnp.where(lower_mask, jnp.exp(jnp.where(lower_mask, seg_diff, 0.0)), 0.0)
    weights = (scores[:, None] * decays * dt_blk[:, :, None, :]).astype(jnp.bfloat16)
    y_intra = jnp.einsum("ghts,gshp->gthp", weights, x_blk, preferred_element_type=jnp.float32)
    y_inter = (
        jnp.einsum("gtn,ghpn->gthp", c_blk, carry_state, precision=HIGH)
        * jnp.swapaxes(jnp.exp(cumulated), 1, 2)[..., None]
    )
    last_cum = cumulated[:, :, -1:]
    scaled = jnp.exp(last_cum - cumulated) * dt_blk
    x_weighted = x_blk.astype(jnp.float32) * jnp.swapaxes(scaled, 1, 2)[..., None]
    new_state = jnp.exp(last_cum)[..., None] * carry_state + jnp.einsum(
        "gshp,gsn->ghpn", x_weighted, b_blk, precision=HIGH
    )
    return (new_state, y_intra + y_inter)


def gram_layout():
    rows = []
    for real in range(1, KW + 1):
        for code in range(BASES**real):
            taps = [None] * (KW - real) + [
                (code // BASES ** (real - 1 - k)) % BASES for k in range(real)
            ]
            rows.append(taps)
    picks = np.zeros((GRAMS, KW * BASES), np.float32)
    for row, taps in enumerate(rows):
        for offset, base in enumerate(taps):
            if base is not None:
                picks[row, offset * BASES + base] = 1.0
    return picks


def gram_tables(emb_full, norm_gain, w_xbc, w_z, w_dt, conv_w, conv_bias):
    row_norm = rms_gain(emb_full.astype(jnp.float32), norm_gain).astype(jnp.bfloat16)
    xbc_rows = jnp.dot(row_norm, w_xbc, preferred_element_type=jnp.float32).astype(jnp.bfloat16)
    z_rows = jnp.dot(row_norm, w_z, preferred_element_type=jnp.float32).astype(jnp.bfloat16)
    dt_rows = jnp.dot(row_norm, w_dt, preferred_element_type=jnp.float32)
    taps = (conv_w[:, None, :] * xbc_rows.astype(jnp.float32)[None]).reshape(KW * BASES, CONVW)
    conv_sum = conv_bias + jnp.dot(jnp.asarray(gram_layout()), taps, precision=HIGH)
    return jax.nn.silu(conv_sum), z_rows, dt_rows


def gram_ids(ext, where_in):
    count = where_in.shape[1]
    code = jnp.zeros_like(where_in)
    ids = jnp.zeros_like(where_in)
    offset_of = 0
    for real in range(1, KW + 1):
        code = code + ext[:, KW - real : KW - real + count] * BASES ** (real - 1)
        chosen = (where_in >= real - 1) if real == KW else (where_in == real - 1)
        ids = jnp.where(chosen, offset_of + code, ids)
        offset_of += BASES**real
    return ids


def gather_all(fwd, rc, axis):
    count = lax.axis_size(axis)
    place = lax.axis_index(axis)
    rows = fwd.shape[0]
    held = jnp.concatenate([fwd, rc], axis=0)
    bit = 0
    while 2**bit < count:
        mask = 2**bit
        other = lax.ppermute(held, axis, [(src, src ^ mask) for src in range(count)])
        upper = (place // mask) % 2 == 1
        low_first = jnp.concatenate([held, other], axis=1)
        high_first = jnp.concatenate([other, held], axis=1)
        held = jnp.concatenate(
            [
                jnp.where(upper, high_first[:rows], low_first[:rows]),
                jnp.where(upper, low_first[rows:], high_first[rows:]),
            ],
            axis=0,
        )
        bit += 1
    return held


def heads_lookup(rows, bases):
    picked = jnp.zeros(bases.shape[:-1] + (rows.shape[1], bases.shape[-1]), jnp.float32)
    for base in range(BASES):
        picked = picked + jnp.where(
            (bases == base)[..., None, :], rows[base][:, None], 0.0
        )
    return picked


def onehot(ids, size):
    return (ids[..., None] == jnp.arange(size, dtype=ids.dtype)).astype(jnp.bfloat16)


def exchange(size):
    rows = lax.broadcasted_iota(jnp.int32, (size, size), 0)
    cols = lax.broadcasted_iota(jnp.int32, (size, size), 1)
    return (rows + cols == size - 1).astype(jnp.bfloat16)


def split_bf16(values):
    high = values.astype(jnp.bfloat16)
    return high, (values - high.astype(jnp.float32)).astype(jnp.bfloat16)


def block_cumsum(values, tri):
    return jnp.einsum("...s,st->...t", values, tri, precision=HIGH)


def local(
    tokens,
    emb_half,
    norm_gain,
    w_xbc,
    w_z,
    w_dt,
    conv_w,
    conv_bias,
    dt_bias,
    a_log,
    d_skip,
    inner_gain,
    w_out,
    final_gain,
    w_head_half,
    teacher_top,
    teacher_vals,
):
    windows, count = tokens.shape
    nseq = lax.axis_size("seq")
    place = lax.axis_index("seq")
    total = count * nseq
    nblk = total // BLK
    nloc = count // BLK
    streams = 2 * windows
    units = streams * nloc
    tri = (jnp.arange(BLK)[:, None] <= jnp.arange(BLK)[None, :]).astype(jnp.float32)

    flip_d = exchange(emb_half.shape[1])
    emb_flip = jnp.dot(emb_half, flip_d, preferred_element_type=jnp.float32).astype(jnp.bfloat16)
    emb_full = jnp.concatenate([emb_half, emb_flip[1:2], emb_flip[0:1]], axis=0)
    act_tab, z_rows, dt_rows = gram_tables(emb_full, norm_gain, w_xbc, w_z, w_dt, conv_w, conv_bias)
    x_tab = act_tab[:, :INNER].astype(jnp.bfloat16)
    b_tab = act_tab[:, INNER : INNER + NS]
    bc_tab = act_tab[:, INNER:]
    x_heads = x_tab.reshape(GRAMS, HEADS, HD).transpose(1, 0, 2)
    neg_rate = -jnp.exp(a_log)[:, None]

    flip_t = exchange(count)
    rc_tok = (BASES - 1) - jnp.dot(
        tokens.astype(jnp.bfloat16), flip_t, preferred_element_type=jnp.float32
    ).astype(jnp.int32)
    local_tok = jnp.concatenate([tokens, rc_tok], axis=0)
    pos0 = jnp.concatenate(
        [jnp.full((windows, 1), place * count), jnp.full((windows, 1), (nseq - 1 - place) * count)]
    ).astype(jnp.int32)

    seq_tok = gather_all(tokens, rc_tok, "seq")
    ext_all = jnp.concatenate([jnp.zeros((streams, KW - 1), seq_tok.dtype), seq_tok], axis=1)
    gram = gram_ids(ext_all, jnp.broadcast_to(jnp.arange(total, dtype=jnp.int32), (streams, total)))
    local_gram = jnp.concatenate(
        [
            lax.dynamic_slice_in_dim(gram[:windows], place * count, count, axis=1),
            lax.dynamic_slice_in_dim(gram[windows:], (nseq - 1 - place) * count, count, axis=1),
        ],
        axis=0,
    )

    oh_loc = onehot(local_gram, GRAMS)
    x_loc = jnp.einsum("rtg,gc->rtc", oh_loc, x_tab, preferred_element_type=jnp.float32).astype(
        jnp.bfloat16
    )
    bc_loc = jnp.einsum("rtg,gc->rtc", oh_loc, bc_tab, precision=HIGH)
    oh_tok = onehot(local_tok, BASES)
    z_loc = jnp.einsum("rtk,kc->rtc", oh_tok, z_rows, preferred_element_type=jnp.float32).astype(
        jnp.bfloat16
    )
    dt_loc = jax.nn.softplus(heads_lookup(dt_rows, local_tok) + dt_bias[:, None])
    ld_loc = neg_rate * dt_loc

    def per_unit(values, axis):
        shape = values.shape
        split = shape[:axis] + (nloc, BLK) + shape[axis + 1 :]
        moved = jnp.moveaxis(values.reshape(split), axis, 1)
        return moved.reshape((units,) + moved.shape[2:])

    x_u = per_unit(x_loc, 1).reshape(units, BLK, HEADS, HD)
    b_u = per_unit(bc_loc[..., :NS], 1)
    c_u = per_unit(bc_loc[..., NS:], 1)
    dt_u = per_unit(dt_loc, 2)
    cum_u = block_cumsum(per_unit(ld_loc, 2), tri)

    scores = jnp.einsum("utn,usn->uts", c_u, b_u, precision=lax.Precision.HIGH)
    seg_diff = cum_u[:, :, :, None] - cum_u[:, :, None, :]
    lower = tri.T > 0
    decays = jnp.where(lower, jnp.exp(jnp.where(lower, seg_diff, 0.0)), 0.0)
    weights = (scores[:, None] * decays * dt_u[:, :, None, :]).astype(jnp.bfloat16)
    y_intra = jnp.einsum("uhts,ushp->uthp", weights, x_u, preferred_element_type=jnp.float32)

    dt_all = jax.nn.softplus(heads_lookup(dt_rows, seq_tok) + dt_bias[:, None])
    ld_all = neg_rate * dt_all
    cum = block_cumsum(ld_all.reshape(streams, HEADS, nblk, BLK), tri)
    blk_total = cum[..., -1]
    within = jnp.exp(blk_total[..., None] - cum) * dt_all.reshape(streams, HEADS, nblk, BLK)

    first_blk = (
        jnp.repeat(pos0[:, 0] // BLK, nloc) + jnp.tile(jnp.arange(nloc, dtype=jnp.int32), streams)
    )
    blk_idx = jnp.arange(nblk)
    total_u = jnp.repeat(blk_total, nloc, axis=0)
    between = (blk_idx[:, None] < blk_idx[None, :])[None] & (
        blk_idx[None, None, :] < first_blk[:, None, None]
    )
    span = jnp.sum(jnp.where(between[:, None], total_u[:, :, None, :], 0.0), axis=3)
    across = jnp.where(blk_idx[None, None, :] < first_blk[:, None, None], jnp.exp(span), 0.0)
    weight = jnp.repeat(within, nloc, axis=0) * across[..., None]
    w_hi, w_lo = split_bf16(weight)
    oh_all = jnp.repeat(onehot(gram, GRAMS), nloc, axis=0).reshape(units, nblk, BLK, GRAMS)
    per_gram = jnp.einsum(
        "uhbs,ubsg->uhg",
        jnp.concatenate([w_hi, w_lo], axis=1),
        oh_all,
        preferred_element_type=jnp.float32,
    )
    per_gram = per_gram[:, :HEADS] + per_gram[:, HEADS:]
    b_hi, b_lo = split_bf16(per_gram[..., None] * b_tab[None, None])
    start_state = jnp.einsum(
        "hgp,uhgn->uhpn", x_heads, b_hi, preferred_element_type=jnp.float32
    ) + jnp.einsum("hgp,uhgn->uhpn", x_heads, b_lo, preferred_element_type=jnp.float32)

    y_inter = (
        jnp.einsum("utn,uhpn->uthp", c_u, start_state, precision=lax.Precision.HIGH)
        * jnp.exp(cum_u).transpose(0, 2, 1)[..., None]
    )
    y_u = y_intra + y_inter + d_skip[:, None] * x_u.astype(jnp.float32)
    z_u = per_unit(z_loc, 1).reshape(units, BLK, HEADS, HD)
    gated_y = y_u * jax.nn.silu(z_u.astype(jnp.float32))
    scaled_y = gated_y * lax.rsqrt(jnp.mean(gated_y * gated_y, axis=-1, keepdims=True) + EPS)
    normed = (scaled_y.reshape(streams, count, INNER) * inner_gain).astype(jnp.bfloat16)
    outputs = jnp.einsum("gre,ed->grd", normed, w_out, preferred_element_type=jnp.float32).astype(
        jnp.bfloat16
    )

    embedded = jnp.einsum(
        "grk,kd->grd", oh_tok[:windows], emb_full, preferred_element_type=jnp.float32
    ).astype(jnp.bfloat16)
    returned = outputs[windows:, ::-1, ::-1]
    hidden_out = (
        embedded.astype(jnp.float32)
        + outputs[:windows].astype(jnp.float32)
        + returned.astype(jnp.float32)
    ).astype(jnp.bfloat16)
    final_normed = rms_gain(hidden_out.astype(jnp.float32), final_gain).astype(jnp.bfloat16)
    head_flip = jnp.dot(flip_d, w_head_half, preferred_element_type=jnp.float32).astype(
        jnp.bfloat16
    )
    head_full = jnp.concatenate([w_head_half, head_flip[:, 1:2], head_flip[:, 0:1]], axis=1)
    logits = jnp.einsum("grd,db->grb", final_normed, head_full, preferred_element_type=jnp.float32)
    log_q = logits - jnp.log(jnp.sum(jnp.exp(logits), axis=-1, keepdims=True))
    top_value = jnp.max(teacher_vals, axis=1, keepdims=True)
    shifted = teacher_vals - top_value
    log_p = shifted - jnp.log(jnp.sum(jnp.exp(shifted), axis=1, keepdims=True))
    matches = teacher_top[..., None] == jnp.arange(4, dtype=jnp.int32)
    picked = jnp.sum(jnp.where(matches, log_q[:, None, :, :], 0.0), axis=-1)
    divergence = jnp.sum(jnp.exp(log_p) * (log_p - picked), axis=1)
    return (hidden_out, divergence)


def solution(mesh):
    placed = (
        P("grp", "seq"),
        P(),
        P(),
        P(),
        P(),
        P(),
        P(),
        P(),
        P(),
        P(),
        P(),
        P(),
        P(),
        P(),
        P(),
        P("grp", None, "seq"),
        P("grp", None, "seq"),
    )
    return jax.shard_map(
        local,
        mesh=mesh,
        in_specs=placed,
        out_specs=(P("grp", "seq", None), P("grp", "seq")),
        check_vma=False,
    )
```

```python
import jax
import jax.numpy as jnp
import numpy as np
from jax import lax
from jax.sharding import PartitionSpec as P

INNER = 1024
HD = 64
NS = 64
KW = 4
BLK = 128
HEADS = 16
CONVW = 1152
BASES = 4
GRAMS = 344


EPS = 1e-05
HIGH = lax.Precision.HIGHEST


def rms_gain(values, gain_row):
    return values * lax.rsqrt(jnp.mean(values * values, axis=-1, keepdims=True) + EPS) * gain_row


def to_blocks(values, block_width):
    streams, count = (values.shape[0], values.shape[1])
    return jnp.moveaxis(
        values.reshape((streams, count // block_width, block_width) + values.shape[2:]), 1, 0
    )


def ssd_block(carry_state, block_in):
    x_blk, b_blk, c_blk, decay_blk, dt_blk = block_in
    cumulated = jnp.cumsum(decay_blk, axis=2)
    block_len = decay_blk.shape[2]
    scores = jnp.einsum("gtn,gsn->gts", c_blk, b_blk, precision=HIGH)
    seg_diff = cumulated[:, :, :, None] - cumulated[:, :, None, :]
    lower_mask = jnp.arange(block_len)[:, None] >= jnp.arange(block_len)[None, :]
    decays = jnp.where(lower_mask, jnp.exp(jnp.where(lower_mask, seg_diff, 0.0)), 0.0)
    weights = (scores[:, None] * decays * dt_blk[:, :, None, :]).astype(jnp.bfloat16)
    y_intra = jnp.einsum("ghts,gshp->gthp", weights, x_blk, preferred_element_type=jnp.float32)
    y_inter = (
        jnp.einsum("gtn,ghpn->gthp", c_blk, carry_state, precision=HIGH)
        * jnp.swapaxes(jnp.exp(cumulated), 1, 2)[..., None]
    )
    last_cum = cumulated[:, :, -1:]
    scaled = jnp.exp(last_cum - cumulated) * dt_blk
    x_weighted = x_blk.astype(jnp.float32) * jnp.swapaxes(scaled, 1, 2)[..., None]
    new_state = jnp.exp(last_cum)[..., None] * carry_state + jnp.einsum(
        "gshp,gsn->ghpn", x_weighted, b_blk, precision=HIGH
    )
    return (new_state, y_intra + y_inter)


def gram_layout():
    rows = []
    for real in range(1, KW + 1):
        for code in range(BASES**real):
            taps = [None] * (KW - real) + [
                (code // BASES ** (real - 1 - k)) % BASES for k in range(real)
            ]
            rows.append(taps)
    picks = np.zeros((GRAMS, KW * BASES), np.float32)
    for row, taps in enumerate(rows):
        for offset, base in enumerate(taps):
            if base is not None:
                picks[row, offset * BASES + base] = 1.0
    return picks


def gram_tables(emb_full, norm_gain, w_xbc, w_z, w_dt, conv_w, conv_bias):
    row_norm = rms_gain(emb_full.astype(jnp.float32), norm_gain).astype(jnp.bfloat16)
    xbc_rows = jnp.dot(row_norm, w_xbc, preferred_element_type=jnp.float32).astype(jnp.bfloat16)
    z_rows = jnp.dot(row_norm, w_z, preferred_element_type=jnp.float32).astype(jnp.bfloat16)
    dt_rows = jnp.dot(row_norm, w_dt, preferred_element_type=jnp.float32)
    taps = (conv_w[:, None, :] * xbc_rows.astype(jnp.float32)[None]).reshape(KW * BASES, CONVW)
    conv_sum = conv_bias + jnp.dot(jnp.asarray(gram_layout()), taps, precision=HIGH)
    return jax.nn.silu(conv_sum), z_rows, dt_rows


def gram_ids(ext, where_in):
    count = where_in.shape[1]
    code = jnp.zeros_like(where_in)
    ids = jnp.zeros_like(where_in)
    offset_of = 0
    for real in range(1, KW + 1):
        code = code + ext[:, KW - real : KW - real + count] * BASES ** (real - 1)
        chosen = (where_in >= real - 1) if real == KW else (where_in == real - 1)
        ids = jnp.where(chosen, offset_of + code, ids)
        offset_of += BASES**real
    return ids


def gather_all(fwd, rc, axis):
    count = lax.axis_size(axis)
    place = lax.axis_index(axis)
    rows = fwd.shape[0]
    held = jnp.concatenate([fwd, rc], axis=0)
    bit = 0
    while 2**bit < count:
        mask = 2**bit
        other = lax.ppermute(held, axis, [(src, src ^ mask) for src in range(count)])
        upper = (place // mask) % 2 == 1
        low_first = jnp.concatenate([held, other], axis=1)
        high_first = jnp.concatenate([other, held], axis=1)
        held = jnp.concatenate(
            [
                jnp.where(upper, high_first[:rows], low_first[:rows]),
                jnp.where(upper, low_first[rows:], high_first[rows:]),
            ],
            axis=0,
        )
        bit += 1
    return held


def heads_lookup(rows, bases):
    picked = jnp.zeros(bases.shape[:-1] + (rows.shape[1], bases.shape[-1]), jnp.float32)
    for base in range(BASES):
        picked = picked + jnp.where(
            (bases == base)[..., None, :], rows[base][:, None], 0.0
        )
    return picked


def onehot(ids, size):
    return (ids[..., None] == jnp.arange(size, dtype=ids.dtype)).astype(jnp.bfloat16)


def exchange(size):
    rows = lax.broadcasted_iota(jnp.int32, (size, size), 0)
    cols = lax.broadcasted_iota(jnp.int32, (size, size), 1)
    return (rows + cols == size - 1).astype(jnp.bfloat16)


def split_bf16(values):
    high = values.astype(jnp.bfloat16)
    return high, (values - high.astype(jnp.float32)).astype(jnp.bfloat16)


def block_cumsum(values, tri):
    return jnp.einsum("...s,st->...t", values, tri, precision=HIGH)


def local(
    tokens,
    emb_half,
    norm_gain,
    w_xbc,
    w_z,
    w_dt,
    conv_w,
    conv_bias,
    dt_bias,
    a_log,
    d_skip,
    inner_gain,
    w_out,
    final_gain,
    w_head_half,
    teacher_top,
    teacher_vals,
):
    windows, count = tokens.shape
    nseq = lax.axis_size("seq")
    place = lax.axis_index("seq")
    total = count * nseq
    nblk = total // BLK
    nloc = count // BLK
    streams = 2 * windows
    units = streams * nloc
    tri = (jnp.arange(BLK)[:, None] <= jnp.arange(BLK)[None, :]).astype(jnp.float32)

    flip_d = exchange(emb_half.shape[1])
    emb_flip = jnp.dot(emb_half, flip_d, preferred_element_type=jnp.float32).astype(jnp.bfloat16)
    emb_full = jnp.concatenate([emb_half, emb_flip[1:2], emb_flip[0:1]], axis=0)
    act_tab, z_rows, dt_rows = gram_tables(emb_full, norm_gain, w_xbc, w_z, w_dt, conv_w, conv_bias)
    x_tab = act_tab[:, :INNER].astype(jnp.bfloat16)
    b_tab = act_tab[:, INNER : INNER + NS]
    bc_tab = act_tab[:, INNER:]
    x_heads = x_tab.reshape(GRAMS, HEADS, HD).transpose(1, 0, 2)
    neg_rate = -jnp.exp(a_log)[:, None]

    flip_t = exchange(count)
    rc_tok = (BASES - 1) - jnp.dot(
        tokens.astype(jnp.bfloat16), flip_t, preferred_element_type=jnp.float32
    ).astype(jnp.int32)
    local_tok = jnp.concatenate([tokens, rc_tok], axis=0)
    pos0 = jnp.concatenate(
        [jnp.full((windows, 1), place * count), jnp.full((windows, 1), (nseq - 1 - place) * count)]
    ).astype(jnp.int32)

    seq_tok = gather_all(tokens, rc_tok, "seq")
    ext_all = jnp.concatenate([jnp.zeros((streams, KW - 1), seq_tok.dtype), seq_tok], axis=1)
    gram = gram_ids(ext_all, jnp.broadcast_to(jnp.arange(total, dtype=jnp.int32), (streams, total)))
    local_gram = jnp.concatenate(
        [
            lax.dynamic_slice_in_dim(gram[:windows], place * count, count, axis=1),
            lax.dynamic_slice_in_dim(gram[windows:], (nseq - 1 - place) * count, count, axis=1),
        ],
        axis=0,
    )

    oh_loc = onehot(local_gram, GRAMS)
    x_loc = jnp.einsum("rtg,gc->rtc", oh_loc, x_tab, preferred_element_type=jnp.float32).astype(
        jnp.bfloat16
    )
    bc_loc = jnp.einsum("rtg,gc->rtc", oh_loc, bc_tab, precision=HIGH)
    oh_tok = onehot(local_tok, BASES)
    z_loc = jnp.einsum("rtk,kc->rtc", oh_tok, z_rows, preferred_element_type=jnp.float32)
    dt_loc = jax.nn.softplus(heads_lookup(dt_rows, local_tok) + dt_bias[:, None])
    ld_loc = neg_rate * dt_loc

    def per_unit(values, axis):
        shape = values.shape
        split = shape[:axis] + (nloc, BLK) + shape[axis + 1 :]
        moved = jnp.moveaxis(values.reshape(split), axis, 1)
        return moved.reshape((units,) + moved.shape[2:])

    x_u = per_unit(x_loc, 1).reshape(units, BLK, HEADS, HD)
    b_u = per_unit(bc_loc[..., :NS], 1)
    c_u = per_unit(bc_loc[..., NS:], 1)
    dt_u = per_unit(dt_loc, 2)
    cum_u = block_cumsum(per_unit(ld_loc, 2), tri)

    scores = jnp.einsum("utn,usn->uts", c_u, b_u, precision=lax.Precision.HIGH)
    seg_diff = cum_u[:, :, :, None] - cum_u[:, :, None, :]
    lower = tri.T > 0
    decays = jnp.where(lower, jnp.exp(jnp.where(lower, seg_diff, 0.0)), 0.0)
    weights = (scores[:, None] * decays * dt_u[:, :, None, :]).astype(jnp.bfloat16)
    y_intra = jnp.einsum("uhts,ushp->uthp", weights, x_u, preferred_element_type=jnp.float32)

    dt_all = jax.nn.softplus(heads_lookup(dt_rows, seq_tok) + dt_bias[:, None])
    ld_all = neg_rate * dt_all
    cum = block_cumsum(ld_all.reshape(streams, HEADS, nblk, BLK), tri)
    blk_total = cum[..., -1]
    within = jnp.exp(blk_total[..., None] - cum) * dt_all.reshape(streams, HEADS, nblk, BLK)

    first_blk = (
        jnp.repeat(pos0[:, 0] // BLK, nloc) + jnp.tile(jnp.arange(nloc, dtype=jnp.int32), streams)
    )
    blk_idx = jnp.arange(nblk)
    total_u = jnp.repeat(blk_total, nloc, axis=0)
    between = (blk_idx[:, None] < blk_idx[None, :])[None] & (
        blk_idx[None, None, :] < first_blk[:, None, None]
    )
    span = jnp.sum(jnp.where(between[:, None], total_u[:, :, None, :], 0.0), axis=3)
    across = jnp.where(blk_idx[None, None, :] < first_blk[:, None, None], jnp.exp(span), 0.0)
    weight = jnp.repeat(within, nloc, axis=0) * across[..., None]
    w_hi, w_lo = split_bf16(weight)
    oh_all = jnp.repeat(onehot(gram, GRAMS), nloc, axis=0).reshape(units, nblk, BLK, GRAMS)
    per_gram = jnp.einsum(
        "uhbs,ubsg->uhg",
        jnp.concatenate([w_hi, w_lo], axis=1),
        oh_all,
        preferred_element_type=jnp.float32,
    )
    per_gram = per_gram[:, :HEADS] + per_gram[:, HEADS:]
    b_hi, b_lo = split_bf16(per_gram[..., None] * b_tab[None, None])
    start_state = jnp.einsum(
        "hgp,uhgn->uhpn", x_heads, b_hi, preferred_element_type=jnp.float32
    ) + jnp.einsum("hgp,uhgn->uhpn", x_heads, b_lo, preferred_element_type=jnp.float32)

    y_inter = (
        jnp.einsum("utn,uhpn->uthp", c_u, start_state, precision=lax.Precision.HIGH)
        * jnp.exp(cum_u).transpose(0, 2, 1)[..., None]
    )
    y_u = y_intra + y_inter + d_skip[:, None] * x_u.astype(jnp.float32)
    z_u = per_unit(z_loc, 1).reshape(units, BLK, HEADS, HD)
    gated_y = y_u * jax.nn.silu(z_u)
    normed = rms_gain(gated_y, inner_gain.reshape(HEADS, HD)).astype(jnp.bfloat16)
    normed = jnp.moveaxis(normed.reshape(streams, nloc, BLK, INNER), 1, 1).reshape(
        streams, count, INNER
    )
    outputs = jnp.einsum("gre,ed->grd", normed, w_out, preferred_element_type=jnp.float32).astype(
        jnp.bfloat16
    )

    embedded = jnp.einsum(
        "grk,kd->grd", oh_tok[:windows], emb_full, preferred_element_type=jnp.float32
    ).astype(jnp.bfloat16)
    returned = outputs[windows:, ::-1, ::-1]
    hidden_out = (
        embedded.astype(jnp.float32)
        + outputs[:windows].astype(jnp.float32)
        + returned.astype(jnp.float32)
    ).astype(jnp.bfloat16)
    final_normed = rms_gain(hidden_out.astype(jnp.float32), final_gain).astype(jnp.bfloat16)
    head_flip = jnp.dot(flip_d, w_head_half, preferred_element_type=jnp.float32).astype(
        jnp.bfloat16
    )
    head_full = jnp.concatenate([w_head_half, head_flip[:, 1:2], head_flip[:, 0:1]], axis=1)
    logits = jnp.einsum("grd,db->grb", final_normed, head_full, preferred_element_type=jnp.float32)
    log_q = logits - jnp.log(jnp.sum(jnp.exp(logits), axis=-1, keepdims=True))
    top_value = jnp.max(teacher_vals, axis=1, keepdims=True)
    shifted = teacher_vals - top_value
    log_p = shifted - jnp.log(jnp.sum(jnp.exp(shifted), axis=1, keepdims=True))
    matches = teacher_top[..., None] == jnp.arange(4, dtype=jnp.int32)
    picked = jnp.sum(jnp.where(matches, log_q[:, None, :, :], 0.0), axis=-1)
    divergence = jnp.sum(jnp.exp(log_p) * (log_p - picked), axis=1)
    return (hidden_out, divergence)


def solution(mesh):
    placed = (
        P("grp", "seq"),
        P(),
        P(),
        P(),
        P(),
        P(),
        P(),
        P(),
        P(),
        P(),
        P(),
        P(),
        P(),
        P(),
        P(),
        P("grp", None, "seq"),
        P("grp", None, "seq"),
    )
    return jax.shard_map(
        local,
        mesh=mesh,
        in_specs=placed,
        out_specs=(P("grp", "seq", None), P("grp", "seq")),
        check_vma=False,
    )
```

```python
import jax
import jax.numpy as jnp
import numpy as np
from jax import lax
from jax.sharding import PartitionSpec as P

INNER = 1024
HD = 64
NS = 64
KW = 4
BLK = 128
HEADS = 16
CONVW = 1152
BASES = 4
GRAMS = 344


EPS = 1e-05
HIGH = lax.Precision.HIGHEST


def rms_gain(values, gain_row):
    return values * lax.rsqrt(jnp.mean(values * values, axis=-1, keepdims=True) + EPS) * gain_row


def to_blocks(values, block_width):
    streams, count = (values.shape[0], values.shape[1])
    return jnp.moveaxis(
        values.reshape((streams, count // block_width, block_width) + values.shape[2:]), 1, 0
    )


def ssd_block(carry_state, block_in):
    x_blk, b_blk, c_blk, decay_blk, dt_blk = block_in
    cumulated = jnp.cumsum(decay_blk, axis=2)
    block_len = decay_blk.shape[2]
    scores = jnp.einsum("gtn,gsn->gts", c_blk, b_blk, precision=HIGH)
    seg_diff = cumulated[:, :, :, None] - cumulated[:, :, None, :]
    lower_mask = jnp.arange(block_len)[:, None] >= jnp.arange(block_len)[None, :]
    decays = jnp.where(lower_mask, jnp.exp(jnp.where(lower_mask, seg_diff, 0.0)), 0.0)
    weights = (scores[:, None] * decays * dt_blk[:, :, None, :]).astype(jnp.bfloat16)
    y_intra = jnp.einsum("ghts,gshp->gthp", weights, x_blk, preferred_element_type=jnp.float32)
    y_inter = (
        jnp.einsum("gtn,ghpn->gthp", c_blk, carry_state, precision=HIGH)
        * jnp.swapaxes(jnp.exp(cumulated), 1, 2)[..., None]
    )
    last_cum = cumulated[:, :, -1:]
    scaled = jnp.exp(last_cum - cumulated) * dt_blk
    x_weighted = x_blk.astype(jnp.float32) * jnp.swapaxes(scaled, 1, 2)[..., None]
    new_state = jnp.exp(last_cum)[..., None] * carry_state + jnp.einsum(
        "gshp,gsn->ghpn", x_weighted, b_blk, precision=HIGH
    )
    return (new_state, y_intra + y_inter)


def gram_layout():
    rows = []
    for real in range(1, KW + 1):
        for code in range(BASES**real):
            taps = [None] * (KW - real) + [
                (code // BASES ** (real - 1 - k)) % BASES for k in range(real)
            ]
            rows.append(taps)
    picks = np.zeros((GRAMS, KW * BASES), np.float32)
    for row, taps in enumerate(rows):
        for offset, base in enumerate(taps):
            if base is not None:
                picks[row, offset * BASES + base] = 1.0
    return picks


def gram_tables(emb_full, norm_gain, w_xbc, w_z, w_dt, conv_w, conv_bias):
    row_norm = rms_gain(emb_full.astype(jnp.float32), norm_gain).astype(jnp.bfloat16)
    xbc_rows = jnp.dot(row_norm, w_xbc, preferred_element_type=jnp.float32).astype(jnp.bfloat16)
    z_rows = jnp.dot(row_norm, w_z, preferred_element_type=jnp.float32).astype(jnp.bfloat16)
    dt_rows = jnp.dot(row_norm, w_dt, preferred_element_type=jnp.float32)
    taps = (conv_w[:, None, :] * xbc_rows.astype(jnp.float32)[None]).reshape(KW * BASES, CONVW)
    conv_sum = conv_bias + jnp.dot(jnp.asarray(gram_layout()), taps, precision=HIGH)
    return jax.nn.silu(conv_sum), z_rows, dt_rows


def gram_ids(ext, where_in):
    count = where_in.shape[1]
    code = jnp.zeros_like(where_in)
    ids = jnp.zeros_like(where_in)
    offset_of = 0
    for real in range(1, KW + 1):
        code = code + ext[:, KW - real : KW - real + count] * BASES ** (real - 1)
        chosen = (where_in >= real - 1) if real == KW else (where_in == real - 1)
        ids = jnp.where(chosen, offset_of + code, ids)
        offset_of += BASES**real
    return ids


def gather_all(fwd, rc, axis):
    count = lax.axis_size(axis)
    place = lax.axis_index(axis)
    rows = fwd.shape[0]
    held = jnp.concatenate([fwd, rc], axis=0)
    bit = 0
    while 2**bit < count:
        mask = 2**bit
        other = lax.ppermute(held, axis, [(src, src ^ mask) for src in range(count)])
        upper = (place // mask) % 2 == 1
        low_first = jnp.concatenate([held, other], axis=1)
        high_first = jnp.concatenate([other, held], axis=1)
        held = jnp.concatenate(
            [
                jnp.where(upper, high_first[:rows], low_first[:rows]),
                jnp.where(upper, low_first[rows:], high_first[rows:]),
            ],
            axis=0,
        )
        bit += 1
    return held


def heads_lookup(rows, bases):
    picked = jnp.zeros(bases.shape[:-1] + (rows.shape[1], bases.shape[-1]), jnp.float32)
    for base in range(BASES):
        picked = picked + jnp.where(
            (bases == base)[..., None, :], rows[base][:, None], 0.0
        )
    return picked


def onehot(ids, size):
    return (ids[..., None] == jnp.arange(size, dtype=ids.dtype)).astype(jnp.bfloat16)


def exchange(size):
    rows = lax.broadcasted_iota(jnp.int32, (size, size), 0)
    cols = lax.broadcasted_iota(jnp.int32, (size, size), 1)
    return (rows + cols == size - 1).astype(jnp.bfloat16)


def split_bf16(values):
    high = values.astype(jnp.bfloat16)
    return high, (values - high.astype(jnp.float32)).astype(jnp.bfloat16)


def block_cumsum(values, tri):
    return jnp.einsum("...s,st->...t", values, tri, precision=HIGH)


def local(
    tokens,
    emb_half,
    norm_gain,
    w_xbc,
    w_z,
    w_dt,
    conv_w,
    conv_bias,
    dt_bias,
    a_log,
    d_skip,
    inner_gain,
    w_out,
    final_gain,
    w_head_half,
    teacher_top,
    teacher_vals,
):
    windows, count = tokens.shape
    nseq = lax.axis_size("seq")
    place = lax.axis_index("seq")
    total = count * nseq
    nblk = total // BLK
    nloc = count // BLK
    streams = 2 * windows
    units = streams * nloc
    tri = (jnp.arange(BLK)[:, None] <= jnp.arange(BLK)[None, :]).astype(jnp.float32)

    flip_d = exchange(emb_half.shape[1])
    emb_flip = jnp.dot(emb_half, flip_d, preferred_element_type=jnp.float32).astype(jnp.bfloat16)
    emb_full = jnp.concatenate([emb_half, emb_flip[1:2], emb_flip[0:1]], axis=0)
    act_tab, z_rows, dt_rows = gram_tables(emb_full, norm_gain, w_xbc, w_z, w_dt, conv_w, conv_bias)
    x_tab = act_tab[:, :INNER].astype(jnp.bfloat16)
    b_tab = act_tab[:, INNER : INNER + NS]
    bc_tab = act_tab[:, INNER:]
    x_heads = x_tab.reshape(GRAMS, HEADS, HD).transpose(1, 0, 2)
    neg_rate = -jnp.exp(a_log)[:, None]

    flip_t = exchange(count)
    rc_tok = (BASES - 1) - jnp.dot(
        tokens.astype(jnp.bfloat16), flip_t, preferred_element_type=jnp.float32
    ).astype(jnp.int32)
    local_tok = jnp.concatenate([tokens, rc_tok], axis=0)
    pos0 = jnp.concatenate(
        [jnp.full((windows, 1), place * count), jnp.full((windows, 1), (nseq - 1 - place) * count)]
    ).astype(jnp.int32)

    seq_tok = gather_all(tokens, rc_tok, "seq")
    ext_all = jnp.concatenate([jnp.zeros((streams, KW - 1), seq_tok.dtype), seq_tok], axis=1)
    gram = gram_ids(ext_all, jnp.broadcast_to(jnp.arange(total, dtype=jnp.int32), (streams, total)))
    local_gram = jnp.concatenate(
        [
            lax.dynamic_slice_in_dim(gram[:windows], place * count, count, axis=1),
            lax.dynamic_slice_in_dim(gram[windows:], (nseq - 1 - place) * count, count, axis=1),
        ],
        axis=0,
    )

    oh_loc = onehot(local_gram, GRAMS)
    x_loc = jnp.einsum("rtg,gc->rtc", oh_loc, x_tab, preferred_element_type=jnp.float32).astype(
        jnp.bfloat16
    )
    bc_loc = jnp.einsum("rtg,gc->rtc", oh_loc, bc_tab, precision=HIGH)
    oh_tok = onehot(local_tok, BASES)
    z_loc = jnp.einsum("rtk,kc->rtc", oh_tok, z_rows, preferred_element_type=jnp.float32)
    dt_loc = jax.nn.softplus(heads_lookup(dt_rows, local_tok) + dt_bias[:, None])
    ld_loc = neg_rate * dt_loc

    def per_unit(values, axis):
        shape = values.shape
        split = shape[:axis] + (nloc, BLK) + shape[axis + 1 :]
        moved = jnp.moveaxis(values.reshape(split), axis, 1)
        return moved.reshape((units,) + moved.shape[2:])

    x_u = per_unit(x_loc, 1).reshape(units, BLK, HEADS, HD)
    b_u = per_unit(bc_loc[..., :NS], 1)
    c_u = per_unit(bc_loc[..., NS:], 1)
    dt_u = per_unit(dt_loc, 2)
    cum_u = block_cumsum(per_unit(ld_loc, 2), tri)

    scores = jnp.einsum("utn,usn->uts", c_u, b_u, precision=lax.Precision.HIGH)
    seg_diff = cum_u[:, :, :, None] - cum_u[:, :, None, :]
    lower = tri.T > 0
    decays = jnp.where(lower, jnp.exp(jnp.where(lower, seg_diff, 0.0)), 0.0)
    weights = (scores[:, None] * decays * dt_u[:, :, None, :]).astype(jnp.bfloat16)
    y_intra = jnp.einsum("uhts,ushp->uthp", weights, x_u, preferred_element_type=jnp.float32)

    dt_all = jax.nn.softplus(heads_lookup(dt_rows, seq_tok) + dt_bias[:, None])
    ld_all = neg_rate * dt_all
    cum = block_cumsum(ld_all.reshape(streams, HEADS, nblk, BLK), tri)
    blk_total = cum[..., -1]
    within = jnp.exp(blk_total[..., None] - cum) * dt_all.reshape(streams, HEADS, nblk, BLK)

    first_blk = (
        jnp.repeat(pos0[:, 0] // BLK, nloc) + jnp.tile(jnp.arange(nloc, dtype=jnp.int32), streams)
    )
    blk_idx = jnp.arange(nblk)
    total_u = jnp.repeat(blk_total, nloc, axis=0)
    between = (blk_idx[:, None] < blk_idx[None, :])[None] & (
        blk_idx[None, None, :] < first_blk[:, None, None]
    )
    span = jnp.sum(jnp.where(between[:, None], total_u[:, :, None, :], 0.0), axis=3)
    across = jnp.where(blk_idx[None, None, :] < first_blk[:, None, None], jnp.exp(span), 0.0)
    weight = jnp.repeat(within, nloc, axis=0) * across[..., None]
    w_hi, w_lo = split_bf16(weight)
    oh_all = jnp.repeat(onehot(gram, GRAMS), nloc, axis=0).reshape(units, nblk, BLK, GRAMS)
    per_gram = jnp.einsum(
        "uhbs,ubsg->uhg",
        jnp.concatenate([w_hi, w_lo], axis=1),
        oh_all,
        preferred_element_type=jnp.float32,
    )
    per_gram = per_gram[:, :HEADS] + per_gram[:, HEADS:]
    b_hi, b_lo = split_bf16(per_gram[..., None] * b_tab[None, None])
    start_state = jnp.einsum("hgp,uhgn->uhpn", x_heads, b_hi, preferred_element_type=jnp.float32)

    y_inter = (
        jnp.einsum("utn,uhpn->uthp", c_u, start_state, precision=lax.Precision.HIGH)
        * jnp.exp(cum_u).transpose(0, 2, 1)[..., None]
    )
    y_u = y_intra + y_inter + d_skip[:, None] * x_u.astype(jnp.float32)
    z_u = per_unit(z_loc, 1).reshape(units, BLK, HEADS, HD)
    gated_y = y_u * jax.nn.silu(z_u)
    normed = rms_gain(gated_y, inner_gain.reshape(HEADS, HD)).astype(jnp.bfloat16)
    normed = jnp.moveaxis(normed.reshape(streams, nloc, BLK, INNER), 1, 1).reshape(
        streams, count, INNER
    )
    outputs = jnp.einsum("gre,ed->grd", normed, w_out, preferred_element_type=jnp.float32).astype(
        jnp.bfloat16
    )

    embedded = jnp.einsum(
        "grk,kd->grd", oh_tok[:windows], emb_full, preferred_element_type=jnp.float32
    ).astype(jnp.bfloat16)
    returned = outputs[windows:, ::-1, ::-1]
    hidden_out = (
        embedded.astype(jnp.float32)
        + outputs[:windows].astype(jnp.float32)
        + returned.astype(jnp.float32)
    ).astype(jnp.bfloat16)
    final_normed = rms_gain(hidden_out.astype(jnp.float32), final_gain).astype(jnp.bfloat16)
    head_flip = jnp.dot(flip_d, w_head_half, preferred_element_type=jnp.float32).astype(
        jnp.bfloat16
    )
    head_full = jnp.concatenate([w_head_half, head_flip[:, 1:2], head_flip[:, 0:1]], axis=1)
    logits = jnp.einsum("grd,db->grb", final_normed, head_full, preferred_element_type=jnp.float32)
    log_q = logits - jnp.log(jnp.sum(jnp.exp(logits), axis=-1, keepdims=True))
    top_value = jnp.max(teacher_vals, axis=1, keepdims=True)
    shifted = teacher_vals - top_value
    log_p = shifted - jnp.log(jnp.sum(jnp.exp(shifted), axis=1, keepdims=True))
    matches = teacher_top[..., None] == jnp.arange(4, dtype=jnp.int32)
    picked = jnp.sum(jnp.where(matches, log_q[:, None, :, :], 0.0), axis=-1)
    divergence = jnp.sum(jnp.exp(log_p) * (log_p - picked), axis=1)
    return (hidden_out, divergence)


def solution(mesh):
    placed = (
        P("grp", "seq"),
        P(),
        P(),
        P(),
        P(),
        P(),
        P(),
        P(),
        P(),
        P(),
        P(),
        P(),
        P(),
        P(),
        P(),
        P("grp", None, "seq"),
        P("grp", None, "seq"),
    )
    return jax.shard_map(
        local,
        mesh=mesh,
        in_specs=placed,
        out_specs=(P("grp", "seq", None), P("grp", "seq")),
        check_vma=False,
    )
```

```python
import jax
import jax.numpy as jnp
import numpy as np
from jax import lax
from jax.sharding import PartitionSpec as P

INNER = 1024
HD = 64
NS = 64
KW = 4
BLK = 128
HEADS = 16
CONVW = 1152
BASES = 4
GRAMS = 344


EPS = 1e-05
HIGH = lax.Precision.HIGHEST


def rms_gain(values, gain_row):
    return values * lax.rsqrt(jnp.mean(values * values, axis=-1, keepdims=True) + EPS) * gain_row


def to_blocks(values, block_width):
    streams, count = (values.shape[0], values.shape[1])
    return jnp.moveaxis(
        values.reshape((streams, count // block_width, block_width) + values.shape[2:]), 1, 0
    )


def ssd_block(carry_state, block_in):
    x_blk, b_blk, c_blk, decay_blk, dt_blk = block_in
    cumulated = jnp.cumsum(decay_blk, axis=2)
    block_len = decay_blk.shape[2]
    scores = jnp.einsum("gtn,gsn->gts", c_blk, b_blk, precision=HIGH)
    seg_diff = cumulated[:, :, :, None] - cumulated[:, :, None, :]
    lower_mask = jnp.arange(block_len)[:, None] >= jnp.arange(block_len)[None, :]
    decays = jnp.where(lower_mask, jnp.exp(jnp.where(lower_mask, seg_diff, 0.0)), 0.0)
    weights = (scores[:, None] * decays * dt_blk[:, :, None, :]).astype(jnp.bfloat16)
    y_intra = jnp.einsum("ghts,gshp->gthp", weights, x_blk, preferred_element_type=jnp.float32)
    y_inter = (
        jnp.einsum("gtn,ghpn->gthp", c_blk, carry_state, precision=HIGH)
        * jnp.swapaxes(jnp.exp(cumulated), 1, 2)[..., None]
    )
    last_cum = cumulated[:, :, -1:]
    scaled = jnp.exp(last_cum - cumulated) * dt_blk
    x_weighted = x_blk.astype(jnp.float32) * jnp.swapaxes(scaled, 1, 2)[..., None]
    new_state = jnp.exp(last_cum)[..., None] * carry_state + jnp.einsum(
        "gshp,gsn->ghpn", x_weighted, b_blk, precision=HIGH
    )
    return (new_state, y_intra + y_inter)


def gram_layout():
    rows = []
    for real in range(1, KW + 1):
        for code in range(BASES**real):
            taps = [None] * (KW - real) + [
                (code // BASES ** (real - 1 - k)) % BASES for k in range(real)
            ]
            rows.append(taps)
    picks = np.zeros((GRAMS, KW * BASES), np.float32)
    for row, taps in enumerate(rows):
        for offset, base in enumerate(taps):
            if base is not None:
                picks[row, offset * BASES + base] = 1.0
    return picks


def gram_tables(emb_full, norm_gain, w_xbc, w_z, w_dt, conv_w, conv_bias):
    row_norm = rms_gain(emb_full.astype(jnp.float32), norm_gain).astype(jnp.bfloat16)
    xbc_rows = jnp.dot(row_norm, w_xbc, preferred_element_type=jnp.float32).astype(jnp.bfloat16)
    z_rows = jnp.dot(row_norm, w_z, preferred_element_type=jnp.float32).astype(jnp.bfloat16)
    dt_rows = jnp.dot(row_norm, w_dt, preferred_element_type=jnp.float32)
    taps = (conv_w[:, None, :] * xbc_rows.astype(jnp.float32)[None]).reshape(KW * BASES, CONVW)
    conv_sum = conv_bias + jnp.dot(jnp.asarray(gram_layout()), taps, precision=HIGH)
    return jax.nn.silu(conv_sum), z_rows, dt_rows


def gram_ids(ext, where_in):
    count = where_in.shape[1]
    code = jnp.zeros_like(where_in)
    ids = jnp.zeros_like(where_in)
    offset_of = 0
    for real in range(1, KW + 1):
        code = code + ext[:, KW - real : KW - real + count] * BASES ** (real - 1)
        chosen = (where_in >= real - 1) if real == KW else (where_in == real - 1)
        ids = jnp.where(chosen, offset_of + code, ids)
        offset_of += BASES**real
    return ids


def gather_all(fwd, rc, axis):
    count = lax.axis_size(axis)
    place = lax.axis_index(axis)
    rows = fwd.shape[0]
    held = jnp.concatenate([fwd, rc], axis=0)
    bit = 0
    while 2**bit < count:
        mask = 2**bit
        other = lax.ppermute(held, axis, [(src, src ^ mask) for src in range(count)])
        upper = (place // mask) % 2 == 1
        low_first = jnp.concatenate([held, other], axis=1)
        high_first = jnp.concatenate([other, held], axis=1)
        held = jnp.concatenate(
            [
                jnp.where(upper, high_first[:rows], low_first[:rows]),
                jnp.where(upper, low_first[rows:], high_first[rows:]),
            ],
            axis=0,
        )
        bit += 1
    return held


def heads_lookup(rows, bases):
    picked = jnp.zeros(bases.shape[:-1] + (rows.shape[1], bases.shape[-1]), jnp.float32)
    for base in range(BASES):
        picked = picked + jnp.where(
            (bases == base)[..., None, :], rows[base][:, None], 0.0
        )
    return picked


def onehot(ids, size):
    return (ids[..., None] == jnp.arange(size, dtype=ids.dtype)).astype(jnp.bfloat16)


def exchange(size):
    rows = lax.broadcasted_iota(jnp.int32, (size, size), 0)
    cols = lax.broadcasted_iota(jnp.int32, (size, size), 1)
    return (rows + cols == size - 1).astype(jnp.bfloat16)


def split_bf16(values):
    high = values.astype(jnp.bfloat16)
    return high, (values - high.astype(jnp.float32)).astype(jnp.bfloat16)


def block_cumsum(values, tri):
    return jnp.einsum("...s,st->...t", values, tri, precision=HIGH)


def local(
    tokens,
    emb_half,
    norm_gain,
    w_xbc,
    w_z,
    w_dt,
    conv_w,
    conv_bias,
    dt_bias,
    a_log,
    d_skip,
    inner_gain,
    w_out,
    final_gain,
    w_head_half,
    teacher_top,
    teacher_vals,
):
    windows, count = tokens.shape
    nseq = lax.axis_size("seq")
    place = lax.axis_index("seq")
    total = count * nseq
    nblk = total // BLK
    nloc = count // BLK
    streams = 2 * windows
    units = streams * nloc
    tri = (jnp.arange(BLK)[:, None] <= jnp.arange(BLK)[None, :]).astype(jnp.float32)

    flip_d = exchange(emb_half.shape[1])
    emb_flip = jnp.dot(emb_half, flip_d, preferred_element_type=jnp.float32).astype(jnp.bfloat16)
    emb_full = jnp.concatenate([emb_half, emb_flip[1:2], emb_flip[0:1]], axis=0)
    act_tab, z_rows, dt_rows = gram_tables(emb_full, norm_gain, w_xbc, w_z, w_dt, conv_w, conv_bias)
    x_tab = act_tab[:, :INNER].astype(jnp.bfloat16)
    b_tab = act_tab[:, INNER : INNER + NS]
    bc_tab = act_tab[:, INNER:]
    x_heads = x_tab.reshape(GRAMS, HEADS, HD).transpose(1, 0, 2)
    neg_rate = -jnp.exp(a_log)[:, None]

    flip_t = exchange(count)
    rc_tok = (BASES - 1) - jnp.dot(
        tokens.astype(jnp.bfloat16), flip_t, preferred_element_type=jnp.float32
    ).astype(jnp.int32)
    local_tok = jnp.concatenate([tokens, rc_tok], axis=0)
    pos0 = jnp.concatenate(
        [jnp.full((windows, 1), place * count), jnp.full((windows, 1), (nseq - 1 - place) * count)]
    ).astype(jnp.int32)

    seq_tok = gather_all(tokens, rc_tok, "seq")
    ext_all = jnp.concatenate([jnp.zeros((streams, KW - 1), seq_tok.dtype), seq_tok], axis=1)
    gram = gram_ids(ext_all, jnp.broadcast_to(jnp.arange(total, dtype=jnp.int32), (streams, total)))
    local_gram = jnp.concatenate(
        [
            lax.dynamic_slice_in_dim(gram[:windows], place * count, count, axis=1),
            lax.dynamic_slice_in_dim(gram[windows:], (nseq - 1 - place) * count, count, axis=1),
        ],
        axis=0,
    )

    oh_loc = onehot(local_gram, GRAMS)
    x_loc = jnp.einsum("rtg,gc->rtc", oh_loc, x_tab, preferred_element_type=jnp.float32).astype(
        jnp.bfloat16
    )
    bc_loc = jnp.einsum("rtg,gc->rtc", oh_loc, bc_tab, precision=HIGH)
    oh_tok = onehot(local_tok, BASES)
    z_loc = jnp.einsum("rtk,kc->rtc", oh_tok, z_rows, preferred_element_type=jnp.float32)
    dt_loc = jax.nn.softplus(heads_lookup(dt_rows, local_tok) + dt_bias[:, None])
    ld_loc = neg_rate * dt_loc

    def per_unit(values, axis):
        shape = values.shape
        split = shape[:axis] + (nloc, BLK) + shape[axis + 1 :]
        moved = jnp.moveaxis(values.reshape(split), axis, 1)
        return moved.reshape((units,) + moved.shape[2:])

    x_u = per_unit(x_loc, 1).reshape(units, BLK, HEADS, HD)
    b_u = per_unit(bc_loc[..., :NS], 1)
    c_u = per_unit(bc_loc[..., NS:], 1)
    dt_u = per_unit(dt_loc, 2)
    cum_u = block_cumsum(per_unit(ld_loc, 2), tri)

    scores = jnp.einsum("utn,usn->uts", c_u, b_u, precision=lax.Precision.HIGH)
    seg_diff = cum_u[:, :, :, None] - cum_u[:, :, None, :]
    lower = tri.T > 0
    decays = jnp.where(lower, jnp.exp(jnp.where(lower, seg_diff, 0.0)), 0.0)
    weights = (scores[:, None] * decays * dt_u[:, :, None, :]).astype(jnp.bfloat16)
    y_intra = jnp.einsum("uhts,ushp->uthp", weights, x_u, preferred_element_type=jnp.float32)

    dt_all = jax.nn.softplus(heads_lookup(dt_rows, seq_tok) + dt_bias[:, None])
    ld_all = neg_rate * dt_all
    cum = block_cumsum(ld_all.reshape(streams, HEADS, nblk, BLK), tri)
    blk_total = cum[..., -1]
    within = jnp.exp(blk_total[..., None] - cum) * dt_all.reshape(streams, HEADS, nblk, BLK)

    first_blk = (
        jnp.repeat(pos0[:, 0] // BLK, nloc) + jnp.tile(jnp.arange(nloc, dtype=jnp.int32), streams)
    )
    blk_idx = jnp.arange(nblk)
    total_u = jnp.repeat(blk_total, nloc, axis=0)
    between = (blk_idx[:, None] < blk_idx[None, :])[None] & (
        blk_idx[None, None, :] < first_blk[:, None, None]
    )
    span = jnp.sum(jnp.where(between[:, None], total_u[:, :, None, :], 0.0), axis=3)
    across = jnp.where(blk_idx[None, None, :] < first_blk[:, None, None], jnp.exp(span), 0.0)
    weight = jnp.repeat(within, nloc, axis=0) * across[..., None]
    oh_all = jnp.repeat(onehot(gram, GRAMS), nloc, axis=0).reshape(units, nblk, BLK, GRAMS)
    per_gram = jnp.einsum(
        "uhbs,ubsg->uhg",
        weight.astype(jnp.bfloat16),
        oh_all,
        preferred_element_type=jnp.float32,
    )
    b_hi, b_lo = split_bf16(per_gram[..., None] * b_tab[None, None])
    start_state = jnp.einsum("hgp,uhgn->uhpn", x_heads, b_hi, preferred_element_type=jnp.float32)

    y_inter = (
        jnp.einsum("utn,uhpn->uthp", c_u, start_state, precision=lax.Precision.HIGH)
        * jnp.exp(cum_u).transpose(0, 2, 1)[..., None]
    )
    y_u = y_intra + y_inter + d_skip[:, None] * x_u.astype(jnp.float32)
    z_u = per_unit(z_loc, 1).reshape(units, BLK, HEADS, HD)
    gated_y = y_u * jax.nn.silu(z_u)
    normed = rms_gain(gated_y, inner_gain.reshape(HEADS, HD)).astype(jnp.bfloat16)
    normed = jnp.moveaxis(normed.reshape(streams, nloc, BLK, INNER), 1, 1).reshape(
        streams, count, INNER
    )
    outputs = jnp.einsum("gre,ed->grd", normed, w_out, preferred_element_type=jnp.float32).astype(
        jnp.bfloat16
    )

    embedded = jnp.einsum(
        "grk,kd->grd", oh_tok[:windows], emb_full, preferred_element_type=jnp.float32
    ).astype(jnp.bfloat16)
    returned = outputs[windows:, ::-1, ::-1]
    hidden_out = (
        embedded.astype(jnp.float32)
        + outputs[:windows].astype(jnp.float32)
        + returned.astype(jnp.float32)
    ).astype(jnp.bfloat16)
    final_normed = rms_gain(hidden_out.astype(jnp.float32), final_gain).astype(jnp.bfloat16)
    head_flip = jnp.dot(flip_d, w_head_half, preferred_element_type=jnp.float32).astype(
        jnp.bfloat16
    )
    head_full = jnp.concatenate([w_head_half, head_flip[:, 1:2], head_flip[:, 0:1]], axis=1)
    logits = jnp.einsum("grd,db->grb", final_normed, head_full, preferred_element_type=jnp.float32)
    log_q = logits - jnp.log(jnp.sum(jnp.exp(logits), axis=-1, keepdims=True))
    top_value = jnp.max(teacher_vals, axis=1, keepdims=True)
    shifted = teacher_vals - top_value
    log_p = shifted - jnp.log(jnp.sum(jnp.exp(shifted), axis=1, keepdims=True))
    matches = teacher_top[..., None] == jnp.arange(4, dtype=jnp.int32)
    picked = jnp.sum(jnp.where(matches, log_q[:, None, :, :], 0.0), axis=-1)
    divergence = jnp.sum(jnp.exp(log_p) * (log_p - picked), axis=1)
    return (hidden_out, divergence)


def solution(mesh):
    placed = (
        P("grp", "seq"),
        P(),
        P(),
        P(),
        P(),
        P(),
        P(),
        P(),
        P(),
        P(),
        P(),
        P(),
        P(),
        P(),
        P(),
        P("grp", None, "seq"),
        P("grp", None, "seq"),
    )
    return jax.shard_map(
        local,
        mesh=mesh,
        in_specs=placed,
        out_specs=(P("grp", "seq", None), P("grp", "seq")),
        check_vma=False,
    )
```

```python
import jax
import jax.numpy as jnp
import numpy as np
from jax import lax
from jax.sharding import PartitionSpec as P

INNER = 1024
HD = 64
NS = 64
KW = 4
BLK = 128
HEADS = 16
CONVW = 1152
BASES = 4
GRAMS = 344


EPS = 1e-05
HIGH = lax.Precision.HIGHEST


def rms_gain(values, gain_row):
    return values * lax.rsqrt(jnp.mean(values * values, axis=-1, keepdims=True) + EPS) * gain_row


def to_blocks(values, block_width):
    streams, count = (values.shape[0], values.shape[1])
    return jnp.moveaxis(
        values.reshape((streams, count // block_width, block_width) + values.shape[2:]), 1, 0
    )


def ssd_block(carry_state, block_in):
    x_blk, b_blk, c_blk, decay_blk, dt_blk = block_in
    cumulated = jnp.cumsum(decay_blk, axis=2)
    block_len = decay_blk.shape[2]
    scores = jnp.einsum("gtn,gsn->gts", c_blk, b_blk, precision=HIGH)
    seg_diff = cumulated[:, :, :, None] - cumulated[:, :, None, :]
    lower_mask = jnp.arange(block_len)[:, None] >= jnp.arange(block_len)[None, :]
    decays = jnp.where(lower_mask, jnp.exp(jnp.where(lower_mask, seg_diff, 0.0)), 0.0)
    weights = (scores[:, None] * decays * dt_blk[:, :, None, :]).astype(jnp.bfloat16)
    y_intra = jnp.einsum("ghts,gshp->gthp", weights, x_blk, preferred_element_type=jnp.float32)
    y_inter = (
        jnp.einsum("gtn,ghpn->gthp", c_blk, carry_state, precision=HIGH)
        * jnp.swapaxes(jnp.exp(cumulated), 1, 2)[..., None]
    )
    last_cum = cumulated[:, :, -1:]
    scaled = jnp.exp(last_cum - cumulated) * dt_blk
    x_weighted = x_blk.astype(jnp.float32) * jnp.swapaxes(scaled, 1, 2)[..., None]
    new_state = jnp.exp(last_cum)[..., None] * carry_state + jnp.einsum(
        "gshp,gsn->ghpn", x_weighted, b_blk, precision=HIGH
    )
    return (new_state, y_intra + y_inter)


def gram_layout():
    rows = []
    for real in range(1, KW + 1):
        for code in range(BASES**real):
            taps = [None] * (KW - real) + [
                (code // BASES ** (real - 1 - k)) % BASES for k in range(real)
            ]
            rows.append(taps)
    picks = np.zeros((GRAMS, KW * BASES), np.float32)
    for row, taps in enumerate(rows):
        for offset, base in enumerate(taps):
            if base is not None:
                picks[row, offset * BASES + base] = 1.0
    return picks


def gram_tables(emb_full, norm_gain, w_xbc, w_z, w_dt, conv_w, conv_bias):
    row_norm = rms_gain(emb_full.astype(jnp.float32), norm_gain).astype(jnp.bfloat16)
    xbc_rows = jnp.dot(row_norm, w_xbc, preferred_element_type=jnp.float32).astype(jnp.bfloat16)
    z_rows = jnp.dot(row_norm, w_z, preferred_element_type=jnp.float32).astype(jnp.bfloat16)
    dt_rows = jnp.dot(row_norm, w_dt, preferred_element_type=jnp.float32)
    taps = (conv_w[:, None, :] * xbc_rows.astype(jnp.float32)[None]).reshape(KW * BASES, CONVW)
    conv_sum = conv_bias + jnp.dot(jnp.asarray(gram_layout()), taps, precision=HIGH)
    return jax.nn.silu(conv_sum), z_rows, dt_rows


def gram_ids(ext, where_in):
    count = where_in.shape[1]
    code = jnp.zeros_like(where_in)
    ids = jnp.zeros_like(where_in)
    offset_of = 0
    for real in range(1, KW + 1):
        code = code + ext[:, KW - real : KW - real + count] * BASES ** (real - 1)
        chosen = (where_in >= real - 1) if real == KW else (where_in == real - 1)
        ids = jnp.where(chosen, offset_of + code, ids)
        offset_of += BASES**real
    return ids


def gather_all(fwd, rc, axis):
    count = lax.axis_size(axis)
    place = lax.axis_index(axis)
    rows = fwd.shape[0]
    held = jnp.concatenate([fwd, rc], axis=0)
    bit = 0
    while 2**bit < count:
        mask = 2**bit
        other = lax.ppermute(held, axis, [(src, src ^ mask) for src in range(count)])
        upper = (place // mask) % 2 == 1
        low_first = jnp.concatenate([held, other], axis=1)
        high_first = jnp.concatenate([other, held], axis=1)
        held = jnp.concatenate(
            [
                jnp.where(upper, high_first[:rows], low_first[:rows]),
                jnp.where(upper, low_first[rows:], high_first[rows:]),
            ],
            axis=0,
        )
        bit += 1
    return held


def heads_lookup(rows, bases):
    picked = jnp.zeros(bases.shape[:-1] + (rows.shape[1], bases.shape[-1]), jnp.float32)
    for base in range(BASES):
        picked = picked + jnp.where(
            (bases == base)[..., None, :], rows[base][:, None], 0.0
        )
    return picked


def onehot(ids, size):
    return (ids[..., None] == jnp.arange(size, dtype=ids.dtype)).astype(jnp.bfloat16)


def exchange(size):
    rows = lax.broadcasted_iota(jnp.int32, (size, size), 0)
    cols = lax.broadcasted_iota(jnp.int32, (size, size), 1)
    return (rows + cols == size - 1).astype(jnp.bfloat16)


def split_bf16(values):
    high = values.astype(jnp.bfloat16)
    return high, (values - high.astype(jnp.float32)).astype(jnp.bfloat16)


def block_cumsum(values, tri):
    return jnp.einsum("...s,st->...t", values, tri, precision=HIGH)


def local(
    tokens,
    emb_half,
    norm_gain,
    w_xbc,
    w_z,
    w_dt,
    conv_w,
    conv_bias,
    dt_bias,
    a_log,
    d_skip,
    inner_gain,
    w_out,
    final_gain,
    w_head_half,
    teacher_top,
    teacher_vals,
):
    windows, count = tokens.shape
    nseq = lax.axis_size("seq")
    place = lax.axis_index("seq")
    total = count * nseq
    nblk = total // BLK
    nloc = count // BLK
    streams = 2 * windows
    units = streams * nloc
    tri = (jnp.arange(BLK)[:, None] <= jnp.arange(BLK)[None, :]).astype(jnp.float32)

    flip_d = exchange(emb_half.shape[1])
    emb_flip = jnp.dot(emb_half, flip_d, preferred_element_type=jnp.float32).astype(jnp.bfloat16)
    emb_full = jnp.concatenate([emb_half, emb_flip[1:2], emb_flip[0:1]], axis=0)
    act_tab, z_rows, dt_rows = gram_tables(emb_full, norm_gain, w_xbc, w_z, w_dt, conv_w, conv_bias)
    x_tab = act_tab[:, :INNER].astype(jnp.bfloat16)
    b_tab = act_tab[:, INNER : INNER + NS]
    bc_tab = act_tab[:, INNER:]
    x_heads = x_tab.reshape(GRAMS, HEADS, HD).transpose(1, 0, 2)
    neg_rate = -jnp.exp(a_log)[:, None]

    flip_t = exchange(count)
    rc_tok = (BASES - 1) - jnp.dot(
        tokens.astype(jnp.bfloat16), flip_t, preferred_element_type=jnp.float32
    ).astype(jnp.int32)
    local_tok = jnp.concatenate([tokens, rc_tok], axis=0)
    pos0 = jnp.concatenate(
        [jnp.full((windows, 1), place * count), jnp.full((windows, 1), (nseq - 1 - place) * count)]
    ).astype(jnp.int32)

    seq_tok = gather_all(tokens, rc_tok, "seq")
    ext_all = jnp.concatenate([jnp.zeros((streams, KW - 1), seq_tok.dtype), seq_tok], axis=1)
    gram = gram_ids(ext_all, jnp.broadcast_to(jnp.arange(total, dtype=jnp.int32), (streams, total)))
    local_gram = jnp.concatenate(
        [
            lax.dynamic_slice_in_dim(gram[:windows], place * count, count, axis=1),
            lax.dynamic_slice_in_dim(gram[windows:], (nseq - 1 - place) * count, count, axis=1),
        ],
        axis=0,
    )

    oh_loc = onehot(local_gram, GRAMS)
    x_loc = jnp.einsum("rtg,gc->rtc", oh_loc, x_tab, preferred_element_type=jnp.float32).astype(
        jnp.bfloat16
    )
    bc_loc = jnp.einsum("rtg,gc->rtc", oh_loc, bc_tab, precision=HIGH)
    oh_tok = onehot(local_tok, BASES)
    gate_rows = jax.nn.silu(z_rows.astype(jnp.float32))
    gate_loc = jnp.einsum("rtk,kc->rtc", oh_tok, gate_rows, precision=HIGH)
    dt_loc = jax.nn.softplus(heads_lookup(dt_rows, local_tok) + dt_bias[:, None])
    ld_loc = neg_rate * dt_loc

    def per_unit(values, axis):
        shape = values.shape
        split = shape[:axis] + (nloc, BLK) + shape[axis + 1 :]
        moved = jnp.moveaxis(values.reshape(split), axis, 1)
        return moved.reshape((units,) + moved.shape[2:])

    x_u = per_unit(x_loc, 1).reshape(units, BLK, HEADS, HD)
    b_u = per_unit(bc_loc[..., :NS], 1)
    c_u = per_unit(bc_loc[..., NS:], 1)
    dt_u = per_unit(dt_loc, 2)
    cum_u = block_cumsum(per_unit(ld_loc, 2), tri)

    scores = jnp.einsum("utn,usn->uts", c_u, b_u, precision=lax.Precision.HIGH)
    seg_diff = cum_u[:, :, :, None] - cum_u[:, :, None, :]
    lower = tri.T > 0
    decays = jnp.where(lower, jnp.exp(jnp.where(lower, seg_diff, 0.0)), 0.0)
    weights = (scores[:, None] * decays * dt_u[:, :, None, :]).astype(jnp.bfloat16)
    y_intra = jnp.einsum("uhts,ushp->uthp", weights, x_u, preferred_element_type=jnp.float32)

    dt_all = jax.nn.softplus(heads_lookup(dt_rows, seq_tok) + dt_bias[:, None])
    ld_all = neg_rate * dt_all
    cum = block_cumsum(ld_all.reshape(streams, HEADS, nblk, BLK), tri)
    blk_total = cum[..., -1]
    within = jnp.exp(blk_total[..., None] - cum) * dt_all.reshape(streams, HEADS, nblk, BLK)

    first_blk = (
        jnp.repeat(pos0[:, 0] // BLK, nloc) + jnp.tile(jnp.arange(nloc, dtype=jnp.int32), streams)
    )
    blk_idx = jnp.arange(nblk)
    total_u = jnp.repeat(blk_total, nloc, axis=0)
    between = (blk_idx[:, None] < blk_idx[None, :])[None] & (
        blk_idx[None, None, :] < first_blk[:, None, None]
    )
    span = jnp.sum(jnp.where(between[:, None], total_u[:, :, None, :], 0.0), axis=3)
    across = jnp.where(blk_idx[None, None, :] < first_blk[:, None, None], jnp.exp(span), 0.0)
    weight = jnp.repeat(within, nloc, axis=0) * across[..., None]
    w_hi, w_lo = split_bf16(weight)
    oh_all = jnp.repeat(onehot(gram, GRAMS), nloc, axis=0).reshape(units, nblk, BLK, GRAMS)
    per_gram = jnp.einsum(
        "uhbs,ubsg->uhg",
        jnp.concatenate([w_hi, w_lo], axis=1),
        oh_all,
        preferred_element_type=jnp.float32,
    )
    per_gram = per_gram[:, :HEADS] + per_gram[:, HEADS:]
    b_hi, b_lo = split_bf16(per_gram[..., None] * b_tab[None, None])
    start_state = jnp.einsum("hgp,uhgn->uhpn", x_heads, b_hi, preferred_element_type=jnp.float32)

    y_inter = (
        jnp.einsum("utn,uhpn->uthp", c_u, start_state, precision=lax.Precision.HIGH)
        * jnp.exp(cum_u).transpose(0, 2, 1)[..., None]
    )
    y_u = y_intra + y_inter + d_skip[:, None] * x_u.astype(jnp.float32)
    gated_y = y_u * per_unit(gate_loc, 1).reshape(units, BLK, HEADS, HD)
    normed = rms_gain(gated_y, inner_gain.reshape(HEADS, HD)).astype(jnp.bfloat16)
    normed = jnp.moveaxis(normed.reshape(streams, nloc, BLK, INNER), 1, 1).reshape(
        streams, count, INNER
    )
    outputs = jnp.einsum("gre,ed->grd", normed, w_out, preferred_element_type=jnp.float32).astype(
        jnp.bfloat16
    )

    embedded = jnp.einsum(
        "grk,kd->grd", oh_tok[:windows], emb_full, preferred_element_type=jnp.float32
    ).astype(jnp.bfloat16)
    returned = outputs[windows:, ::-1, ::-1]
    hidden_out = (
        embedded.astype(jnp.float32)
        + outputs[:windows].astype(jnp.float32)
        + returned.astype(jnp.float32)
    ).astype(jnp.bfloat16)
    final_normed = rms_gain(hidden_out.astype(jnp.float32), final_gain).astype(jnp.bfloat16)
    head_flip = jnp.dot(flip_d, w_head_half, preferred_element_type=jnp.float32).astype(
        jnp.bfloat16
    )
    head_full = jnp.concatenate([w_head_half, head_flip[:, 1:2], head_flip[:, 0:1]], axis=1)
    logits = jnp.einsum("grd,db->grb", final_normed, head_full, preferred_element_type=jnp.float32)
    log_q = logits - jnp.log(jnp.sum(jnp.exp(logits), axis=-1, keepdims=True))
    top_value = jnp.max(teacher_vals, axis=1, keepdims=True)
    shifted = teacher_vals - top_value
    log_p = shifted - jnp.log(jnp.sum(jnp.exp(shifted), axis=1, keepdims=True))
    matches = teacher_top[..., None] == jnp.arange(4, dtype=jnp.int32)
    picked = jnp.sum(jnp.where(matches, log_q[:, None, :, :], 0.0), axis=-1)
    divergence = jnp.sum(jnp.exp(log_p) * (log_p - picked), axis=1)
    return (hidden_out, divergence)


def solution(mesh):
    placed = (
        P("grp", "seq"),
        P(),
        P(),
        P(),
        P(),
        P(),
        P(),
        P(),
        P(),
        P(),
        P(),
        P(),
        P(),
        P(),
        P(),
        P("grp", None, "seq"),
        P("grp", None, "seq"),
    )
    return jax.shard_map(
        local,
        mesh=mesh,
        in_specs=placed,
        out_specs=(P("grp", "seq", None), P("grp", "seq")),
        check_vma=False,
    )
```

```python
import jax
import jax.numpy as jnp
import numpy as np
from jax import lax
from jax.sharding import PartitionSpec as P

INNER = 1024
HD = 64
NS = 64
KW = 4
BLK = 128
HEADS = 16
CONVW = 1152
BASES = 4
GRAMS = 344


EPS = 1e-05
HIGH = lax.Precision.HIGHEST


def rms_gain(values, gain_row):
    return values * lax.rsqrt(jnp.mean(values * values, axis=-1, keepdims=True) + EPS) * gain_row


def to_blocks(values, block_width):
    streams, count = (values.shape[0], values.shape[1])
    return jnp.moveaxis(
        values.reshape((streams, count // block_width, block_width) + values.shape[2:]), 1, 0
    )


def ssd_block(carry_state, block_in):
    x_blk, b_blk, c_blk, decay_blk, dt_blk = block_in
    cumulated = jnp.cumsum(decay_blk, axis=2)
    block_len = decay_blk.shape[2]
    scores = jnp.einsum("gtn,gsn->gts", c_blk, b_blk, precision=HIGH)
    seg_diff = cumulated[:, :, :, None] - cumulated[:, :, None, :]
    lower_mask = jnp.arange(block_len)[:, None] >= jnp.arange(block_len)[None, :]
    decays = jnp.where(lower_mask, jnp.exp(jnp.where(lower_mask, seg_diff, 0.0)), 0.0)
    weights = (scores[:, None] * decays * dt_blk[:, :, None, :]).astype(jnp.bfloat16)
    y_intra = jnp.einsum("ghts,gshp->gthp", weights, x_blk, preferred_element_type=jnp.float32)
    y_inter = (
        jnp.einsum("gtn,ghpn->gthp", c_blk, carry_state, precision=HIGH)
        * jnp.swapaxes(jnp.exp(cumulated), 1, 2)[..., None]
    )
    last_cum = cumulated[:, :, -1:]
    scaled = jnp.exp(last_cum - cumulated) * dt_blk
    x_weighted = x_blk.astype(jnp.float32) * jnp.swapaxes(scaled, 1, 2)[..., None]
    new_state = jnp.exp(last_cum)[..., None] * carry_state + jnp.einsum(
        "gshp,gsn->ghpn", x_weighted, b_blk, precision=HIGH
    )
    return (new_state, y_intra + y_inter)


def gram_layout():
    rows = []
    for real in range(1, KW + 1):
        for code in range(BASES**real):
            taps = [None] * (KW - real) + [
                (code // BASES ** (real - 1 - k)) % BASES for k in range(real)
            ]
            rows.append(taps)
    picks = np.zeros((GRAMS, KW * BASES), np.float32)
    for row, taps in enumerate(rows):
        for offset, base in enumerate(taps):
            if base is not None:
                picks[row, offset * BASES + base] = 1.0
    return picks


def gram_tables(emb_full, norm_gain, w_xbc, w_z, w_dt, conv_w, conv_bias):
    row_norm = rms_gain(emb_full.astype(jnp.float32), norm_gain).astype(jnp.bfloat16)
    xbc_rows = jnp.dot(row_norm, w_xbc, preferred_element_type=jnp.float32).astype(jnp.bfloat16)
    z_rows = jnp.dot(row_norm, w_z, preferred_element_type=jnp.float32).astype(jnp.bfloat16)
    dt_rows = jnp.dot(row_norm, w_dt, preferred_element_type=jnp.float32)
    taps = (conv_w[:, None, :] * xbc_rows.astype(jnp.float32)[None]).reshape(KW * BASES, CONVW)
    conv_sum = conv_bias + jnp.dot(jnp.asarray(gram_layout()), taps, precision=HIGH)
    return jax.nn.silu(conv_sum), z_rows, dt_rows


def gram_ids(ext, where_in):
    count = where_in.shape[1]
    code = jnp.zeros_like(where_in)
    ids = jnp.zeros_like(where_in)
    offset_of = 0
    for real in range(1, KW + 1):
        code = code + ext[:, KW - real : KW - real + count] * BASES ** (real - 1)
        chosen = (where_in >= real - 1) if real == KW else (where_in == real - 1)
        ids = jnp.where(chosen, offset_of + code, ids)
        offset_of += BASES**real
    return ids


def gather_all(fwd, rc, axis):
    count = lax.axis_size(axis)
    place = lax.axis_index(axis)
    rows = fwd.shape[0]
    held = jnp.concatenate([fwd, rc], axis=0)
    bit = 0
    while 2**bit < count:
        mask = 2**bit
        other = lax.ppermute(held, axis, [(src, src ^ mask) for src in range(count)])
        upper = (place // mask) % 2 == 1
        low_first = jnp.concatenate([held, other], axis=1)
        high_first = jnp.concatenate([other, held], axis=1)
        held = jnp.concatenate(
            [
                jnp.where(upper, high_first[:rows], low_first[:rows]),
                jnp.where(upper, low_first[rows:], high_first[rows:]),
            ],
            axis=0,
        )
        bit += 1
    return held


def heads_lookup(rows, bases):
    picked = jnp.zeros(bases.shape[:-1] + (rows.shape[1], bases.shape[-1]), jnp.float32)
    for base in range(BASES):
        picked = picked + jnp.where(
            (bases == base)[..., None, :], rows[base][:, None], 0.0
        )
    return picked


def onehot(ids, size):
    return (ids[..., None] == jnp.arange(size, dtype=ids.dtype)).astype(jnp.bfloat16)


def exchange(size):
    rows = lax.broadcasted_iota(jnp.int32, (size, size), 0)
    cols = lax.broadcasted_iota(jnp.int32, (size, size), 1)
    return (rows + cols == size - 1).astype(jnp.bfloat16)


def split_bf16(values):
    high = values.astype(jnp.bfloat16)
    return high, (values - high.astype(jnp.float32)).astype(jnp.bfloat16)


def block_cumsum(values, tri):
    return jnp.einsum("...s,st->...t", values, tri, precision=HIGH)


def needed_per_gram(seq_tok, gram, dt_rows, dt_bias, neg_rate, tri, place, windows, nblk):
    need = nblk - 1

    def arranged(values):
        fwd = values[:windows].reshape(windows, nblk, BLK)
        rc = values[windows:].reshape(windows, nblk, BLK)[:, ::-1]
        joined = jnp.concatenate([rc, fwd], axis=1)
        return lax.dynamic_slice_in_dim(joined, place + 1, need, axis=1)

    tok_n = arranged(seq_tok)
    gram_n = arranged(gram)
    dt_n = jax.nn.softplus(
        heads_lookup(dt_rows, tok_n.reshape(windows, need * BLK)) + dt_bias[:, None]
    ).reshape(windows, HEADS, need, BLK)
    cum = block_cumsum(neg_rate[:, :, None] * dt_n, tri)
    blk_total = cum[..., -1]
    within = jnp.exp(blk_total[..., None] - cum) * dt_n
    idx = jnp.arange(need)
    is_fwd = idx >= (nblk - 1 - place)
    pick = jnp.where(is_fwd[:, None], idx[None, :] > idx[:, None], idx[None, :] < idx[:, None])
    span = jnp.sum(jnp.where(pick[None, None], blk_total[:, :, None, :], 0.0), axis=3)
    weight = within * jnp.exp(span)[..., None]
    fwd_part = is_fwd[None, None, :, None]
    w_hi, w_lo = split_bf16(
        jnp.concatenate(
            [jnp.where(fwd_part, weight, 0.0), jnp.where(fwd_part, 0.0, weight)], axis=1
        )
    )
    summed = jnp.einsum(
        "whbs,wbsg->whg",
        jnp.concatenate([w_hi, w_lo], axis=1),
        onehot(gram_n, GRAMS),
        preferred_element_type=jnp.float32,
    )
    summed = summed[:, : 2 * HEADS] + summed[:, 2 * HEADS :]
    return jnp.concatenate([summed[:, :HEADS], summed[:, HEADS:]], axis=0)


def local(
    tokens,
    emb_half,
    norm_gain,
    w_xbc,
    w_z,
    w_dt,
    conv_w,
    conv_bias,
    dt_bias,
    a_log,
    d_skip,
    inner_gain,
    w_out,
    final_gain,
    w_head_half,
    teacher_top,
    teacher_vals,
):
    windows, count = tokens.shape
    nseq = lax.axis_size("seq")
    place = lax.axis_index("seq")
    total = count * nseq
    nblk = total // BLK
    nloc = count // BLK
    streams = 2 * windows
    units = streams * nloc
    tri = (jnp.arange(BLK)[:, None] <= jnp.arange(BLK)[None, :]).astype(jnp.float32)

    flip_d = exchange(emb_half.shape[1])
    emb_flip = jnp.dot(emb_half, flip_d, preferred_element_type=jnp.float32).astype(jnp.bfloat16)
    emb_full = jnp.concatenate([emb_half, emb_flip[1:2], emb_flip[0:1]], axis=0)
    act_tab, z_rows, dt_rows = gram_tables(emb_full, norm_gain, w_xbc, w_z, w_dt, conv_w, conv_bias)
    x_tab = act_tab[:, :INNER].astype(jnp.bfloat16)
    b_tab = act_tab[:, INNER : INNER + NS]
    bc_tab = act_tab[:, INNER:]
    x_heads = x_tab.reshape(GRAMS, HEADS, HD).transpose(1, 0, 2)
    neg_rate = -jnp.exp(a_log)[:, None]

    flip_t = exchange(count)
    rc_tok = (BASES - 1) - jnp.dot(
        tokens.astype(jnp.bfloat16), flip_t, preferred_element_type=jnp.float32
    ).astype(jnp.int32)
    local_tok = jnp.concatenate([tokens, rc_tok], axis=0)
    pos0 = jnp.concatenate(
        [jnp.full((windows, 1), place * count), jnp.full((windows, 1), (nseq - 1 - place) * count)]
    ).astype(jnp.int32)

    seq_tok = gather_all(tokens, rc_tok, "seq")
    ext_all = jnp.concatenate([jnp.zeros((streams, KW - 1), seq_tok.dtype), seq_tok], axis=1)
    gram = gram_ids(ext_all, jnp.broadcast_to(jnp.arange(total, dtype=jnp.int32), (streams, total)))
    local_gram = jnp.concatenate(
        [
            lax.dynamic_slice_in_dim(gram[:windows], place * count, count, axis=1),
            lax.dynamic_slice_in_dim(gram[windows:], (nseq - 1 - place) * count, count, axis=1),
        ],
        axis=0,
    )

    oh_loc = onehot(local_gram, GRAMS)
    x_loc = jnp.einsum("rtg,gc->rtc", oh_loc, x_tab, preferred_element_type=jnp.float32).astype(
        jnp.bfloat16
    )
    bc_loc = jnp.einsum("rtg,gc->rtc", oh_loc, bc_tab, precision=HIGH)
    oh_tok = onehot(local_tok, BASES)
    z_loc = jnp.einsum("rtk,kc->rtc", oh_tok, z_rows, preferred_element_type=jnp.float32)
    dt_loc = jax.nn.softplus(heads_lookup(dt_rows, local_tok) + dt_bias[:, None])
    ld_loc = neg_rate * dt_loc

    def per_unit(values, axis):
        shape = values.shape
        split = shape[:axis] + (nloc, BLK) + shape[axis + 1 :]
        moved = jnp.moveaxis(values.reshape(split), axis, 1)
        return moved.reshape((units,) + moved.shape[2:])

    x_u = per_unit(x_loc, 1).reshape(units, BLK, HEADS, HD)
    b_u = per_unit(bc_loc[..., :NS], 1)
    c_u = per_unit(bc_loc[..., NS:], 1)
    dt_u = per_unit(dt_loc, 2)
    cum_u = block_cumsum(per_unit(ld_loc, 2), tri)

    scores = jnp.einsum("utn,usn->uts", c_u, b_u, precision=lax.Precision.HIGH)
    seg_diff = cum_u[:, :, :, None] - cum_u[:, :, None, :]
    lower = tri.T > 0
    decays = jnp.where(lower, jnp.exp(jnp.where(lower, seg_diff, 0.0)), 0.0)
    weights = (scores[:, None] * decays * dt_u[:, :, None, :]).astype(jnp.bfloat16)
    y_intra = jnp.einsum("uhts,ushp->uthp", weights, x_u, preferred_element_type=jnp.float32)

    if nloc == 1:
        per_gram = needed_per_gram(
            seq_tok, gram, dt_rows, dt_bias, neg_rate, tri, place, windows, nblk
        )
    else:
        dt_all = jax.nn.softplus(heads_lookup(dt_rows, seq_tok) + dt_bias[:, None])
        ld_all = neg_rate * dt_all
        cum = block_cumsum(ld_all.reshape(streams, HEADS, nblk, BLK), tri)
        blk_total = cum[..., -1]
        within = jnp.exp(blk_total[..., None] - cum) * dt_all.reshape(streams, HEADS, nblk, BLK)

        first_blk = (
            jnp.repeat(pos0[:, 0] // BLK, nloc) + jnp.tile(jnp.arange(nloc, dtype=jnp.int32), streams)
        )
        blk_idx = jnp.arange(nblk)
        total_u = jnp.repeat(blk_total, nloc, axis=0)
        between = (blk_idx[:, None] < blk_idx[None, :])[None] & (
            blk_idx[None, None, :] < first_blk[:, None, None]
        )
        span = jnp.sum(jnp.where(between[:, None], total_u[:, :, None, :], 0.0), axis=3)
        across = jnp.where(blk_idx[None, None, :] < first_blk[:, None, None], jnp.exp(span), 0.0)
        weight = jnp.repeat(within, nloc, axis=0) * across[..., None]
        w_hi, w_lo = split_bf16(weight)
        oh_all = jnp.repeat(onehot(gram, GRAMS), nloc, axis=0).reshape(units, nblk, BLK, GRAMS)
        per_gram = jnp.einsum(
            "uhbs,ubsg->uhg",
            jnp.concatenate([w_hi, w_lo], axis=1),
            oh_all,
            preferred_element_type=jnp.float32,
        )
        per_gram = per_gram[:, :HEADS] + per_gram[:, HEADS:]
    b_hi, b_lo = split_bf16(per_gram[..., None] * b_tab[None, None])
    start_state = jnp.einsum("hgp,uhgn->uhpn", x_heads, b_hi, preferred_element_type=jnp.float32)

    y_inter = (
        jnp.einsum("utn,uhpn->uthp", c_u, start_state, precision=lax.Precision.HIGH)
        * jnp.exp(cum_u).transpose(0, 2, 1)[..., None]
    )
    y_u = y_intra + y_inter + d_skip[:, None] * x_u.astype(jnp.float32)
    z_u = per_unit(z_loc, 1).reshape(units, BLK, HEADS, HD)
    gated_y = y_u * jax.nn.silu(z_u)
    normed = rms_gain(gated_y, inner_gain.reshape(HEADS, HD)).astype(jnp.bfloat16)
    normed = jnp.moveaxis(normed.reshape(streams, nloc, BLK, INNER), 1, 1).reshape(
        streams, count, INNER
    )
    outputs = jnp.einsum("gre,ed->grd", normed, w_out, preferred_element_type=jnp.float32).astype(
        jnp.bfloat16
    )

    embedded = jnp.einsum(
        "grk,kd->grd", oh_tok[:windows], emb_full, preferred_element_type=jnp.float32
    ).astype(jnp.bfloat16)
    returned = outputs[windows:, ::-1, ::-1]
    hidden_out = (
        embedded.astype(jnp.float32)
        + outputs[:windows].astype(jnp.float32)
        + returned.astype(jnp.float32)
    ).astype(jnp.bfloat16)
    final_normed = rms_gain(hidden_out.astype(jnp.float32), final_gain).astype(jnp.bfloat16)
    head_flip = jnp.dot(flip_d, w_head_half, preferred_element_type=jnp.float32).astype(
        jnp.bfloat16
    )
    head_full = jnp.concatenate([w_head_half, head_flip[:, 1:2], head_flip[:, 0:1]], axis=1)
    logits = jnp.einsum("grd,db->grb", final_normed, head_full, preferred_element_type=jnp.float32)
    log_q = logits - jnp.log(jnp.sum(jnp.exp(logits), axis=-1, keepdims=True))
    top_value = jnp.max(teacher_vals, axis=1, keepdims=True)
    shifted = teacher_vals - top_value
    log_p = shifted - jnp.log(jnp.sum(jnp.exp(shifted), axis=1, keepdims=True))
    matches = teacher_top[..., None] == jnp.arange(4, dtype=jnp.int32)
    picked = jnp.sum(jnp.where(matches, log_q[:, None, :, :], 0.0), axis=-1)
    divergence = jnp.sum(jnp.exp(log_p) * (log_p - picked), axis=1)
    return (hidden_out, divergence)


def solution(mesh):
    placed = (
        P("grp", "seq"),
        P(),
        P(),
        P(),
        P(),
        P(),
        P(),
        P(),
        P(),
        P(),
        P(),
        P(),
        P(),
        P(),
        P(),
        P("grp", None, "seq"),
        P("grp", None, "seq"),
    )
    return jax.shard_map(
        local,
        mesh=mesh,
        in_specs=placed,
        out_specs=(P("grp", "seq", None), P("grp", "seq")),
        check_vma=False,
    )
```

```python
import jax
import jax.numpy as jnp
import numpy as np
from jax import lax
from jax.sharding import PartitionSpec as P

INNER = 1024
HD = 64
NS = 64
KW = 4
BLK = 128
HEADS = 16
CONVW = 1152
BASES = 4
GRAMS = 344


EPS = 1e-05
HIGH = lax.Precision.HIGHEST


def rms_gain(values, gain_row):
    return values * lax.rsqrt(jnp.mean(values * values, axis=-1, keepdims=True) + EPS) * gain_row


def to_blocks(values, block_width):
    streams, count = (values.shape[0], values.shape[1])
    return jnp.moveaxis(
        values.reshape((streams, count // block_width, block_width) + values.shape[2:]), 1, 0
    )


def ssd_block(carry_state, block_in):
    x_blk, b_blk, c_blk, decay_blk, dt_blk = block_in
    cumulated = jnp.cumsum(decay_blk, axis=2)
    block_len = decay_blk.shape[2]
    scores = jnp.einsum("gtn,gsn->gts", c_blk, b_blk, precision=HIGH)
    seg_diff = cumulated[:, :, :, None] - cumulated[:, :, None, :]
    lower_mask = jnp.arange(block_len)[:, None] >= jnp.arange(block_len)[None, :]
    decays = jnp.where(lower_mask, jnp.exp(jnp.where(lower_mask, seg_diff, 0.0)), 0.0)
    weights = (scores[:, None] * decays * dt_blk[:, :, None, :]).astype(jnp.bfloat16)
    y_intra = jnp.einsum("ghts,gshp->gthp", weights, x_blk, preferred_element_type=jnp.float32)
    y_inter = (
        jnp.einsum("gtn,ghpn->gthp", c_blk, carry_state, precision=HIGH)
        * jnp.swapaxes(jnp.exp(cumulated), 1, 2)[..., None]
    )
    last_cum = cumulated[:, :, -1:]
    scaled = jnp.exp(last_cum - cumulated) * dt_blk
    x_weighted = x_blk.astype(jnp.float32) * jnp.swapaxes(scaled, 1, 2)[..., None]
    new_state = jnp.exp(last_cum)[..., None] * carry_state + jnp.einsum(
        "gshp,gsn->ghpn", x_weighted, b_blk, precision=HIGH
    )
    return (new_state, y_intra + y_inter)


def gram_layout():
    rows = []
    for real in range(1, KW + 1):
        for code in range(BASES**real):
            taps = [None] * (KW - real) + [
                (code // BASES ** (real - 1 - k)) % BASES for k in range(real)
            ]
            rows.append(taps)
    picks = np.zeros((GRAMS, KW * BASES), np.float32)
    for row, taps in enumerate(rows):
        for offset, base in enumerate(taps):
            if base is not None:
                picks[row, offset * BASES + base] = 1.0
    return picks


def gram_tables(emb_full, norm_gain, w_xbc, w_z, w_dt, conv_w, conv_bias):
    row_norm = rms_gain(emb_full.astype(jnp.float32), norm_gain).astype(jnp.bfloat16)
    xbc_rows = jnp.dot(row_norm, w_xbc, preferred_element_type=jnp.float32).astype(jnp.bfloat16)
    z_rows = jnp.dot(row_norm, w_z, preferred_element_type=jnp.float32).astype(jnp.bfloat16)
    dt_rows = jnp.dot(row_norm, w_dt, preferred_element_type=jnp.float32)
    taps = (conv_w[:, None, :] * xbc_rows.astype(jnp.float32)[None]).reshape(KW * BASES, CONVW)
    conv_sum = conv_bias + jnp.dot(jnp.asarray(gram_layout()), taps, precision=HIGH)
    return jax.nn.silu(conv_sum), z_rows, dt_rows


def gram_ids(ext, where_in):
    count = where_in.shape[1]
    code = jnp.zeros_like(where_in)
    ids = jnp.zeros_like(where_in)
    offset_of = 0
    for real in range(1, KW + 1):
        code = code + ext[:, KW - real : KW - real + count] * BASES ** (real - 1)
        chosen = (where_in >= real - 1) if real == KW else (where_in == real - 1)
        ids = jnp.where(chosen, offset_of + code, ids)
        offset_of += BASES**real
    return ids


def gather_all(fwd, rc, axis):
    count = lax.axis_size(axis)
    place = lax.axis_index(axis)
    rows = fwd.shape[0]
    held = jnp.concatenate([fwd, rc], axis=0)
    bit = 0
    while 2**bit < count:
        mask = 2**bit
        other = lax.ppermute(held, axis, [(src, src ^ mask) for src in range(count)])
        upper = (place // mask) % 2 == 1
        low_first = jnp.concatenate([held, other], axis=1)
        high_first = jnp.concatenate([other, held], axis=1)
        held = jnp.concatenate(
            [
                jnp.where(upper, high_first[:rows], low_first[:rows]),
                jnp.where(upper, low_first[rows:], high_first[rows:]),
            ],
            axis=0,
        )
        bit += 1
    return held


def heads_lookup(rows, bases):
    picked = jnp.zeros(bases.shape[:-1] + (rows.shape[1], bases.shape[-1]), jnp.float32)
    for base in range(BASES):
        picked = picked + jnp.where(
            (bases == base)[..., None, :], rows[base][:, None], 0.0
        )
    return picked


def onehot(ids, size):
    return (ids[..., None] == jnp.arange(size, dtype=ids.dtype)).astype(jnp.bfloat16)


def exchange(size):
    rows = lax.broadcasted_iota(jnp.int32, (size, size), 0)
    cols = lax.broadcasted_iota(jnp.int32, (size, size), 1)
    return (rows + cols == size - 1).astype(jnp.bfloat16)


def split_bf16(values):
    high = values.astype(jnp.bfloat16)
    return high, (values - high.astype(jnp.float32)).astype(jnp.bfloat16)


def block_cumsum(values, tri):
    return jnp.einsum("...s,st->...t", values, tri, precision=HIGH)


def needed_per_gram(seq_tok, gram, dt_rows, dt_bias, neg_rate, tri, place, windows, nblk):
    need = nblk - 1

    def arranged(values):
        fwd = values[:windows].reshape(windows, nblk, BLK)
        rc = values[windows:].reshape(windows, nblk, BLK)[:, ::-1]
        joined = jnp.concatenate([rc, fwd], axis=1)
        return lax.dynamic_slice_in_dim(joined, place + 1, need, axis=1)

    tok_n = arranged(seq_tok)
    gram_n = arranged(gram)
    dt_n = jax.nn.softplus(
        heads_lookup(dt_rows, tok_n.reshape(windows, need * BLK)) + dt_bias[:, None]
    ).reshape(windows, HEADS, need, BLK)
    cum = block_cumsum(neg_rate[:, :, None] * dt_n, tri)
    blk_total = cum[..., -1]
    within = jnp.exp(blk_total[..., None] - cum) * dt_n
    idx = jnp.arange(need)
    is_fwd = idx >= (nblk - 1 - place)
    pick = jnp.where(is_fwd[:, None], idx[None, :] > idx[:, None], idx[None, :] < idx[:, None])
    span = jnp.sum(jnp.where(pick[None, None], blk_total[:, :, None, :], 0.0), axis=3)
    weight = within * jnp.exp(span)[..., None]
    fwd_part = is_fwd[None, None, :, None]
    w_hi, w_lo = split_bf16(
        jnp.concatenate(
            [jnp.where(fwd_part, weight, 0.0), jnp.where(fwd_part, 0.0, weight)], axis=1
        )
    )
    summed = jnp.einsum(
        "whbs,wbsg->whg",
        jnp.concatenate([w_hi, w_lo], axis=1),
        onehot(gram_n, GRAMS),
        preferred_element_type=jnp.float32,
    )
    summed = summed[:, : 2 * HEADS] + summed[:, 2 * HEADS :]
    return jnp.concatenate([summed[:, :HEADS], summed[:, HEADS:]], axis=0)


def local(
    tokens,
    emb_half,
    norm_gain,
    w_xbc,
    w_z,
    w_dt,
    conv_w,
    conv_bias,
    dt_bias,
    a_log,
    d_skip,
    inner_gain,
    w_out,
    final_gain,
    w_head_half,
    teacher_top,
    teacher_vals,
):
    windows, count = tokens.shape
    nseq = lax.axis_size("seq")
    place = lax.axis_index("seq")
    total = count * nseq
    nblk = total // BLK
    nloc = count // BLK
    streams = 2 * windows
    units = streams * nloc
    tri = (jnp.arange(BLK)[:, None] <= jnp.arange(BLK)[None, :]).astype(jnp.float32)

    flip_d = exchange(emb_half.shape[1])
    emb_flip = jnp.dot(emb_half, flip_d, preferred_element_type=jnp.float32).astype(jnp.bfloat16)
    emb_full = jnp.concatenate([emb_half, emb_flip[1:2], emb_flip[0:1]], axis=0)
    act_tab, z_rows, dt_rows = gram_tables(emb_full, norm_gain, w_xbc, w_z, w_dt, conv_w, conv_bias)
    x_tab = act_tab[:, :INNER].astype(jnp.bfloat16)
    b_tab = act_tab[:, INNER : INNER + NS]
    bc_tab = act_tab[:, INNER:]
    x_heads = x_tab.reshape(GRAMS, HEADS, HD).transpose(1, 0, 2)
    neg_rate = -jnp.exp(a_log)[:, None]

    flip_t = exchange(count)
    rc_tok = (BASES - 1) - jnp.dot(
        tokens.astype(jnp.bfloat16), flip_t, preferred_element_type=jnp.float32
    ).astype(jnp.int32)
    local_tok = jnp.concatenate([tokens, rc_tok], axis=0)
    pos0 = jnp.concatenate(
        [jnp.full((windows, 1), place * count), jnp.full((windows, 1), (nseq - 1 - place) * count)]
    ).astype(jnp.int32)

    seq_tok = gather_all(tokens, rc_tok, "seq")
    ext_all = jnp.concatenate([jnp.zeros((streams, KW - 1), seq_tok.dtype), seq_tok], axis=1)
    gram = gram_ids(ext_all, jnp.broadcast_to(jnp.arange(total, dtype=jnp.int32), (streams, total)))
    local_gram = jnp.concatenate(
        [
            lax.dynamic_slice_in_dim(gram[:windows], place * count, count, axis=1),
            lax.dynamic_slice_in_dim(gram[windows:], (nseq - 1 - place) * count, count, axis=1),
        ],
        axis=0,
    )

    oh_loc = onehot(local_gram, GRAMS)
    x_loc = jnp.einsum("rtg,gc->rtc", oh_loc, x_tab, preferred_element_type=jnp.float32).astype(
        jnp.bfloat16
    )
    bc_loc = jnp.einsum("rtg,gc->rtc", oh_loc, bc_tab, precision=HIGH)
    oh_tok = onehot(local_tok, BASES)
    z_loc = jnp.einsum("rtk,kc->rtc", oh_tok, z_rows, preferred_element_type=jnp.float32).astype(
        jnp.bfloat16
    )
    dt_loc = jax.nn.softplus(heads_lookup(dt_rows, local_tok) + dt_bias[:, None])
    ld_loc = neg_rate * dt_loc

    def per_unit(values, axis):
        shape = values.shape
        split = shape[:axis] + (nloc, BLK) + shape[axis + 1 :]
        moved = jnp.moveaxis(values.reshape(split), axis, 1)
        return moved.reshape((units,) + moved.shape[2:])

    x_u = per_unit(x_loc, 1).reshape(units, BLK, HEADS, HD)
    b_u = per_unit(bc_loc[..., :NS], 1)
    c_u = per_unit(bc_loc[..., NS:], 1)
    dt_u = per_unit(dt_loc, 2)
    cum_u = block_cumsum(per_unit(ld_loc, 2), tri)

    scores = jnp.einsum("utn,usn->uts", c_u, b_u, precision=lax.Precision.HIGH)
    seg_diff = cum_u[:, :, :, None] - cum_u[:, :, None, :]
    lower = tri.T > 0
    decays = jnp.where(lower, jnp.exp(jnp.where(lower, seg_diff, 0.0)), 0.0)
    weights = (scores[:, None] * decays * dt_u[:, :, None, :]).astype(jnp.bfloat16)
    y_intra = jnp.einsum("uhts,ushp->uthp", weights, x_u, preferred_element_type=jnp.float32)

    if nloc == 1:
        per_gram = needed_per_gram(
            seq_tok, gram, dt_rows, dt_bias, neg_rate, tri, place, windows, nblk
        )
    else:
        dt_all = jax.nn.softplus(heads_lookup(dt_rows, seq_tok) + dt_bias[:, None])
        ld_all = neg_rate * dt_all
        cum = block_cumsum(ld_all.reshape(streams, HEADS, nblk, BLK), tri)
        blk_total = cum[..., -1]
        within = jnp.exp(blk_total[..., None] - cum) * dt_all.reshape(streams, HEADS, nblk, BLK)

        first_blk = (
            jnp.repeat(pos0[:, 0] // BLK, nloc) + jnp.tile(jnp.arange(nloc, dtype=jnp.int32), streams)
        )
        blk_idx = jnp.arange(nblk)
        total_u = jnp.repeat(blk_total, nloc, axis=0)
        between = (blk_idx[:, None] < blk_idx[None, :])[None] & (
            blk_idx[None, None, :] < first_blk[:, None, None]
        )
        span = jnp.sum(jnp.where(between[:, None], total_u[:, :, None, :], 0.0), axis=3)
        across = jnp.where(blk_idx[None, None, :] < first_blk[:, None, None], jnp.exp(span), 0.0)
        weight = jnp.repeat(within, nloc, axis=0) * across[..., None]
        w_hi, w_lo = split_bf16(weight)
        oh_all = jnp.repeat(onehot(gram, GRAMS), nloc, axis=0).reshape(units, nblk, BLK, GRAMS)
        per_gram = jnp.einsum(
            "uhbs,ubsg->uhg",
            jnp.concatenate([w_hi, w_lo], axis=1),
            oh_all,
            preferred_element_type=jnp.float32,
        )
        per_gram = per_gram[:, :HEADS] + per_gram[:, HEADS:]
    b_hi, b_lo = split_bf16(per_gram[..., None] * b_tab[None, None])
    start_state = jnp.einsum("hgp,uhgn->uhpn", x_heads, b_hi, preferred_element_type=jnp.float32)

    y_inter = (
        jnp.einsum("utn,uhpn->uthp", c_u, start_state, precision=lax.Precision.HIGH)
        * jnp.exp(cum_u).transpose(0, 2, 1)[..., None]
    )
    y_u = y_intra + y_inter + d_skip[:, None] * x_u.astype(jnp.float32)
    z_u = per_unit(z_loc, 1).reshape(units, BLK, HEADS, HD)
    gated_y = y_u * jax.nn.silu(z_u.astype(jnp.float32))
    normed = rms_gain(gated_y, inner_gain.reshape(HEADS, HD)).astype(jnp.bfloat16)
    normed = jnp.moveaxis(normed.reshape(streams, nloc, BLK, INNER), 1, 1).reshape(
        streams, count, INNER
    )
    outputs = jnp.einsum("gre,ed->grd", normed, w_out, preferred_element_type=jnp.float32).astype(
        jnp.bfloat16
    )

    embedded = jnp.einsum(
        "grk,kd->grd", oh_tok[:windows], emb_full, preferred_element_type=jnp.float32
    ).astype(jnp.bfloat16)
    returned = outputs[windows:, ::-1, ::-1]
    hidden_out = (
        embedded.astype(jnp.float32)
        + outputs[:windows].astype(jnp.float32)
        + returned.astype(jnp.float32)
    ).astype(jnp.bfloat16)
    final_normed = rms_gain(hidden_out.astype(jnp.float32), final_gain).astype(jnp.bfloat16)
    head_flip = jnp.dot(flip_d, w_head_half, preferred_element_type=jnp.float32).astype(
        jnp.bfloat16
    )
    head_full = jnp.concatenate([w_head_half, head_flip[:, 1:2], head_flip[:, 0:1]], axis=1)
    logits = jnp.einsum("grd,db->grb", final_normed, head_full, preferred_element_type=jnp.float32)
    log_q = logits - jnp.log(jnp.sum(jnp.exp(logits), axis=-1, keepdims=True))
    top_value = jnp.max(teacher_vals, axis=1, keepdims=True)
    shifted = teacher_vals - top_value
    log_p = shifted - jnp.log(jnp.sum(jnp.exp(shifted), axis=1, keepdims=True))
    matches = teacher_top[..., None] == jnp.arange(4, dtype=jnp.int32)
    picked = jnp.sum(jnp.where(matches, log_q[:, None, :, :], 0.0), axis=-1)
    divergence = jnp.sum(jnp.exp(log_p) * (log_p - picked), axis=1)
    return (hidden_out, divergence)


def solution(mesh):
    placed = (
        P("grp", "seq"),
        P(),
        P(),
        P(),
        P(),
        P(),
        P(),
        P(),
        P(),
        P(),
        P(),
        P(),
        P(),
        P(),
        P(),
        P("grp", None, "seq"),
        P("grp", None, "seq"),
    )
    return jax.shard_map(
        local,
        mesh=mesh,
        in_specs=placed,
        out_specs=(P("grp", "seq", None), P("grp", "seq")),
        check_vma=False,
    )
```

```python
import jax
import jax.numpy as jnp
import numpy as np
from jax import lax
from jax.sharding import PartitionSpec as P

INNER = 1024
HD = 64
NS = 64
KW = 4
BLK = 128
HEADS = 16
CONVW = 1152
BASES = 4
GRAMS = 344


EPS = 1e-05
HIGH = lax.Precision.HIGHEST


def rms_gain(values, gain_row):
    return values * lax.rsqrt(jnp.mean(values * values, axis=-1, keepdims=True) + EPS) * gain_row


def to_blocks(values, block_width):
    streams, count = (values.shape[0], values.shape[1])
    return jnp.moveaxis(
        values.reshape((streams, count // block_width, block_width) + values.shape[2:]), 1, 0
    )


def ssd_block(carry_state, block_in):
    x_blk, b_blk, c_blk, decay_blk, dt_blk = block_in
    cumulated = jnp.cumsum(decay_blk, axis=2)
    block_len = decay_blk.shape[2]
    scores = jnp.einsum("gtn,gsn->gts", c_blk, b_blk, precision=HIGH)
    seg_diff = cumulated[:, :, :, None] - cumulated[:, :, None, :]
    lower_mask = jnp.arange(block_len)[:, None] >= jnp.arange(block_len)[None, :]
    decays = jnp.where(lower_mask, jnp.exp(jnp.where(lower_mask, seg_diff, 0.0)), 0.0)
    weights = (scores[:, None] * decays * dt_blk[:, :, None, :]).astype(jnp.bfloat16)
    y_intra = jnp.einsum("ghts,gshp->gthp", weights, x_blk, preferred_element_type=jnp.float32)
    y_inter = (
        jnp.einsum("gtn,ghpn->gthp", c_blk, carry_state, precision=HIGH)
        * jnp.swapaxes(jnp.exp(cumulated), 1, 2)[..., None]
    )
    last_cum = cumulated[:, :, -1:]
    scaled = jnp.exp(last_cum - cumulated) * dt_blk
    x_weighted = x_blk.astype(jnp.float32) * jnp.swapaxes(scaled, 1, 2)[..., None]
    new_state = jnp.exp(last_cum)[..., None] * carry_state + jnp.einsum(
        "gshp,gsn->ghpn", x_weighted, b_blk, precision=HIGH
    )
    return (new_state, y_intra + y_inter)


def gram_layout():
    rows = []
    for real in range(1, KW + 1):
        for code in range(BASES**real):
            taps = [None] * (KW - real) + [
                (code // BASES ** (real - 1 - k)) % BASES for k in range(real)
            ]
            rows.append(taps)
    picks = np.zeros((GRAMS, KW * BASES), np.float32)
    for row, taps in enumerate(rows):
        for offset, base in enumerate(taps):
            if base is not None:
                picks[row, offset * BASES + base] = 1.0
    return picks


def gram_tables(emb_full, norm_gain, w_xbc, w_z, w_dt, conv_w, conv_bias):
    row_norm = rms_gain(emb_full.astype(jnp.float32), norm_gain).astype(jnp.bfloat16)
    xbc_rows = jnp.dot(row_norm, w_xbc, preferred_element_type=jnp.float32).astype(jnp.bfloat16)
    z_rows = jnp.dot(row_norm, w_z, preferred_element_type=jnp.float32).astype(jnp.bfloat16)
    dt_rows = jnp.dot(row_norm, w_dt, preferred_element_type=jnp.float32)
    taps = (conv_w[:, None, :] * xbc_rows.astype(jnp.float32)[None]).reshape(KW * BASES, CONVW)
    conv_sum = conv_bias[:, None] + jnp.dot(taps.T, jnp.asarray(gram_layout().T), precision=HIGH)
    return jax.nn.silu(conv_sum), z_rows, dt_rows


def gram_ids(ext, where_in):
    count = where_in.shape[1]
    code = jnp.zeros_like(where_in)
    ids = jnp.zeros_like(where_in)
    offset_of = 0
    for real in range(1, KW + 1):
        code = code + ext[:, KW - real : KW - real + count] * BASES ** (real - 1)
        chosen = (where_in >= real - 1) if real == KW else (where_in == real - 1)
        ids = jnp.where(chosen, offset_of + code, ids)
        offset_of += BASES**real
    return ids


def gather_all(fwd, rc, axis):
    count = lax.axis_size(axis)
    place = lax.axis_index(axis)
    rows = fwd.shape[0]
    held = jnp.concatenate([fwd, rc], axis=0)
    bit = 0
    while 2**bit < count:
        mask = 2**bit
        other = lax.ppermute(held, axis, [(src, src ^ mask) for src in range(count)])
        upper = (place // mask) % 2 == 1
        low_first = jnp.concatenate([held, other], axis=1)
        high_first = jnp.concatenate([other, held], axis=1)
        held = jnp.concatenate(
            [
                jnp.where(upper, high_first[:rows], low_first[:rows]),
                jnp.where(upper, low_first[rows:], high_first[rows:]),
            ],
            axis=0,
        )
        bit += 1
    return held


def heads_lookup(rows, bases):
    picked = jnp.zeros(bases.shape[:-1] + (rows.shape[1], bases.shape[-1]), jnp.float32)
    for base in range(BASES):
        picked = picked + jnp.where(
            (bases == base)[..., None, :], rows[base][:, None], 0.0
        )
    return picked


def onehot(ids, size):
    return (ids[..., None] == jnp.arange(size, dtype=ids.dtype)).astype(jnp.bfloat16)


def exchange(size):
    rows = lax.broadcasted_iota(jnp.int32, (size, size), 0)
    cols = lax.broadcasted_iota(jnp.int32, (size, size), 1)
    return (rows + cols == size - 1).astype(jnp.bfloat16)


def split_bf16(values):
    high = values.astype(jnp.bfloat16)
    return high, (values - high.astype(jnp.float32)).astype(jnp.bfloat16)


def block_cumsum(values, tri):
    return jnp.einsum("...s,st->...t", values, tri, precision=HIGH)


def needed_per_gram(seq_tok, gram, dt_rows, dt_bias, neg_rate, tri, place, windows, nblk):
    need = nblk - 1

    def arranged(values):
        fwd = values[:windows].reshape(windows, nblk, BLK)
        rc = values[windows:].reshape(windows, nblk, BLK)[:, ::-1]
        joined = jnp.concatenate([rc, fwd], axis=1)
        return lax.dynamic_slice_in_dim(joined, place + 1, need, axis=1)

    tok_n = arranged(seq_tok)
    gram_n = arranged(gram)
    dt_n = jax.nn.softplus(
        heads_lookup(dt_rows, tok_n.reshape(windows, need * BLK)) + dt_bias[:, None]
    ).reshape(windows, HEADS, need, BLK)
    cum = block_cumsum(neg_rate[:, :, None] * dt_n, tri)
    blk_total = cum[..., -1]
    within = jnp.exp(blk_total[..., None] - cum) * dt_n
    idx = jnp.arange(need)
    is_fwd = idx >= (nblk - 1 - place)
    pick = jnp.where(is_fwd[:, None], idx[None, :] > idx[:, None], idx[None, :] < idx[:, None])
    span = jnp.sum(jnp.where(pick[None, None], blk_total[:, :, None, :], 0.0), axis=3)
    weight = within * jnp.exp(span)[..., None]
    fwd_part = is_fwd[None, None, :, None]
    w_hi, w_lo = split_bf16(
        jnp.concatenate(
            [jnp.where(fwd_part, weight, 0.0), jnp.where(fwd_part, 0.0, weight)], axis=1
        )
    )
    summed = jnp.einsum(
        "whbs,wbsg->whg",
        jnp.concatenate([w_hi, w_lo], axis=1),
        onehot(gram_n, GRAMS),
        preferred_element_type=jnp.float32,
    )
    summed = summed[:, : 2 * HEADS] + summed[:, 2 * HEADS :]
    return jnp.concatenate([summed[:, :HEADS], summed[:, HEADS:]], axis=0)


def local(
    tokens,
    emb_half,
    norm_gain,
    w_xbc,
    w_z,
    w_dt,
    conv_w,
    conv_bias,
    dt_bias,
    a_log,
    d_skip,
    inner_gain,
    w_out,
    final_gain,
    w_head_half,
    teacher_top,
    teacher_vals,
):
    windows, count = tokens.shape
    nseq = lax.axis_size("seq")
    place = lax.axis_index("seq")
    total = count * nseq
    nblk = total // BLK
    nloc = count // BLK
    streams = 2 * windows
    units = streams * nloc
    tri = (jnp.arange(BLK)[:, None] <= jnp.arange(BLK)[None, :]).astype(jnp.float32)

    flip_d = exchange(emb_half.shape[1])
    emb_flip = jnp.dot(emb_half, flip_d, preferred_element_type=jnp.float32).astype(jnp.bfloat16)
    emb_full = jnp.concatenate([emb_half, emb_flip[1:2], emb_flip[0:1]], axis=0)
    act_tab, z_rows, dt_rows = gram_tables(emb_full, norm_gain, w_xbc, w_z, w_dt, conv_w, conv_bias)
    x_tab = act_tab[:INNER].astype(jnp.bfloat16)
    b_tab = act_tab[INNER : INNER + NS]
    bc_tab = act_tab[INNER:]
    x_heads = x_tab.reshape(HEADS, HD, GRAMS)
    neg_rate = -jnp.exp(a_log)[:, None]

    flip_t = exchange(count)
    rc_tok = (BASES - 1) - jnp.dot(
        tokens.astype(jnp.bfloat16), flip_t, preferred_element_type=jnp.float32
    ).astype(jnp.int32)
    local_tok = jnp.concatenate([tokens, rc_tok], axis=0)
    pos0 = jnp.concatenate(
        [jnp.full((windows, 1), place * count), jnp.full((windows, 1), (nseq - 1 - place) * count)]
    ).astype(jnp.int32)

    seq_tok = gather_all(tokens, rc_tok, "seq")
    ext_all = jnp.concatenate([jnp.zeros((streams, KW - 1), seq_tok.dtype), seq_tok], axis=1)
    gram = gram_ids(ext_all, jnp.broadcast_to(jnp.arange(total, dtype=jnp.int32), (streams, total)))
    local_gram = jnp.concatenate(
        [
            lax.dynamic_slice_in_dim(gram[:windows], place * count, count, axis=1),
            lax.dynamic_slice_in_dim(gram[windows:], (nseq - 1 - place) * count, count, axis=1),
        ],
        axis=0,
    )

    oh_loc = onehot(local_gram, GRAMS)
    x_loc = jnp.einsum("rtg,cg->rtc", oh_loc, x_tab, preferred_element_type=jnp.float32).astype(
        jnp.bfloat16
    )
    bc_loc = jnp.einsum("rtg,cg->rtc", oh_loc, bc_tab, precision=HIGH)
    oh_tok = onehot(local_tok, BASES)
    z_loc = jnp.einsum("rtk,kc->rtc", oh_tok, z_rows, preferred_element_type=jnp.float32)
    dt_loc = jax.nn.softplus(heads_lookup(dt_rows, local_tok) + dt_bias[:, None])
    ld_loc = neg_rate * dt_loc

    def per_unit(values, axis):
        shape = values.shape
        split = shape[:axis] + (nloc, BLK) + shape[axis + 1 :]
        moved = jnp.moveaxis(values.reshape(split), axis, 1)
        return moved.reshape((units,) + moved.shape[2:])

    x_u = per_unit(x_loc, 1).reshape(units, BLK, HEADS, HD)
    b_u = per_unit(bc_loc[..., :NS], 1)
    c_u = per_unit(bc_loc[..., NS:], 1)
    dt_u = per_unit(dt_loc, 2)
    cum_u = block_cumsum(per_unit(ld_loc, 2), tri)

    scores = jnp.einsum("utn,usn->uts", c_u, b_u, precision=lax.Precision.HIGH)
    seg_diff = cum_u[:, :, :, None] - cum_u[:, :, None, :]
    lower = tri.T > 0
    decays = jnp.where(lower, jnp.exp(jnp.where(lower, seg_diff, 0.0)), 0.0)
    weights = (scores[:, None] * decays * dt_u[:, :, None, :]).astype(jnp.bfloat16)
    y_intra = jnp.einsum("uhts,ushp->uthp", weights, x_u, preferred_element_type=jnp.float32)

    if nloc == 1:
        per_gram = needed_per_gram(
            seq_tok, gram, dt_rows, dt_bias, neg_rate, tri, place, windows, nblk
        )
    else:
        dt_all = jax.nn.softplus(heads_lookup(dt_rows, seq_tok) + dt_bias[:, None])
        ld_all = neg_rate * dt_all
        cum = block_cumsum(ld_all.reshape(streams, HEADS, nblk, BLK), tri)
        blk_total = cum[..., -1]
        within = jnp.exp(blk_total[..., None] - cum) * dt_all.reshape(streams, HEADS, nblk, BLK)

        first_blk = (
            jnp.repeat(pos0[:, 0] // BLK, nloc) + jnp.tile(jnp.arange(nloc, dtype=jnp.int32), streams)
        )
        blk_idx = jnp.arange(nblk)
        total_u = jnp.repeat(blk_total, nloc, axis=0)
        between = (blk_idx[:, None] < blk_idx[None, :])[None] & (
            blk_idx[None, None, :] < first_blk[:, None, None]
        )
        span = jnp.sum(jnp.where(between[:, None], total_u[:, :, None, :], 0.0), axis=3)
        across = jnp.where(blk_idx[None, None, :] < first_blk[:, None, None], jnp.exp(span), 0.0)
        weight = jnp.repeat(within, nloc, axis=0) * across[..., None]
        w_hi, w_lo = split_bf16(weight)
        oh_all = jnp.repeat(onehot(gram, GRAMS), nloc, axis=0).reshape(units, nblk, BLK, GRAMS)
        per_gram = jnp.einsum(
            "uhbs,ubsg->uhg",
            jnp.concatenate([w_hi, w_lo], axis=1),
            oh_all,
            preferred_element_type=jnp.float32,
        )
        per_gram = per_gram[:, :HEADS] + per_gram[:, HEADS:]
    b_hi, b_lo = split_bf16(per_gram[:, :, None, :] * b_tab[None, None])
    start_state = jnp.einsum("hpg,uhng->uhpn", x_heads, b_hi, preferred_element_type=jnp.float32)

    y_inter = (
        jnp.einsum("utn,uhpn->uthp", c_u, start_state, precision=lax.Precision.HIGH)
        * jnp.exp(cum_u).transpose(0, 2, 1)[..., None]
    )
    y_u = y_intra + y_inter + d_skip[:, None] * x_u.astype(jnp.float32)
    z_u = per_unit(z_loc, 1).reshape(units, BLK, HEADS, HD)
    gated_y = y_u * jax.nn.silu(z_u)
    normed = rms_gain(gated_y, inner_gain.reshape(HEADS, HD)).astype(jnp.bfloat16)
    normed = jnp.moveaxis(normed.reshape(streams, nloc, BLK, INNER), 1, 1).reshape(
        streams, count, INNER
    )
    outputs = jnp.einsum("gre,ed->grd", normed, w_out, preferred_element_type=jnp.float32).astype(
        jnp.bfloat16
    )

    embedded = jnp.einsum(
        "grk,kd->grd", oh_tok[:windows], emb_full, preferred_element_type=jnp.float32
    ).astype(jnp.bfloat16)
    returned = outputs[windows:, ::-1, ::-1]
    hidden_out = (
        embedded.astype(jnp.float32)
        + outputs[:windows].astype(jnp.float32)
        + returned.astype(jnp.float32)
    ).astype(jnp.bfloat16)
    final_normed = rms_gain(hidden_out.astype(jnp.float32), final_gain).astype(jnp.bfloat16)
    head_flip = jnp.dot(flip_d, w_head_half, preferred_element_type=jnp.float32).astype(
        jnp.bfloat16
    )
    head_full = jnp.concatenate([w_head_half, head_flip[:, 1:2], head_flip[:, 0:1]], axis=1)
    logits = jnp.einsum("grd,db->grb", final_normed, head_full, preferred_element_type=jnp.float32)
    log_q = logits - jnp.log(jnp.sum(jnp.exp(logits), axis=-1, keepdims=True))
    top_value = jnp.max(teacher_vals, axis=1, keepdims=True)
    shifted = teacher_vals - top_value
    log_p = shifted - jnp.log(jnp.sum(jnp.exp(shifted), axis=1, keepdims=True))
    matches = teacher_top[..., None] == jnp.arange(4, dtype=jnp.int32)
    picked = jnp.sum(jnp.where(matches, log_q[:, None, :, :], 0.0), axis=-1)
    divergence = jnp.sum(jnp.exp(log_p) * (log_p - picked), axis=1)
    return (hidden_out, divergence)


def solution(mesh):
    placed = (
        P("grp", "seq"),
        P(),
        P(),
        P(),
        P(),
        P(),
        P(),
        P(),
        P(),
        P(),
        P(),
        P(),
        P(),
        P(),
        P(),
        P("grp", None, "seq"),
        P("grp", None, "seq"),
    )
    return jax.shard_map(
        local,
        mesh=mesh,
        in_specs=placed,
        out_specs=(P("grp", "seq", None), P("grp", "seq")),
        check_vma=False,
    )
```

```python
import jax
import jax.numpy as jnp
import numpy as np
from jax import lax
from jax.sharding import PartitionSpec as P

INNER = 1024
HD = 64
NS = 64
KW = 4
BLK = 128
HEADS = 16
CONVW = 1152
BASES = 4
GRAMS = 344


EPS = 1e-05
HIGH = lax.Precision.HIGHEST


def rms_gain(values, gain_row):
    return values * lax.rsqrt(jnp.mean(values * values, axis=-1, keepdims=True) + EPS) * gain_row


def to_blocks(values, block_width):
    streams, count = (values.shape[0], values.shape[1])
    return jnp.moveaxis(
        values.reshape((streams, count // block_width, block_width) + values.shape[2:]), 1, 0
    )


def ssd_block(carry_state, block_in):
    x_blk, b_blk, c_blk, decay_blk, dt_blk = block_in
    cumulated = jnp.cumsum(decay_blk, axis=2)
    block_len = decay_blk.shape[2]
    scores = jnp.einsum("gtn,gsn->gts", c_blk, b_blk, precision=HIGH)
    seg_diff = cumulated[:, :, :, None] - cumulated[:, :, None, :]
    lower_mask = jnp.arange(block_len)[:, None] >= jnp.arange(block_len)[None, :]
    decays = jnp.where(lower_mask, jnp.exp(jnp.where(lower_mask, seg_diff, 0.0)), 0.0)
    weights = (scores[:, None] * decays * dt_blk[:, :, None, :]).astype(jnp.bfloat16)
    y_intra = jnp.einsum("ghts,gshp->gthp", weights, x_blk, preferred_element_type=jnp.float32)
    y_inter = (
        jnp.einsum("gtn,ghpn->gthp", c_blk, carry_state, precision=HIGH)
        * jnp.swapaxes(jnp.exp(cumulated), 1, 2)[..., None]
    )
    last_cum = cumulated[:, :, -1:]
    scaled = jnp.exp(last_cum - cumulated) * dt_blk
    x_weighted = x_blk.astype(jnp.float32) * jnp.swapaxes(scaled, 1, 2)[..., None]
    new_state = jnp.exp(last_cum)[..., None] * carry_state + jnp.einsum(
        "gshp,gsn->ghpn", x_weighted, b_blk, precision=HIGH
    )
    return (new_state, y_intra + y_inter)


def gram_layout():
    rows = []
    for real in range(1, KW + 1):
        for code in range(BASES**real):
            taps = [None] * (KW - real) + [
                (code // BASES ** (real - 1 - k)) % BASES for k in range(real)
            ]
            rows.append(taps)
    picks = np.zeros((GRAMS, KW * BASES), np.float32)
    for row, taps in enumerate(rows):
        for offset, base in enumerate(taps):
            if base is not None:
                picks[row, offset * BASES + base] = 1.0
    return picks


def gram_tables(emb_full, norm_gain, w_xbc, w_z, w_dt, conv_w, conv_bias):
    row_norm = rms_gain(emb_full.astype(jnp.float32), norm_gain).astype(jnp.bfloat16)
    xbc_rows = jnp.dot(row_norm, w_xbc, preferred_element_type=jnp.float32).astype(jnp.bfloat16)
    z_rows = jnp.dot(row_norm, w_z, preferred_element_type=jnp.float32).astype(jnp.bfloat16)
    dt_rows = jnp.dot(row_norm, w_dt, preferred_element_type=jnp.float32)
    taps = (conv_w[:, None, :] * xbc_rows.astype(jnp.float32)[None]).reshape(KW * BASES, CONVW)
    conv_sum = conv_bias + jnp.dot(jnp.asarray(gram_layout()), taps, precision=HIGH)
    return jax.nn.silu(conv_sum), z_rows, dt_rows


def gram_ids(ext, where_in):
    count = where_in.shape[1]
    code = jnp.zeros_like(where_in)
    ids = jnp.zeros_like(where_in)
    offset_of = 0
    for real in range(1, KW + 1):
        code = code + ext[:, KW - real : KW - real + count] * BASES ** (real - 1)
        chosen = (where_in >= real - 1) if real == KW else (where_in == real - 1)
        ids = jnp.where(chosen, offset_of + code, ids)
        offset_of += BASES**real
    return ids


def gather_all(fwd, rc, axis):
    count = lax.axis_size(axis)
    place = lax.axis_index(axis)
    rows = fwd.shape[0]
    held = jnp.concatenate([fwd, rc], axis=0)
    bit = 0
    while 2**bit < count:
        mask = 2**bit
        other = lax.ppermute(held, axis, [(src, src ^ mask) for src in range(count)])
        upper = (place // mask) % 2 == 1
        low_first = jnp.concatenate([held, other], axis=1)
        high_first = jnp.concatenate([other, held], axis=1)
        held = jnp.concatenate(
            [
                jnp.where(upper, high_first[:rows], low_first[:rows]),
                jnp.where(upper, low_first[rows:], high_first[rows:]),
            ],
            axis=0,
        )
        bit += 1
    return held


def heads_lookup(rows, bases):
    picked = jnp.zeros(bases.shape[:-1] + (rows.shape[1], bases.shape[-1]), jnp.float32)
    for base in range(BASES):
        picked = picked + jnp.where(
            (bases == base)[..., None, :], rows[base][:, None], 0.0
        )
    return picked


def onehot(ids, size):
    return (ids[..., None] == jnp.arange(size, dtype=ids.dtype)).astype(jnp.bfloat16)


def exchange(size):
    rows = lax.broadcasted_iota(jnp.int32, (size, size), 0)
    cols = lax.broadcasted_iota(jnp.int32, (size, size), 1)
    return (rows + cols == size - 1).astype(jnp.bfloat16)


def split_bf16(values):
    high = values.astype(jnp.bfloat16)
    return high, (values - high.astype(jnp.float32)).astype(jnp.bfloat16)


def block_cumsum(values, tri):
    return jnp.einsum("...s,st->...t", values, tri, precision=HIGH)


def needed_per_gram(seq_tok, gram, dt_rows, dt_bias, neg_rate, tri, place, windows, nblk):
    need = nblk - 1

    def arranged(values):
        fwd = values[:windows].reshape(windows, nblk, BLK)
        rc = values[windows:].reshape(windows, nblk, BLK)[:, ::-1]
        joined = jnp.concatenate([rc, fwd], axis=1)
        return lax.dynamic_slice_in_dim(joined, place + 1, need, axis=1)

    tok_n = arranged(seq_tok)
    gram_n = arranged(gram)
    dt_n = jax.nn.softplus(
        heads_lookup(dt_rows, tok_n.reshape(windows, need * BLK)) + dt_bias[:, None]
    ).reshape(windows, HEADS, need, BLK)
    cum = block_cumsum(neg_rate[:, :, None] * dt_n, tri)
    blk_total = cum[..., -1]
    within = jnp.exp(blk_total[..., None] - cum) * dt_n
    idx = jnp.arange(need)
    is_fwd = idx >= (nblk - 1 - place)
    pick = jnp.where(is_fwd[:, None], idx[None, :] > idx[:, None], idx[None, :] < idx[:, None])
    span = jnp.sum(jnp.where(pick[None, None], blk_total[:, :, None, :], 0.0), axis=3)
    weight = within * jnp.exp(span)[..., None]
    fwd_part = is_fwd[None, None, :, None]
    w_hi, w_lo = split_bf16(
        jnp.concatenate(
            [jnp.where(fwd_part, weight, 0.0), jnp.where(fwd_part, 0.0, weight)], axis=1
        )
    )
    summed = jnp.einsum(
        "whbs,wbsg->whg",
        jnp.concatenate([w_hi, w_lo], axis=1),
        onehot(gram_n, GRAMS),
        preferred_element_type=jnp.float32,
    )
    summed = summed[:, : 2 * HEADS] + summed[:, 2 * HEADS :]
    return jnp.concatenate([summed[:, :HEADS], summed[:, HEADS:]], axis=0)


def local(
    tokens,
    emb_half,
    norm_gain,
    w_xbc,
    w_z,
    w_dt,
    conv_w,
    conv_bias,
    dt_bias,
    a_log,
    d_skip,
    inner_gain,
    w_out,
    final_gain,
    w_head_half,
    teacher_top,
    teacher_vals,
):
    windows, count = tokens.shape
    nseq = lax.axis_size("seq")
    place = lax.axis_index("seq")
    total = count * nseq
    nblk = total // BLK
    nloc = count // BLK
    streams = 2 * windows
    units = streams * nloc
    tri = (jnp.arange(BLK)[:, None] <= jnp.arange(BLK)[None, :]).astype(jnp.float32)

    flip_d = exchange(emb_half.shape[1])
    emb_flip = jnp.dot(emb_half, flip_d, preferred_element_type=jnp.float32).astype(jnp.bfloat16)
    emb_full = jnp.concatenate([emb_half, emb_flip[1:2], emb_flip[0:1]], axis=0)
    act_tab, z_rows, dt_rows = gram_tables(emb_full, norm_gain, w_xbc, w_z, w_dt, conv_w, conv_bias)
    x_tab = act_tab[:, :INNER].astype(jnp.bfloat16)
    b_tab = act_tab[:, INNER : INNER + NS]
    bc_tab = act_tab[:, INNER:]
    x_heads = x_tab.reshape(GRAMS, HEADS, HD).transpose(1, 0, 2)
    neg_rate = -jnp.exp(a_log)[:, None]

    flip_t = exchange(count)
    rc_tok = (BASES - 1) - jnp.dot(
        tokens.astype(jnp.bfloat16), flip_t, preferred_element_type=jnp.float32
    ).astype(jnp.int32)
    local_tok = jnp.concatenate([tokens, rc_tok], axis=0)
    pos0 = jnp.concatenate(
        [jnp.full((windows, 1), place * count), jnp.full((windows, 1), (nseq - 1 - place) * count)]
    ).astype(jnp.int32)

    seq_tok = gather_all(tokens, rc_tok, "seq")
    ext_all = jnp.concatenate([jnp.zeros((streams, KW - 1), seq_tok.dtype), seq_tok], axis=1)
    gram = gram_ids(ext_all, jnp.broadcast_to(jnp.arange(total, dtype=jnp.int32), (streams, total)))
    local_gram = jnp.concatenate(
        [
            lax.dynamic_slice_in_dim(gram[:windows], place * count, count, axis=1),
            lax.dynamic_slice_in_dim(gram[windows:], (nseq - 1 - place) * count, count, axis=1),
        ],
        axis=0,
    )

    oh_loc = onehot(local_gram, GRAMS)
    x_loc = jnp.take(x_tab, local_gram, axis=0)
    bc_loc = jnp.einsum("rtg,gc->rtc", oh_loc, bc_tab, precision=HIGH)
    oh_tok = onehot(local_tok, BASES)
    z_loc = jnp.einsum("rtk,kc->rtc", oh_tok, z_rows, preferred_element_type=jnp.float32)
    dt_loc = jax.nn.softplus(heads_lookup(dt_rows, local_tok) + dt_bias[:, None])
    ld_loc = neg_rate * dt_loc

    def per_unit(values, axis):
        shape = values.shape
        split = shape[:axis] + (nloc, BLK) + shape[axis + 1 :]
        moved = jnp.moveaxis(values.reshape(split), axis, 1)
        return moved.reshape((units,) + moved.shape[2:])

    x_u = per_unit(x_loc, 1).reshape(units, BLK, HEADS, HD)
    b_u = per_unit(bc_loc[..., :NS], 1)
    c_u = per_unit(bc_loc[..., NS:], 1)
    dt_u = per_unit(dt_loc, 2)
    cum_u = block_cumsum(per_unit(ld_loc, 2), tri)

    scores = jnp.einsum("utn,usn->uts", c_u, b_u, precision=lax.Precision.HIGH)
    seg_diff = cum_u[:, :, :, None] - cum_u[:, :, None, :]
    lower = tri.T > 0
    decays = jnp.where(lower, jnp.exp(jnp.where(lower, seg_diff, 0.0)), 0.0)
    weights = (scores[:, None] * decays * dt_u[:, :, None, :]).astype(jnp.bfloat16)
    y_intra = jnp.einsum("uhts,ushp->uthp", weights, x_u, preferred_element_type=jnp.float32)

    if nloc == 1:
        per_gram = needed_per_gram(
            seq_tok, gram, dt_rows, dt_bias, neg_rate, tri, place, windows, nblk
        )
    else:
        dt_all = jax.nn.softplus(heads_lookup(dt_rows, seq_tok) + dt_bias[:, None])
        ld_all = neg_rate * dt_all
        cum = block_cumsum(ld_all.reshape(streams, HEADS, nblk, BLK), tri)
        blk_total = cum[..., -1]
        within = jnp.exp(blk_total[..., None] - cum) * dt_all.reshape(streams, HEADS, nblk, BLK)

        first_blk = (
            jnp.repeat(pos0[:, 0] // BLK, nloc) + jnp.tile(jnp.arange(nloc, dtype=jnp.int32), streams)
        )
        blk_idx = jnp.arange(nblk)
        total_u = jnp.repeat(blk_total, nloc, axis=0)
        between = (blk_idx[:, None] < blk_idx[None, :])[None] & (
            blk_idx[None, None, :] < first_blk[:, None, None]
        )
        span = jnp.sum(jnp.where(between[:, None], total_u[:, :, None, :], 0.0), axis=3)
        across = jnp.where(blk_idx[None, None, :] < first_blk[:, None, None], jnp.exp(span), 0.0)
        weight = jnp.repeat(within, nloc, axis=0) * across[..., None]
        w_hi, w_lo = split_bf16(weight)
        oh_all = jnp.repeat(onehot(gram, GRAMS), nloc, axis=0).reshape(units, nblk, BLK, GRAMS)
        per_gram = jnp.einsum(
            "uhbs,ubsg->uhg",
            jnp.concatenate([w_hi, w_lo], axis=1),
            oh_all,
            preferred_element_type=jnp.float32,
        )
        per_gram = per_gram[:, :HEADS] + per_gram[:, HEADS:]
    b_hi, b_lo = split_bf16(per_gram[..., None] * b_tab[None, None])
    start_state = jnp.einsum("hgp,uhgn->uhpn", x_heads, b_hi, preferred_element_type=jnp.float32)

    y_inter = (
        jnp.einsum("utn,uhpn->uthp", c_u, start_state, precision=lax.Precision.HIGH)
        * jnp.exp(cum_u).transpose(0, 2, 1)[..., None]
    )
    y_u = y_intra + y_inter + d_skip[:, None] * x_u.astype(jnp.float32)
    z_u = per_unit(z_loc, 1).reshape(units, BLK, HEADS, HD)
    gated_y = y_u * jax.nn.silu(z_u)
    normed = rms_gain(gated_y, inner_gain.reshape(HEADS, HD)).astype(jnp.bfloat16)
    normed = jnp.moveaxis(normed.reshape(streams, nloc, BLK, INNER), 1, 1).reshape(
        streams, count, INNER
    )
    outputs = jnp.einsum("gre,ed->grd", normed, w_out, preferred_element_type=jnp.float32).astype(
        jnp.bfloat16
    )

    embedded = jnp.einsum(
        "grk,kd->grd", oh_tok[:windows], emb_full, preferred_element_type=jnp.float32
    ).astype(jnp.bfloat16)
    returned = outputs[windows:, ::-1, ::-1]
    hidden_out = (
        embedded.astype(jnp.float32)
        + outputs[:windows].astype(jnp.float32)
        + returned.astype(jnp.float32)
    ).astype(jnp.bfloat16)
    final_normed = rms_gain(hidden_out.astype(jnp.float32), final_gain).astype(jnp.bfloat16)
    head_flip = jnp.dot(flip_d, w_head_half, preferred_element_type=jnp.float32).astype(
        jnp.bfloat16
    )
    head_full = jnp.concatenate([w_head_half, head_flip[:, 1:2], head_flip[:, 0:1]], axis=1)
    logits = jnp.einsum("grd,db->grb", final_normed, head_full, preferred_element_type=jnp.float32)
    log_q = logits - jnp.log(jnp.sum(jnp.exp(logits), axis=-1, keepdims=True))
    top_value = jnp.max(teacher_vals, axis=1, keepdims=True)
    shifted = teacher_vals - top_value
    log_p = shifted - jnp.log(jnp.sum(jnp.exp(shifted), axis=1, keepdims=True))
    matches = teacher_top[..., None] == jnp.arange(4, dtype=jnp.int32)
    picked = jnp.sum(jnp.where(matches, log_q[:, None, :, :], 0.0), axis=-1)
    divergence = jnp.sum(jnp.exp(log_p) * (log_p - picked), axis=1)
    return (hidden_out, divergence)


def solution(mesh):
    placed = (
        P("grp", "seq"),
        P(),
        P(),
        P(),
        P(),
        P(),
        P(),
        P(),
        P(),
        P(),
        P(),
        P(),
        P(),
        P(),
        P(),
        P("grp", None, "seq"),
        P("grp", None, "seq"),
    )
    return jax.shard_map(
        local,
        mesh=mesh,
        in_specs=placed,
        out_specs=(P("grp", "seq", None), P("grp", "seq")),
        check_vma=False,
    )
```

```python
import jax
import jax.numpy as jnp
import numpy as np
from jax import lax
from jax.sharding import PartitionSpec as P

INNER = 1024
HD = 64
NS = 64
KW = 4
BLK = 128
HEADS = 16
CONVW = 1152
BASES = 4
GRAMS = 344


EPS = 1e-05
HIGH = lax.Precision.HIGHEST


def rms_gain(values, gain_row):
    return values * lax.rsqrt(jnp.mean(values * values, axis=-1, keepdims=True) + EPS) * gain_row


def to_blocks(values, block_width):
    streams, count = (values.shape[0], values.shape[1])
    return jnp.moveaxis(
        values.reshape((streams, count // block_width, block_width) + values.shape[2:]), 1, 0
    )


def ssd_block(carry_state, block_in):
    x_blk, b_blk, c_blk, decay_blk, dt_blk = block_in
    cumulated = jnp.cumsum(decay_blk, axis=2)
    block_len = decay_blk.shape[2]
    scores = jnp.einsum("gtn,gsn->gts", c_blk, b_blk, precision=HIGH)
    seg_diff = cumulated[:, :, :, None] - cumulated[:, :, None, :]
    lower_mask = jnp.arange(block_len)[:, None] >= jnp.arange(block_len)[None, :]
    decays = jnp.where(lower_mask, jnp.exp(jnp.where(lower_mask, seg_diff, 0.0)), 0.0)
    weights = (scores[:, None] * decays * dt_blk[:, :, None, :]).astype(jnp.bfloat16)
    y_intra = jnp.einsum("ghts,gshp->gthp", weights, x_blk, preferred_element_type=jnp.float32)
    y_inter = (
        jnp.einsum("gtn,ghpn->gthp", c_blk, carry_state, precision=HIGH)
        * jnp.swapaxes(jnp.exp(cumulated), 1, 2)[..., None]
    )
    last_cum = cumulated[:, :, -1:]
    scaled = jnp.exp(last_cum - cumulated) * dt_blk
    x_weighted = x_blk.astype(jnp.float32) * jnp.swapaxes(scaled, 1, 2)[..., None]
    new_state = jnp.exp(last_cum)[..., None] * carry_state + jnp.einsum(
        "gshp,gsn->ghpn", x_weighted, b_blk, precision=HIGH
    )
    return (new_state, y_intra + y_inter)


def silu(values):
    return values * (0.5 * jnp.tanh(0.5 * values) + 0.5)


def gram_layout():
    rows = []
    for real in range(1, KW + 1):
        for code in range(BASES**real):
            taps = [None] * (KW - real) + [
                (code // BASES ** (real - 1 - k)) % BASES for k in range(real)
            ]
            rows.append(taps)
    picks = np.zeros((GRAMS, KW * BASES), np.float32)
    for row, taps in enumerate(rows):
        for offset, base in enumerate(taps):
            if base is not None:
                picks[row, offset * BASES + base] = 1.0
    return picks


def gram_tables(emb_full, norm_gain, w_xbc, w_z, w_dt, conv_w, conv_bias):
    row_norm = rms_gain(emb_full.astype(jnp.float32), norm_gain).astype(jnp.bfloat16)
    xbc_rows = jnp.dot(row_norm, w_xbc, preferred_element_type=jnp.float32).astype(jnp.bfloat16)
    z_rows = jnp.dot(row_norm, w_z, preferred_element_type=jnp.float32).astype(jnp.bfloat16)
    dt_rows = jnp.dot(row_norm, w_dt, preferred_element_type=jnp.float32)
    taps = (conv_w[:, None, :] * xbc_rows.astype(jnp.float32)[None]).reshape(KW * BASES, CONVW)
    conv_sum = conv_bias + jnp.dot(jnp.asarray(gram_layout()), taps, precision=HIGH)
    return silu(conv_sum), z_rows, dt_rows


def gram_ids(ext, where_in):
    count = where_in.shape[1]
    code = jnp.zeros_like(where_in)
    ids = jnp.zeros_like(where_in)
    offset_of = 0
    for real in range(1, KW + 1):
        code = code + ext[:, KW - real : KW - real + count] * BASES ** (real - 1)
        chosen = (where_in >= real - 1) if real == KW else (where_in == real - 1)
        ids = jnp.where(chosen, offset_of + code, ids)
        offset_of += BASES**real
    return ids


def gather_all(fwd, rc, axis):
    count = lax.axis_size(axis)
    place = lax.axis_index(axis)
    rows = fwd.shape[0]
    held = jnp.concatenate([fwd, rc], axis=0)
    bit = 0
    while 2**bit < count:
        mask = 2**bit
        other = lax.ppermute(held, axis, [(src, src ^ mask) for src in range(count)])
        upper = (place // mask) % 2 == 1
        low_first = jnp.concatenate([held, other], axis=1)
        high_first = jnp.concatenate([other, held], axis=1)
        held = jnp.concatenate(
            [
                jnp.where(upper, high_first[:rows], low_first[:rows]),
                jnp.where(upper, low_first[rows:], high_first[rows:]),
            ],
            axis=0,
        )
        bit += 1
    return held


def heads_lookup(rows, bases):
    picked = jnp.zeros(bases.shape[:-1] + (rows.shape[1], bases.shape[-1]), jnp.float32)
    for base in range(BASES):
        picked = picked + jnp.where(
            (bases == base)[..., None, :], rows[base][:, None], 0.0
        )
    return picked


def onehot(ids, size):
    return (ids[..., None] == jnp.arange(size, dtype=ids.dtype)).astype(jnp.bfloat16)


def exchange(size):
    rows = lax.broadcasted_iota(jnp.int32, (size, size), 0)
    cols = lax.broadcasted_iota(jnp.int32, (size, size), 1)
    return (rows + cols == size - 1).astype(jnp.bfloat16)


def split_bf16(values):
    high = values.astype(jnp.bfloat16)
    return high, (values - high.astype(jnp.float32)).astype(jnp.bfloat16)


def block_cumsum(values, tri):
    return jnp.einsum("...s,st->...t", values, tri, precision=HIGH)


def needed_per_gram(seq_tok, gram, dt_rows, dt_bias, neg_rate, tri, place, windows, nblk):
    need = nblk - 1

    def arranged(values):
        fwd = values[:windows].reshape(windows, nblk, BLK)
        rc = values[windows:].reshape(windows, nblk, BLK)[:, ::-1]
        joined = jnp.concatenate([rc, fwd], axis=1)
        return lax.dynamic_slice_in_dim(joined, place + 1, need, axis=1)

    tok_n = arranged(seq_tok)
    gram_n = arranged(gram)
    dt_n = jax.nn.softplus(
        heads_lookup(dt_rows, tok_n.reshape(windows, need * BLK)) + dt_bias[:, None]
    ).reshape(windows, HEADS, need, BLK)
    cum = block_cumsum(neg_rate[:, :, None] * dt_n, tri)
    blk_total = cum[..., -1]
    within = jnp.exp(blk_total[..., None] - cum) * dt_n
    idx = jnp.arange(need)
    is_fwd = idx >= (nblk - 1 - place)
    pick = jnp.where(is_fwd[:, None], idx[None, :] > idx[:, None], idx[None, :] < idx[:, None])
    span = jnp.sum(jnp.where(pick[None, None], blk_total[:, :, None, :], 0.0), axis=3)
    weight = within * jnp.exp(span)[..., None]
    fwd_part = is_fwd[None, None, :, None]
    w_hi, w_lo = split_bf16(
        jnp.concatenate(
            [jnp.where(fwd_part, weight, 0.0), jnp.where(fwd_part, 0.0, weight)], axis=1
        )
    )
    summed = jnp.einsum(
        "whbs,wbsg->whg",
        jnp.concatenate([w_hi, w_lo], axis=1),
        onehot(gram_n, GRAMS),
        preferred_element_type=jnp.float32,
    )
    summed = summed[:, : 2 * HEADS] + summed[:, 2 * HEADS :]
    return jnp.concatenate([summed[:, :HEADS], summed[:, HEADS:]], axis=0)


def local(
    tokens,
    emb_half,
    norm_gain,
    w_xbc,
    w_z,
    w_dt,
    conv_w,
    conv_bias,
    dt_bias,
    a_log,
    d_skip,
    inner_gain,
    w_out,
    final_gain,
    w_head_half,
    teacher_top,
    teacher_vals,
):
    windows, count = tokens.shape
    nseq = lax.axis_size("seq")
    place = lax.axis_index("seq")
    total = count * nseq
    nblk = total // BLK
    nloc = count // BLK
    streams = 2 * windows
    units = streams * nloc
    tri = (jnp.arange(BLK)[:, None] <= jnp.arange(BLK)[None, :]).astype(jnp.float32)

    flip_d = exchange(emb_half.shape[1])
    emb_flip = jnp.dot(emb_half, flip_d, preferred_element_type=jnp.float32).astype(jnp.bfloat16)
    emb_full = jnp.concatenate([emb_half, emb_flip[1:2], emb_flip[0:1]], axis=0)
    act_tab, z_rows, dt_rows = gram_tables(emb_full, norm_gain, w_xbc, w_z, w_dt, conv_w, conv_bias)
    x_tab = act_tab[:, :INNER].astype(jnp.bfloat16)
    b_tab = act_tab[:, INNER : INNER + NS]
    bc_tab = act_tab[:, INNER:]
    x_heads = x_tab.reshape(GRAMS, HEADS, HD).transpose(1, 0, 2)
    neg_rate = -jnp.exp(a_log)[:, None]

    flip_t = exchange(count)
    rc_tok = (BASES - 1) - jnp.dot(
        tokens.astype(jnp.bfloat16), flip_t, preferred_element_type=jnp.float32
    ).astype(jnp.int32)
    local_tok = jnp.concatenate([tokens, rc_tok], axis=0)
    pos0 = jnp.concatenate(
        [jnp.full((windows, 1), place * count), jnp.full((windows, 1), (nseq - 1 - place) * count)]
    ).astype(jnp.int32)

    seq_tok = gather_all(tokens, rc_tok, "seq")
    ext_all = jnp.concatenate([jnp.zeros((streams, KW - 1), seq_tok.dtype), seq_tok], axis=1)
    gram = gram_ids(ext_all, jnp.broadcast_to(jnp.arange(total, dtype=jnp.int32), (streams, total)))
    local_gram = jnp.concatenate(
        [
            lax.dynamic_slice_in_dim(gram[:windows], place * count, count, axis=1),
            lax.dynamic_slice_in_dim(gram[windows:], (nseq - 1 - place) * count, count, axis=1),
        ],
        axis=0,
    )

    oh_loc = onehot(local_gram, GRAMS)
    x_loc = jnp.einsum("rtg,gc->rtc", oh_loc, x_tab, preferred_element_type=jnp.float32).astype(
        jnp.bfloat16
    )
    bc_loc = jnp.einsum("rtg,gc->rtc", oh_loc, bc_tab, precision=HIGH)
    oh_tok = onehot(local_tok, BASES)
    z_loc = jnp.einsum("rtk,kc->rtc", oh_tok, z_rows, preferred_element_type=jnp.float32)
    dt_loc = jax.nn.softplus(heads_lookup(dt_rows, local_tok) + dt_bias[:, None])
    ld_loc = neg_rate * dt_loc

    def per_unit(values, axis):
        shape = values.shape
        split = shape[:axis] + (nloc, BLK) + shape[axis + 1 :]
        moved = jnp.moveaxis(values.reshape(split), axis, 1)
        return moved.reshape((units,) + moved.shape[2:])

    x_u = per_unit(x_loc, 1).reshape(units, BLK, HEADS, HD)
    b_u = per_unit(bc_loc[..., :NS], 1)
    c_u = per_unit(bc_loc[..., NS:], 1)
    dt_u = per_unit(dt_loc, 2)
    cum_u = block_cumsum(per_unit(ld_loc, 2), tri)

    scores = jnp.einsum("utn,usn->uts", c_u, b_u, precision=lax.Precision.HIGH)
    seg_diff = cum_u[:, :, :, None] - cum_u[:, :, None, :]
    lower = tri.T > 0
    decays = jnp.where(lower, jnp.exp(jnp.where(lower, seg_diff, 0.0)), 0.0)
    weights = (scores[:, None] * decays * dt_u[:, :, None, :]).astype(jnp.bfloat16)
    y_intra = jnp.einsum("uhts,ushp->uthp", weights, x_u, preferred_element_type=jnp.float32)

    if nloc == 1:
        per_gram = needed_per_gram(
            seq_tok, gram, dt_rows, dt_bias, neg_rate, tri, place, windows, nblk
        )
    else:
        dt_all = jax.nn.softplus(heads_lookup(dt_rows, seq_tok) + dt_bias[:, None])
        ld_all = neg_rate * dt_all
        cum = block_cumsum(ld_all.reshape(streams, HEADS, nblk, BLK), tri)
        blk_total = cum[..., -1]
        within = jnp.exp(blk_total[..., None] - cum) * dt_all.reshape(streams, HEADS, nblk, BLK)

        first_blk = (
            jnp.repeat(pos0[:, 0] // BLK, nloc) + jnp.tile(jnp.arange(nloc, dtype=jnp.int32), streams)
        )
        blk_idx = jnp.arange(nblk)
        total_u = jnp.repeat(blk_total, nloc, axis=0)
        between = (blk_idx[:, None] < blk_idx[None, :])[None] & (
            blk_idx[None, None, :] < first_blk[:, None, None]
        )
        span = jnp.sum(jnp.where(between[:, None], total_u[:, :, None, :], 0.0), axis=3)
        across = jnp.where(blk_idx[None, None, :] < first_blk[:, None, None], jnp.exp(span), 0.0)
        weight = jnp.repeat(within, nloc, axis=0) * across[..., None]
        w_hi, w_lo = split_bf16(weight)
        oh_all = jnp.repeat(onehot(gram, GRAMS), nloc, axis=0).reshape(units, nblk, BLK, GRAMS)
        per_gram = jnp.einsum(
            "uhbs,ubsg->uhg",
            jnp.concatenate([w_hi, w_lo], axis=1),
            oh_all,
            preferred_element_type=jnp.float32,
        )
        per_gram = per_gram[:, :HEADS] + per_gram[:, HEADS:]
    b_hi, b_lo = split_bf16(per_gram[..., None] * b_tab[None, None])
    start_state = jnp.einsum("hgp,uhgn->uhpn", x_heads, b_hi, preferred_element_type=jnp.float32)

    y_inter = (
        jnp.einsum("utn,uhpn->uthp", c_u, start_state, precision=lax.Precision.HIGH)
        * jnp.exp(cum_u).transpose(0, 2, 1)[..., None]
    )
    y_u = y_intra + y_inter + d_skip[:, None] * x_u.astype(jnp.float32)
    z_u = per_unit(z_loc, 1).reshape(units, BLK, HEADS, HD)
    gated_y = y_u * silu(z_u)
    normed = rms_gain(gated_y, inner_gain.reshape(HEADS, HD)).astype(jnp.bfloat16)
    normed = jnp.moveaxis(normed.reshape(streams, nloc, BLK, INNER), 1, 1).reshape(
        streams, count, INNER
    )
    outputs = jnp.einsum("gre,ed->grd", normed, w_out, preferred_element_type=jnp.float32).astype(
        jnp.bfloat16
    )

    embedded = jnp.einsum(
        "grk,kd->grd", oh_tok[:windows], emb_full, preferred_element_type=jnp.float32
    ).astype(jnp.bfloat16)
    returned = outputs[windows:, ::-1, ::-1]
    hidden_out = (
        embedded.astype(jnp.float32)
        + outputs[:windows].astype(jnp.float32)
        + returned.astype(jnp.float32)
    ).astype(jnp.bfloat16)
    final_normed = rms_gain(hidden_out.astype(jnp.float32), final_gain).astype(jnp.bfloat16)
    head_flip = jnp.dot(flip_d, w_head_half, preferred_element_type=jnp.float32).astype(
        jnp.bfloat16
    )
    head_full = jnp.concatenate([w_head_half, head_flip[:, 1:2], head_flip[:, 0:1]], axis=1)
    logits = jnp.einsum("grd,db->grb", final_normed, head_full, preferred_element_type=jnp.float32)
    log_q = logits - jnp.log(jnp.sum(jnp.exp(logits), axis=-1, keepdims=True))
    top_value = jnp.max(teacher_vals, axis=1, keepdims=True)
    shifted = teacher_vals - top_value
    log_p = shifted - jnp.log(jnp.sum(jnp.exp(shifted), axis=1, keepdims=True))
    matches = teacher_top[..., None] == jnp.arange(4, dtype=jnp.int32)
    picked = jnp.sum(jnp.where(matches, log_q[:, None, :, :], 0.0), axis=-1)
    divergence = jnp.sum(jnp.exp(log_p) * (log_p - picked), axis=1)
    return (hidden_out, divergence)


def solution(mesh):
    placed = (
        P("grp", "seq"),
        P(),
        P(),
        P(),
        P(),
        P(),
        P(),
        P(),
        P(),
        P(),
        P(),
        P(),
        P(),
        P(),
        P(),
        P("grp", None, "seq"),
        P("grp", None, "seq"),
    )
    return jax.shard_map(
        local,
        mesh=mesh,
        in_specs=placed,
        out_specs=(P("grp", "seq", None), P("grp", "seq")),
        check_vma=False,
    )
```
